32 devices in a mesh: groups: 2 (over y), head: 8 (over z, x), req: 2 (over core).
Axes of the slice: x: 2, y: 2, z: 4, core: 2. Of those that a mesh axis runs over, the one named last changes fastest.
Arguments:
- tokens: bfloat16 [2, 64, 2048], P('req', ('groups', 'head')), parts along dimension 1, may hold values from -4 to 4
- ssm_state: bfloat16 [2, 8, 128, 64, 128], P('req', 'groups', 'head'), parts along dimension 1, may hold values from -2 to 2
- conv_x_state: bfloat16 [2, 8, 3, 8192], P('req', 'groups', None, 'head'), parts along dimension 1, may hold values from -6 to 6
- conv_bc_state: bfloat16 [2, 8, 3, 2048], P('req', 'groups', None, 'head'), parts along dimension 1, may hold values from -6 to 6
- expert_ids: int32 [2, 64, 2], P('req', ('groups', 'head')), parts along dimension 1, may hold values from 0 to 7, all different within a row; in each aligned block of 4 rows (0 to 3, 4 to 7, ..., all dimensions but the last counted through in order) at most 2 rows name the same one
- mixer_gain: float32 [2048], replicated, may hold values from 0.5 to 1.5
- weight_xz: bfloat16 [2048, 16384], P(None, 'head'), may hold values from -0.125 to 0.125
- weight_bc: bfloat16 [2048, 2048], P(None, 'head'), may hold values from -0.125 to 0.125
- weight_delta: bfloat16 [2048, 128], P(None, 'head'), may hold values from -0.125 to 0.125
- delta_bias: float32 [128], P('head'), may hold values from -4 to -1
- decay_log: float32 [128], P('head'), may hold values from 0 to 2.8
- skip_gain: float32 [128], P('head'), may hold values from 0.5 to 1.5
- conv_x_kernel: float32 [4, 8192], P(None, 'head'), may hold values from -3 to 3
- conv_x_bias: float32 [8192], P('head'), may hold values from -3 to 3
- conv_bc_kernel: float32 [4, 2048], P(None, 'head'), may hold values from -3 to 3
- conv_bc_bias: float32 [2048], P('head'), may hold values from -3 to 3
- gated_gain: float32 [8192], P('head'), may hold values from 0.5 to 1.5
- weight_out: bfloat16 [8192, 2048], P('head'), may hold values from -0.0625 to 0.0625
- ffn_gain: float32 [2048], replicated, may hold values from 0.5 to 1.5
- router_weight: bfloat16 [2048, 8], replicated, may hold values from -0.125 to 0.125
- weight_up: bfloat16 [2048, 16384], P(None, 'head'), may hold values from -0.125 to 0.125
- weight_down: bfloat16 [16384, 2048], P('head'), may hold values from -0.125 to 0.125
Outputs:
- layer_out: bfloat16 [2, 64, 2048], P('req', ('groups', 'head')), parts along dimension 1
- new_state: bfloat16 [2, 8, 128, 64, 128], P('req', 'groups', 'head'), parts along dimension 1
- new_conv_x: bfloat16 [2, 8, 3, 8192], P('req', 'groups', None, 'head'), parts along dimension 1
- new_conv_bc: bfloat16 [2, 8, 3, 2048], P('req', 'groups', None, 'head'), parts along dimension 1
The draws below stay inside these ranges and needn't reach their ends.
There are 2 independent parts, one for each index of `groups`. The reference program is written for one: setup_inputs(seed, part) draws one part's arguments, and reference() takes and returns one part's arrays. A program takes and returns all parts, laid end to end along the dimension named above; an argument that names none is the same for every part. Nothing has to cross between parts.
Inputs may be any that keep to these rules, and one draw needn't show every extreme that they name: `expert_ids`: each row names 2 different experts; in each aligned block of 4 rows no expert is named more than 2 times, and the bound is reached.
All inputs are finite; a program needn't handle non-finite values.
Results may differ from the reference program's by a relative error of at most 0.017.
Values may be sent and summed in bfloat16 or wider, within the bound.
No kernel may reach another device: no remote copies, remote signals or barrier semaphores. Data moves between devices by JAX's collectives and lax.ppermute only.
A program may use at most 128 MiB of HBM per device.

```python
import math
import jax
import jax.numpy as jnp
import numpy as np
from jax import lax

D = 2048
HEADS = 128
P_SIZE = 64
N = 128
G = 8
CONV = 4
FF = 2048
EXPERTS = 8
TOP = 2
STEPS = 8
TOK_DEV = 4
CAP = 2
ROWS = 32
REQS = 4
N_REQ = 2


def draw_tokens(key, part):
    key_base, key_rows, key_cols = jax.random.split(key, 3)
    row_scale = jnp.exp(jax.random.uniform(key_rows, (N_REQ, ROWS, 1), jnp.float32, math.log(0.03), math.log(0.3)))
    column_scale = jnp.exp(jax.random.uniform(key_cols, (D,), jnp.float32, math.log(0.5), math.log(2.0)))
    base_values = jnp.clip(jax.random.normal(key_base, (N_REQ, ROWS, D), jnp.float32), -5.0, 5.0)
    return (base_values * row_scale * column_scale).astype(jnp.bfloat16)


def block_scale(key, shape, shards, least, top_value):
    def one(position, blocks):
        steps = jax.random.uniform(jax.random.fold_in(jax.random.fold_in(key, 6), position), (blocks,), jnp.float32, least / len(shards), top_value / len(shards))
        return jnp.repeat(jnp.exp(steps), shape[position] // blocks).reshape((-1,) + (1,) * (len(shape) - position - 1))

    factor_of = one(*shards[0])
    for cut in shards[1:]:
        factor_of = factor_of * one(*cut)
    return factor_of


def routed_block(own_key, own, number, rows, count, top, most, lean):
    ranking = jax.random.permutation(own_key, count)
    heavy_load, ordinary = load_shares(count, rows * top, most, lean, True), load_shares(count, rows * top, most, lean, False)
    places = jnp.arange(count)

    def named(sizes, rotation):
        used = int((sizes > 0).sum())
        fixed = max(1, used // 4)
        shifted = fixed + (places - fixed + rotation * (used - fixed)) % max(1, count - fixed)
        return jnp.zeros((count,), jnp.int32).at[ranking[jnp.where(places < fixed, places, shifted)]].set(jnp.asarray(sizes, jnp.int32))

    sizes = jnp.where(number % 4 == 0, named(heavy_load, number // 4), named(ordinary, number - number // 4 - 1))
    mixed = jax.random.permutation(jax.random.fold_in(own, 3), count)
    giver, sink = mixed[0:count // 2 * 2:2], mixed[1:count // 2 * 2:2]
    room = jnp.minimum(sizes[giver] - 1, most - sizes[sink]) // 2
    room = jnp.where((giver == ranking[0]) | (sink == ranking[0]) | (sizes[sink] == 0), 0, jnp.maximum(room, 0))
    shifted = jax.random.randint(jax.random.fold_in(own, 4), (count // 2,), 0, 1 << 20) % (room + 1)
    sizes = sizes.at[giver].add(-shifted).at[sink].add(shifted)
    members = jnp.searchsorted(jnp.cumsum(sizes), jnp.arange(rows * top), side="right").astype(jnp.int32)
    listing = members.reshape(top, rows).T
    listing = listing[jax.random.permutation(jax.random.fold_in(own, 1), rows)]
    rotation = jax.random.randint(jax.random.fold_in(own, 2), (rows, 1), 0, top)
    return jnp.take_along_axis(listing, (jnp.arange(top)[None, :] + rotation) % top, axis=1)


def load_shares(number_of, total, reach, skew, full):
    weights = [(1 << 20) // math.isqrt(rank ** skew) + 1 for rank in range(1, number_of + 1)]
    largest = reach if full else min(reach, max(-(-total // number_of), total * weights[0] // sum(weights)))
    least = 1 if total - largest >= number_of - 1 else 0
    counts, spare = [largest] + [least] * (number_of - 1), total - largest - least * (number_of - 1)
    while spare > 0:
        candidates = [i for i in range(1, number_of) if counts[i] < largest] or [i for i in range(1, number_of) if counts[i] < reach]
        whole, remaining = sum([weights[i] for i in candidates]), spare
        for i in candidates:
            more = min(reach - counts[i], max(1, remaining * weights[i] // whole), spare)
            counts[i] = counts[i] + more
            spare = spare - more
    return np.array(counts)


def centred(own_key, extent, spread, bound, cuts=(), kind=jnp.bfloat16):
    entries = jax.random.normal(own_key, extent, jnp.float32) * spread
    if len(cuts) > 0:
        entries = block_scale(own_key, extent, cuts, -0.22, 0.18) * entries
    return jnp.clip(entries, min=-bound, max=bound).astype(kind)


def setup_inputs(seed: int = 0, part: int = 0) -> dict:
    keys = jax.random.split(jax.random.key(seed), 23)
    part_keys = jax.random.split(jax.random.fold_in(keys[22], part), 23)
    tokens = draw_tokens(jax.random.fold_in(jax.random.fold_in(keys[22], part), 71), part)
    ssm_state = centred(part_keys[1], (N_REQ, REQS, HEADS, P_SIZE, N), 0.25, 2.0, ((0, 2), (2, 8)))
    conv_x_state = centred(part_keys[2], (N_REQ, REQS, CONV - 1, HEADS * P_SIZE), 1.0, 6.0, ((0, 2), (3, 8)))
    conv_bc_state = centred(part_keys[3], (N_REQ, REQS, CONV - 1, 2 * G * N), 1.0, 6.0, ((0, 2), (3, 8)))
    expert_ids_keys = jax.random.split(jax.random.fold_in(part_keys[4], 1), N_REQ * ROWS // TOK_DEV)
    expert_ids_turns = jax.random.permutation(jax.random.fold_in(part_keys[4], 3), N_REQ * ROWS // TOK_DEV)
    expert_ids = jax.vmap(lambda own, number: routed_block(jax.random.fold_in(part_keys[4], 2), own, number, TOK_DEV, EXPERTS, TOP, CAP, 2))(expert_ids_keys, expert_ids_turns).reshape((N_REQ, ROWS, TOP))
    mixer_gain = jnp.clip(1.0 + 0.1 * jax.random.normal(keys[5], (D,), jnp.float32), 0.5, 1.5)
    weight_xz = centred(keys[6], (D, 2 * HEADS * P_SIZE), D ** -0.5, 0.125, ((1, 8),))
    weight_bc = centred(keys[7], (D, 2 * G * N), D ** -0.5, 0.125, ((1, 8),))
    weight_delta = centred(keys[8], (D, HEADS), D ** -0.5, 0.125, ((1, 8),))
    delta_bias = jnp.clip(-4.0 + 3.0 * jax.random.uniform(keys[9], (HEADS,), jnp.float32) ** block_scale(keys[9], (HEADS,), ((0, 8),), -0.2, 0.2), -4.0, -1.0)
    decay_log = jnp.clip(2.8 * jax.random.uniform(keys[10], (HEADS,), jnp.float32) ** block_scale(keys[10], (HEADS,), ((0, 8),), -0.2, 0.2), 0.0, 2.8)
    skip_gain = jnp.clip(0.5 + 1.0 * jax.random.uniform(keys[11], (HEADS,), jnp.float32) ** block_scale(keys[11], (HEADS,), ((0, 8),), -0.2, 0.2), 0.5, 1.5)
    conv_x_kernel = centred(keys[12], (CONV, HEADS * P_SIZE), CONV ** -0.5, 3.0, ((1, 8),), jnp.float32)
    conv_x_bias = centred(keys[13], (HEADS * P_SIZE,), 0.5, 3.0, ((0, 8),), jnp.float32)
    conv_bc_kernel = centred(keys[14], (CONV, 2 * G * N), CONV ** -0.5, 3.0, ((1, 8),), jnp.float32)
    conv_bc_bias = centred(keys[15], (2 * G * N,), 0.5, 3.0, ((0, 8),), jnp.float32)
    gated_gain = jnp.clip(1.0 + 0.1 * jax.random.normal(keys[16], (HEADS * P_SIZE,), jnp.float32), 0.5, 1.5)
    weight_out = centred(keys[17], (HEADS * P_SIZE, D), (HEADS * P_SIZE) ** -0.5, 0.0625, ((0, 8),))
    ffn_gain = jnp.clip(1.0 + 0.1 * jax.random.normal(keys[18], (D,), jnp.float32), 0.5, 1.5)
    router_weight = centred(keys[19], (D, EXPERTS), D ** -0.5, 0.125)
    weight_up = centred(keys[20], (D, EXPERTS * FF), D ** -0.5, 0.125, ((1, 8),))
    weight_down = centred(keys[21], (EXPERTS * FF, D), FF ** -0.5, 0.125, ((0, 8),))
    return {"tokens": tokens, "ssm_state": ssm_state, "conv_x_state": conv_x_state, "conv_bc_state": conv_bc_state, "expert_ids": expert_ids, "mixer_gain": mixer_gain, "weight_xz": weight_xz, "weight_bc": weight_bc, "weight_delta": weight_delta, "delta_bias": delta_bias, "decay_log": decay_log, "skip_gain": skip_gain, "conv_x_kernel": conv_x_kernel, "conv_x_bias": conv_x_bias, "conv_bc_kernel": conv_bc_kernel, "conv_bc_bias": conv_bc_bias, "gated_gain": gated_gain, "weight_out": weight_out, "ffn_gain": ffn_gain, "router_weight": router_weight, "weight_up": weight_up, "weight_down": weight_down}


eps = 1e-05
highest = lax.Precision.HIGHEST

def norm_rows(values, gain):
    mean_square = lax.optimization_barrier(jnp.mean(values * values, axis=-1, keepdims=True))
    return values * lax.rsqrt(mean_square + eps) * gain

def causal_conv(past_rows, fresh_rows, kernel, offset):
    window = jnp.concatenate([past_rows, fresh_rows], axis=1)
    window_wide = window.astype(jnp.float32)
    fresh_count = fresh_rows.shape[1]
    running = offset + kernel[0] * window_wide[:, 0:fresh_count]
    for tap_index in range(1, kernel.shape[0]):
        running = running + kernel[tap_index] * window_wide[:, tap_index:tap_index + fresh_count]
    return (jax.nn.silu(running), window[:, fresh_count:])

def reference(tokens, ssm_state, conv_x_state, conv_bc_state, expert_ids, mixer_gain, weight_xz, weight_bc, weight_delta, delta_bias, decay_log, skip_gain, conv_x_kernel, conv_x_bias, conv_bc_kernel, conv_bc_bias, gated_gain, weight_out, ffn_gain, router_weight, weight_up, weight_down):
    requests = N_REQ * REQS
    inputs = tokens.reshape(requests * STEPS, D)
    normed = norm_rows(inputs.astype(jnp.float32), mixer_gain).astype(jnp.bfloat16)
    proj_xz = jnp.dot(normed, weight_xz, preferred_element_type=jnp.float32).reshape(requests, STEPS, HEADS, 2, P_SIZE)
    x_fresh = proj_xz[:, :, :, 0, :].reshape(requests, STEPS, HEADS * P_SIZE).astype(jnp.bfloat16)
    z_gate = proj_xz[:, :, :, 1, :]
    bc_fresh = jnp.dot(normed, weight_bc, preferred_element_type=jnp.float32).reshape(requests, STEPS, 2 * G * N).astype(jnp.bfloat16)
    delta = jax.nn.softplus(jnp.dot(normed, weight_delta, preferred_element_type=jnp.float32).reshape(requests, STEPS, HEADS) + delta_bias)
    x_conv, conv_x_new = causal_conv(conv_x_state.reshape(requests, CONV - 1, HEADS * P_SIZE), x_fresh, conv_x_kernel, conv_x_bias)
    bc_conv, conv_bc_new = causal_conv(conv_bc_state.reshape(requests, CONV - 1, 2 * G * N), bc_fresh, conv_bc_kernel, conv_bc_bias)
    bc_conv = lax.optimization_barrier(bc_conv.astype(jnp.bfloat16)).astype(jnp.float32)
    x_heads = x_conv.reshape(requests, STEPS, HEADS, P_SIZE)
    b_heads = jnp.repeat(bc_conv[:, :, :G * N].reshape(requests, STEPS, G, N), HEADS // G, axis=2)
    c_heads = jnp.repeat(bc_conv[:, :, G * N:].reshape(requests, STEPS, G, N), HEADS // G, axis=2)
    decay_rate = jnp.exp(delta * -jnp.exp(decay_log))
    ssm_now = ssm_state.reshape(requests, HEADS, P_SIZE, N)
    readings = []
    for step_index in range(STEPS):
        x_step = x_heads[:, step_index]
        fresh_state = decay_rate[:, step_index, :, None, None] * ssm_now.astype(jnp.float32) + (delta[:, step_index, :, None] * x_step)[..., None] * b_heads[:, step_index, :, None, :]
        reading = jnp.einsum('rhpn,rhn->rhp', fresh_state, c_heads[:, step_index], precision=highest) + skip_gain[:, None] * x_step
        readings.append(reading)
        ssm_now = fresh_state.astype(jnp.bfloat16)
    gated_out = jnp.stack(readings, axis=1) * jax.nn.silu(z_gate)
    grouped = gated_out.reshape(requests * STEPS, HEADS, P_SIZE)
    group_normed = norm_rows(grouped, gated_gain.reshape(HEADS, P_SIZE)).astype(jnp.bfloat16).reshape(requests * STEPS, HEADS * P_SIZE)
    mixer_out = jnp.dot(group_normed, weight_out, preferred_element_type=jnp.float32)
    residual = (inputs.astype(jnp.float32) + mixer_out).astype(jnp.bfloat16)
    ffn_in = norm_rows(residual.astype(jnp.float32), ffn_gain).astype(jnp.bfloat16)
    logits = jnp.dot(ffn_in, router_weight, preferred_element_type=jnp.float32)
    chosen = expert_ids.reshape(requests * STEPS, TOP)
    picked = jnp.take_along_axis(logits, chosen, axis=1)
    first_weight = jax.nn.sigmoid(picked[:, 0] - picked[:, 1])
    share = jnp.stack([first_weight, 1.0 - first_weight], axis=1)
    combined = jnp.zeros((requests * STEPS, D), jnp.float32)
    for expert in range(EXPERTS):
        hidden = jnp.square(jnp.maximum(jnp.dot(ffn_in, weight_up[:, expert * FF:(expert + 1) * FF], preferred_element_type=jnp.float32), 0.0)).astype(jnp.bfloat16)
        result = jnp.dot(hidden, weight_down[expert * FF:(expert + 1) * FF], preferred_element_type=jnp.float32)
        share_weight = lax.optimization_barrier(jnp.sum(share * (chosen == expert).astype(share.dtype), axis=1))
        combined = combined + share_weight[:, None] * result
    layer_out = (residual.astype(jnp.float32) + combined).astype(jnp.bfloat16).reshape(N_REQ, ROWS, D)
    return (layer_out, ssm_now.reshape(N_REQ, REQS, HEADS, P_SIZE, N), conv_x_new.reshape(N_REQ, REQS, CONV - 1, HEADS * P_SIZE), conv_bc_new.reshape(N_REQ, REQS, CONV - 1, 2 * G * N))
```

```python
import jax
import jax.numpy as jnp
from jax import lax
from jax.sharding import PartitionSpec as P

HEADS = 128
G = 8
EXPERTS = 8
TOP = 2
STEPS = 8
CAP = 2


eps = 1e-05
highest = lax.Precision.HIGHEST


def norm_rows(values, gain):
    mean_square = jnp.mean(values * values, axis=-1, keepdims=True)
    return values * lax.rsqrt(mean_square + eps) * gain


def causal_conv(past_rows, fresh_rows, kernel, offset):
    window = jnp.concatenate([past_rows, fresh_rows], axis=1)
    window_wide = window.astype(jnp.float32)
    fresh_count = fresh_rows.shape[1]
    running = offset + kernel[0] * window_wide[:, 0:fresh_count]
    for tap_index in range(1, kernel.shape[0]):
        running = running + kernel[tap_index] * window_wide[:, tap_index : tap_index + fresh_count]
    return (jax.nn.silu(running), window[:, fresh_count:])


def route_share(ffn_in, router_weight, chosen_ids):
    logits = jnp.dot(ffn_in, router_weight, preferred_element_type=jnp.float32)
    match_table = (chosen_ids[:, :, None] == jnp.arange(EXPERTS)[None, None, :]).astype(jnp.float32)
    picked = jnp.einsum("mke,me->mk", match_table, logits, precision=highest)
    first_weight = jax.nn.sigmoid(picked[:, 0] - picked[:, 1])
    return jnp.stack([first_weight, 1.0 - first_weight], axis=1)


def expert_hidden(rows_in, weight_up):
    return jnp.square(
        jnp.maximum(jnp.dot(rows_in, weight_up, preferred_element_type=jnp.float32), 0.0)
    ).astype(jnp.bfloat16)


def shards(
    tokens,
    ssm_state,
    conv_x_state,
    conv_bc_state,
    expert_ids,
    mixer_gain,
    weight_xz,
    weight_bc,
    weight_delta,
    delta_bias,
    decay_log,
    skip_gain,
    conv_x_kernel,
    conv_x_bias,
    conv_bc_kernel,
    conv_bc_bias,
    gated_gain,
    weight_out,
    ffn_gain,
    router_weight,
    weight_up,
    weight_down,
):
    head_count = lax.axis_size("head")
    my_index = lax.axis_index("head")
    tok_local = tokens.shape[1]
    width = tokens.shape[2]
    requests = ssm_state.shape[1]
    heads_local = ssm_state.shape[2]
    head_dim = ssm_state.shape[3]
    state_dim = ssm_state.shape[4]
    gathered = lax.all_gather(tokens, "head", axis=1, tiled=True)
    inputs = gathered.reshape(requests * STEPS, width)
    normed = norm_rows(inputs.astype(jnp.float32), mixer_gain).astype(jnp.bfloat16)
    proj_xz = jnp.dot(normed, weight_xz, preferred_element_type=jnp.float32).reshape(
        requests, STEPS, heads_local, 2, head_dim
    )
    x_fresh = (
        proj_xz[:, :, :, 0, :].reshape(requests, STEPS, heads_local * head_dim).astype(jnp.bfloat16)
    )
    z_gate = proj_xz[:, :, :, 1, :]
    bc_fresh = (
        jnp.dot(normed, weight_bc, preferred_element_type=jnp.float32)
        .reshape(requests, STEPS, -1)
        .astype(jnp.bfloat16)
    )
    delta = jax.nn.softplus(
        jnp.dot(normed, weight_delta, preferred_element_type=jnp.float32).reshape(
            requests, STEPS, heads_local
        )
        + delta_bias
    )
    x_conv, conv_x_new = causal_conv(conv_x_state[0], x_fresh, conv_x_kernel, conv_x_bias)
    bc_conv, conv_bc_new = causal_conv(conv_bc_state[0], bc_fresh, conv_bc_kernel, conv_bc_bias)
    bc_conv = bc_conv.astype(jnp.bfloat16)
    bc_all = lax.all_gather(bc_conv, "head", axis=2, tiled=True)
    bc_list = [bc_all[:, step_index] for step_index in range(STEPS)]
    head_global = my_index * heads_local + jnp.arange(heads_local)
    group_pick = (head_global[:, None] // (HEADS // G) == jnp.arange(G)[None, :]).astype(
        jnp.float32
    )
    x_heads = x_conv.reshape(requests, STEPS, heads_local, head_dim)
    decay_rate = jnp.exp(delta * -jnp.exp(decay_log))
    ssm_now = ssm_state[0]
    readings = []
    for step_index in range(STEPS):
        bc_values = bc_list[step_index].astype(jnp.float32).reshape(requests, 2, G, state_dim)
        b_heads = jnp.einsum("rgn,hg->rhn", bc_values[:, 0], group_pick, precision=highest)
        c_heads = jnp.einsum("rgn,hg->rhn", bc_values[:, 1], group_pick, precision=highest)
        x_step = x_heads[:, step_index]
        fresh_state = (
            decay_rate[:, step_index, :, None, None] * ssm_now.astype(jnp.float32)
            + (delta[:, step_index, :, None] * x_step)[..., None] * b_heads[:, :, None, :]
        )
        readings.append(
            jnp.einsum("rhpn,rhn->rhp", fresh_state, c_heads, precision=highest)
            + skip_gain[:, None] * x_step
        )
        ssm_now = fresh_state.astype(jnp.bfloat16)
    gated_out = jnp.stack(readings, axis=1) * jax.nn.silu(z_gate)
    group_normed = (
        norm_rows(gated_out, gated_gain.reshape(heads_local, head_dim))
        .astype(jnp.bfloat16)
        .reshape(requests * STEPS, heads_local * head_dim)
    )
    per_expert = head_count // EXPERTS
    mixer_out = lax.psum_scatter(
        jnp.dot(group_normed, weight_out, preferred_element_type=jnp.float32),
        "head",
        scatter_dimension=0,
        tiled=True,
    )
    residual = (tokens[0].astype(jnp.float32) + mixer_out).astype(jnp.bfloat16)
    ffn_in = norm_rows(residual.astype(jnp.float32), ffn_gain).astype(jnp.bfloat16)
    share = route_share(ffn_in, router_weight, expert_ids[0])
    chosen = expert_ids[0].reshape(-1)
    onehot = (chosen[:, None] == jnp.arange(EXPERTS)[None, :]).astype(jnp.int32)
    earlier = jnp.cumsum(onehot, axis=0) - onehot
    position = jnp.sum(earlier * onehot, axis=1)
    slot_index = chosen * CAP + position
    place = (jnp.arange(EXPERTS * CAP)[:, None] == slot_index[None, :]).astype(jnp.bfloat16)
    routed_rows = jnp.repeat(ffn_in, TOP, axis=0)
    packed = jnp.dot(place, routed_rows, preferred_element_type=jnp.float32).astype(jnp.bfloat16)
    outgoing = jnp.repeat(packed.reshape(EXPERTS, CAP, width), per_expert, axis=0)
    received = lax.all_to_all(outgoing, "head", split_axis=0, concat_axis=0, tiled=True)
    flat_rows = received.reshape(-1, width)
    hidden = expert_hidden(flat_rows, weight_up)
    computed = jnp.dot(hidden, weight_down, preferred_element_type=jnp.float32).reshape(
        received.shape[0], received.shape[1], width
    )
    returned = lax.all_to_all(
        computed.astype(jnp.bfloat16), "head", split_axis=0, concat_axis=0, tiled=True
    ).astype(computed.dtype)
    summed = (
        returned.reshape(EXPERTS, per_expert, CAP, width).sum(axis=1).reshape(EXPERTS * CAP, width)
    )
    per_route = jnp.dot(place.astype(jnp.float32).T, summed, precision=highest).reshape(
        tok_local, TOP, width
    )
    combined = jnp.sum(share[:, :, None] * per_route, axis=1)
    layer_out = (residual.astype(jnp.float32) + combined).astype(jnp.bfloat16)
    return (layer_out[None], ssm_now[None], conv_x_new[None], conv_bc_new[None])


def solution(mesh):
    return jax.shard_map(
        shards,
        mesh=mesh,
        in_specs=(
            P("req", ("groups", "head"), None),
            P("req", "groups", "head", None, None),
            P("req", "groups", None, "head"),
            P("req", "groups", None, "head"),
            P("req", ("groups", "head"), None),
            P(),
            P(None, "head"),
            P(None, "head"),
            P(None, "head"),
            P("head"),
            P("head"),
            P("head"),
            P(None, "head"),
            P("head"),
            P(None, "head"),
            P("head"),
            P("head"),
            P("head", None),
            P(),
            P(),
            P(None, "head"),
            P("head", None),
        ),
        out_specs=(
            P("req", ("groups", "head"), None),
            P("req", "groups", "head", None, None),
            P("req", "groups", None, "head"),
            P("req", "groups", None, "head"),
        ),
        check_vma=False,
    )
```

```python
import jax
import jax.numpy as jnp
from jax import lax
from jax.sharding import PartitionSpec as P

HEADS = 128
G = 8
EXPERTS = 8
TOP = 2
STEPS = 8
CAP = 2


eps = 1e-05
highest = lax.Precision.HIGHEST


def norm_rows(values, gain):
    mean_square = jnp.mean(values * values, axis=-1, keepdims=True)
    return values * lax.rsqrt(mean_square + eps) * gain


def causal_conv(past_rows, fresh_rows, kernel, offset):
    window = jnp.concatenate([past_rows, fresh_rows], axis=1)
    window_wide = window.astype(jnp.float32)
    fresh_count = fresh_rows.shape[1]
    running = offset + kernel[0] * window_wide[:, 0:fresh_count]
    for tap_index in range(1, kernel.shape[0]):
        running = running + kernel[tap_index] * window_wide[:, tap_index : tap_index + fresh_count]
    return (jax.nn.silu(running), window[:, fresh_count:])


def route_share(ffn_in, router_weight, chosen_ids):
    logits = jnp.dot(ffn_in, router_weight, preferred_element_type=jnp.float32)
    match_table = (chosen_ids[:, :, None] == jnp.arange(EXPERTS)[None, None, :]).astype(jnp.float32)
    picked = jnp.einsum("mke,me->mk", match_table, logits, precision=highest)
    first_weight = jax.nn.sigmoid(picked[:, 0] - picked[:, 1])
    return jnp.stack([first_weight, 1.0 - first_weight], axis=1)


def expert_hidden(rows_in, weight_up):
    return jnp.square(
        jnp.maximum(jnp.dot(rows_in, weight_up, preferred_element_type=jnp.float32), 0.0)
    ).astype(jnp.bfloat16)


def broadcast_gather(block, count):
    copies = jnp.broadcast_to(block[None], (count,) + block.shape)
    return lax.all_to_all(copies, "head", 0, 0, tiled=True)


def shards(
    tokens,
    ssm_state,
    conv_x_state,
    conv_bc_state,
    expert_ids,
    mixer_gain,
    weight_xz,
    weight_bc,
    weight_delta,
    delta_bias,
    decay_log,
    skip_gain,
    conv_x_kernel,
    conv_x_bias,
    conv_bc_kernel,
    conv_bc_bias,
    gated_gain,
    weight_out,
    ffn_gain,
    router_weight,
    weight_up,
    weight_down,
):
    head_count = lax.axis_size("head")
    my_index = lax.axis_index("head")
    tok_local = tokens.shape[1]
    width = tokens.shape[2]
    requests = ssm_state.shape[1]
    heads_local = ssm_state.shape[2]
    head_dim = ssm_state.shape[3]
    state_dim = ssm_state.shape[4]
    gathered = broadcast_gather(tokens[0], head_count)
    inputs = gathered.reshape(requests * STEPS, width)
    normed = norm_rows(inputs.astype(jnp.float32), mixer_gain).astype(jnp.bfloat16)
    proj_xz = jnp.dot(normed, weight_xz, preferred_element_type=jnp.float32).reshape(
        requests, STEPS, heads_local, 2, head_dim
    )
    x_fresh = (
        proj_xz[:, :, :, 0, :].reshape(requests, STEPS, heads_local * head_dim).astype(jnp.bfloat16)
    )
    z_gate = proj_xz[:, :, :, 1, :]
    bc_fresh = (
        jnp.dot(normed, weight_bc, preferred_element_type=jnp.float32)
        .reshape(requests, STEPS, -1)
        .astype(jnp.bfloat16)
    )
    delta = jax.nn.softplus(
        jnp.dot(normed, weight_delta, preferred_element_type=jnp.float32).reshape(
            requests, STEPS, heads_local
        )
        + delta_bias
    )
    x_conv, conv_x_new = causal_conv(conv_x_state[0], x_fresh, conv_x_kernel, conv_x_bias)
    bc_conv, conv_bc_new = causal_conv(conv_bc_state[0], bc_fresh, conv_bc_kernel, conv_bc_bias)
    bc_conv = bc_conv.astype(jnp.bfloat16)
    bc_all = jnp.moveaxis(broadcast_gather(bc_conv, head_count), 0, 2).reshape(
        requests, STEPS, -1
    )
    bc_list = [bc_all[:, step_index] for step_index in range(STEPS)]
    head_global = my_index * heads_local + jnp.arange(heads_local)
    group_pick = (head_global[:, None] // (HEADS // G) == jnp.arange(G)[None, :]).astype(
        jnp.float32
    )
    x_heads = x_conv.reshape(requests, STEPS, heads_local, head_dim)
    decay_rate = jnp.exp(delta * -jnp.exp(decay_log))
    ssm_now = ssm_state[0]
    readings = []
    for step_index in range(STEPS):
        bc_values = bc_list[step_index].astype(jnp.float32).reshape(requests, 2, G, state_dim)
        b_heads = jnp.einsum("rgn,hg->rhn", bc_values[:, 0], group_pick, precision=highest)
        c_heads = jnp.einsum("rgn,hg->rhn", bc_values[:, 1], group_pick, precision=highest)
        x_step = x_heads[:, step_index]
        fresh_state = (
            decay_rate[:, step_index, :, None, None] * ssm_now.astype(jnp.float32)
            + (delta[:, step_index, :, None] * x_step)[..., None] * b_heads[:, :, None, :]
        )
        readings.append(
            jnp.einsum("rhpn,rhn->rhp", fresh_state, c_heads, precision=highest)
            + skip_gain[:, None] * x_step
        )
        ssm_now = fresh_state.astype(jnp.bfloat16)
    gated_out = jnp.stack(readings, axis=1) * jax.nn.silu(z_gate)
    group_normed = (
        norm_rows(gated_out, gated_gain.reshape(heads_local, head_dim))
        .astype(jnp.bfloat16)
        .reshape(requests * STEPS, heads_local * head_dim)
    )
    per_expert = head_count // EXPERTS
    mixer_part = jnp.dot(group_normed, weight_out, preferred_element_type=jnp.float32)
    mixer_out = lax.all_to_all(
        mixer_part.reshape(head_count, tok_local, width), "head", 0, 0, tiled=True
    ).sum(axis=0)
    residual = (tokens[0].astype(jnp.float32) + mixer_out).astype(jnp.bfloat16)
    ffn_in = norm_rows(residual.astype(jnp.float32), ffn_gain).astype(jnp.bfloat16)
    share = route_share(ffn_in, router_weight, expert_ids[0])
    chosen = expert_ids[0].reshape(-1)
    onehot = (chosen[:, None] == jnp.arange(EXPERTS)[None, :]).astype(jnp.int32)
    earlier = jnp.cumsum(onehot, axis=0) - onehot
    position = jnp.sum(earlier * onehot, axis=1)
    slot_index = chosen * CAP + position
    place = (jnp.arange(EXPERTS * CAP)[:, None] == slot_index[None, :]).astype(jnp.bfloat16)
    routed_rows = jnp.repeat(ffn_in, TOP, axis=0)
    packed = jnp.dot(place, routed_rows, preferred_element_type=jnp.float32).astype(jnp.bfloat16)
    outgoing = jnp.repeat(packed.reshape(EXPERTS, CAP, width), per_expert, axis=0)
    received = lax.all_to_all(outgoing, "head", split_axis=0, concat_axis=0, tiled=True)
    flat_rows = received.reshape(-1, width)
    hidden = expert_hidden(flat_rows, weight_up)
    computed = jnp.dot(hidden, weight_down, preferred_element_type=jnp.float32).reshape(
        received.shape[0], received.shape[1], width
    )
    returned = lax.all_to_all(
        computed.astype(jnp.bfloat16), "head", split_axis=0, concat_axis=0, tiled=True
    ).astype(computed.dtype)
    summed = (
        returned.reshape(EXPERTS, per_expert, CAP, width).sum(axis=1).reshape(EXPERTS * CAP, width)
    )
    per_route = jnp.dot(place.astype(jnp.float32).T, summed, precision=highest).reshape(
        tok_local, TOP, width
    )
    combined = jnp.sum(share[:, :, None] * per_route, axis=1)
    layer_out = (residual.astype(jnp.float32) + combined).astype(jnp.bfloat16)
    return (layer_out[None], ssm_now[None], conv_x_new[None], conv_bc_new[None])


def solution(mesh):
    return jax.shard_map(
        shards,
        mesh=mesh,
        in_specs=(
            P("req", ("groups", "head"), None),
            P("req", "groups", "head", None, None),
            P("req", "groups", None, "head"),
            P("req", "groups", None, "head"),
            P("req", ("groups", "head"), None),
            P(),
            P(None, "head"),
            P(None, "head"),
            P(None, "head"),
            P("head"),
            P("head"),
            P("head"),
            P(None, "head"),
            P("head"),
            P(None, "head"),
            P("head"),
            P("head"),
            P("head", None),
            P(),
            P(),
            P(None, "head"),
            P("head", None),
        ),
        out_specs=(
            P("req", ("groups", "head"), None),
            P("req", "groups", "head", None, None),
            P("req", "groups", None, "head"),
            P("req", "groups", None, "head"),
        ),
        check_vma=False,
    )
```

```python
import jax
import jax.numpy as jnp
from jax import lax
from jax.experimental import pallas as pl
from jax.sharding import PartitionSpec as P

HEADS = 128
G = 8
EXPERTS = 8
TOP = 2
STEPS = 8
CAP = 2


eps = 1e-05
highest = lax.Precision.HIGHEST


def norm_rows(values, gain):
    mean_square = jnp.mean(values * values, axis=-1, keepdims=True)
    return values * lax.rsqrt(mean_square + eps) * gain


def causal_conv(past_rows, fresh_rows, kernel, offset):
    window = jnp.concatenate([past_rows, fresh_rows], axis=1)
    window_wide = window.astype(jnp.float32)
    fresh_count = fresh_rows.shape[1]
    running = offset + kernel[0] * window_wide[:, 0:fresh_count]
    for tap_index in range(1, kernel.shape[0]):
        running = running + kernel[tap_index] * window_wide[:, tap_index : tap_index + fresh_count]
    return (jax.nn.silu(running), window[:, fresh_count:])


def route_share(ffn_in, router_weight, chosen_ids):
    logits = jnp.dot(ffn_in, router_weight, preferred_element_type=jnp.float32)
    match_table = (chosen_ids[:, :, None] == jnp.arange(EXPERTS)[None, None, :]).astype(jnp.float32)
    picked = jnp.einsum("mke,me->mk", match_table, logits, precision=highest)
    first_weight = jax.nn.sigmoid(picked[:, 0] - picked[:, 1])
    return jnp.stack([first_weight, 1.0 - first_weight], axis=1)


def expert_hidden(rows_in, weight_up):
    return jnp.square(
        jnp.maximum(jnp.dot(rows_in, weight_up, preferred_element_type=jnp.float32), 0.0)
    ).astype(jnp.bfloat16)


def ssm_scan_kernel(s_ref, dec_ref, dx_ref, b_ref, c_ref, s_out_ref, read_ref):
    tiles = s_ref.shape[1]
    steps = dec_ref.shape[2]

    def tile(j, carry):
        state = s_ref[0, j].astype(jnp.float32)
        b_all = b_ref[0, j]
        c_all = c_ref[0, j]
        dec_all = dec_ref[0, j]
        dx_all = dx_ref[0, j]
        for t in range(steps):
            fresh = dec_all[t : t + 1, :] * state + dx_all[t : t + 1, :] * b_all[:, t : t + 1]
            read_ref[0, j, t : t + 1, :] = jnp.sum(fresh * c_all[:, t : t + 1], axis=0, keepdims=True)
            state = fresh.astype(jnp.bfloat16).astype(jnp.float32)
        s_out_ref[0, j] = state.astype(jnp.bfloat16)
        return carry

    lax.fori_loop(0, tiles, tile, 0)


def ssm_scan(state_tiles, decay_tiles, dx_tiles, b_tiles, c_tiles):
    requests, tiles, state_dim, lanes = state_tiles.shape
    steps = decay_tiles.shape[2]
    big = pl.BlockSpec((1, tiles, state_dim, lanes), lambda r: (r, 0, 0, 0))
    per_step = pl.BlockSpec((1, tiles, steps, lanes), lambda r: (r, 0, 0, 0))
    columns = pl.BlockSpec((1, tiles, state_dim, steps), lambda r: (r, 0, 0, 0))
    return pl.pallas_call(
        ssm_scan_kernel,
        grid=(requests,),
        in_specs=[big, per_step, per_step, columns, columns],
        out_specs=[big, per_step],
        out_shape=[
            jax.ShapeDtypeStruct(state_tiles.shape, jnp.bfloat16),
            jax.ShapeDtypeStruct(decay_tiles.shape, jnp.float32),
        ],
    )(state_tiles, decay_tiles, dx_tiles, b_tiles, c_tiles)


def broadcast_gather(block, count):
    copies = jnp.broadcast_to(block[None], (count,) + block.shape)
    return lax.all_to_all(copies, "head", 0, 0, tiled=True)


def shards(
    tokens,
    ssm_state,
    conv_x_state,
    conv_bc_state,
    expert_ids,
    mixer_gain,
    weight_xz,
    weight_bc,
    weight_delta,
    delta_bias,
    decay_log,
    skip_gain,
    conv_x_kernel,
    conv_x_bias,
    conv_bc_kernel,
    conv_bc_bias,
    gated_gain,
    weight_out,
    ffn_gain,
    router_weight,
    weight_up,
    weight_down,
):
    head_count = lax.axis_size("head")
    my_index = lax.axis_index("head")
    tok_local = tokens.shape[1]
    width = tokens.shape[2]
    requests = ssm_state.shape[1]
    heads_local = ssm_state.shape[2]
    head_dim = ssm_state.shape[3]
    state_dim = ssm_state.shape[4]
    gathered = broadcast_gather(tokens[0], head_count)
    inputs = gathered.reshape(requests * STEPS, width)
    normed = norm_rows(inputs.astype(jnp.float32), mixer_gain).astype(jnp.bfloat16)
    proj_xz = jnp.dot(normed, weight_xz, preferred_element_type=jnp.float32).reshape(
        requests, STEPS, heads_local, 2, head_dim
    )
    x_fresh = (
        proj_xz[:, :, :, 0, :].reshape(requests, STEPS, heads_local * head_dim).astype(jnp.bfloat16)
    )
    z_gate = proj_xz[:, :, :, 1, :]
    bc_fresh = (
        jnp.dot(normed, weight_bc, preferred_element_type=jnp.float32)
        .reshape(requests, STEPS, -1)
        .astype(jnp.bfloat16)
    )
    delta = jax.nn.softplus(
        jnp.dot(normed, weight_delta, preferred_element_type=jnp.float32).reshape(
            requests, STEPS, heads_local
        )
        + delta_bias
    )
    x_conv, conv_x_new = causal_conv(conv_x_state[0], x_fresh, conv_x_kernel, conv_x_bias)
    bc_conv, conv_bc_new = causal_conv(conv_bc_state[0], bc_fresh, conv_bc_kernel, conv_bc_bias)
    bc_conv = bc_conv.astype(jnp.bfloat16)
    bc_all = jnp.moveaxis(broadcast_gather(bc_conv, head_count), 0, 2).reshape(
        requests, STEPS, -1
    )
    x_heads = x_conv.reshape(requests, STEPS, heads_local, head_dim)
    decay_rate = jnp.exp(delta * -jnp.exp(decay_log))
    pack = 2 if heads_local % 2 == 0 else 1
    tiles = heads_local // pack
    lanes = pack * head_dim

    def to_tiles(per_head):
        return per_head.reshape(requests, STEPS, tiles, lanes).transpose(0, 2, 1, 3)

    decay_tiles = to_tiles(
        jnp.broadcast_to(decay_rate[..., None], (requests, STEPS, heads_local, head_dim))
    )
    dx_tiles = to_tiles(delta[..., None] * x_heads)
    tile_group = (my_index * heads_local + jnp.arange(tiles) * pack) // (HEADS // G)
    bc_values = bc_all.astype(jnp.float32).reshape(requests, STEPS, 2, G, state_dim)
    b_tiles = jnp.take(bc_values[:, :, 0], tile_group, axis=2).transpose(0, 2, 3, 1)
    c_tiles = jnp.take(bc_values[:, :, 1], tile_group, axis=2).transpose(0, 2, 3, 1)
    state_tiles = (
        ssm_state[0]
        .reshape(requests, tiles, pack, head_dim, state_dim)
        .transpose(0, 1, 4, 2, 3)
        .reshape(requests, tiles, state_dim, lanes)
    )
    state_out, read_tiles = ssm_scan(state_tiles, decay_tiles, dx_tiles, b_tiles, c_tiles)
    ssm_now = (
        state_out.reshape(requests, tiles, state_dim, pack, head_dim)
        .transpose(0, 1, 3, 4, 2)
        .reshape(requests, heads_local, head_dim, state_dim)
    )
    scan_read = read_tiles.transpose(0, 2, 1, 3).reshape(requests, STEPS, heads_local, head_dim)
    readings = scan_read + skip_gain[:, None] * x_heads
    gated_out = readings * jax.nn.silu(z_gate)
    group_normed = (
        norm_rows(gated_out, gated_gain.reshape(heads_local, head_dim))
        .astype(jnp.bfloat16)
        .reshape(requests * STEPS, heads_local * head_dim)
    )
    per_expert = head_count // EXPERTS
    mixer_part = jnp.dot(group_normed, weight_out, preferred_element_type=jnp.float32)
    mixer_out = lax.all_to_all(
        mixer_part.reshape(head_count, tok_local, width), "head", 0, 0, tiled=True
    ).sum(axis=0)
    residual = (tokens[0].astype(jnp.float32) + mixer_out).astype(jnp.bfloat16)
    ffn_in = norm_rows(residual.astype(jnp.float32), ffn_gain).astype(jnp.bfloat16)
    share = route_share(ffn_in, router_weight, expert_ids[0])
    chosen = expert_ids[0].reshape(-1)
    onehot = (chosen[:, None] == jnp.arange(EXPERTS)[None, :]).astype(jnp.int32)
    earlier = jnp.cumsum(onehot, axis=0) - onehot
    position = jnp.sum(earlier * onehot, axis=1)
    slot_index = chosen * CAP + position
    place = (jnp.arange(EXPERTS * CAP)[:, None] == slot_index[None, :]).astype(jnp.bfloat16)
    routed_rows = jnp.repeat(ffn_in, TOP, axis=0)
    packed = jnp.dot(place, routed_rows, preferred_element_type=jnp.float32).astype(jnp.bfloat16)
    outgoing = jnp.repeat(packed.reshape(EXPERTS, CAP, width), per_expert, axis=0)
    received = lax.all_to_all(outgoing, "head", split_axis=0, concat_axis=0, tiled=True)
    flat_rows = received.reshape(-1, width)
    hidden = expert_hidden(flat_rows, weight_up)
    computed = jnp.dot(hidden, weight_down, preferred_element_type=jnp.float32).reshape(
        received.shape[0], received.shape[1], width
    )
    returned = lax.all_to_all(
        computed.astype(jnp.bfloat16), "head", split_axis=0, concat_axis=0, tiled=True
    ).astype(computed.dtype)
    summed = (
        returned.reshape(EXPERTS, per_expert, CAP, width).sum(axis=1).reshape(EXPERTS * CAP, width)
    )
    per_route = jnp.dot(place.astype(jnp.float32).T, summed, precision=highest).reshape(
        tok_local, TOP, width
    )
    combined = jnp.sum(share[:, :, None] * per_route, axis=1)
    layer_out = (residual.astype(jnp.float32) + combined).astype(jnp.bfloat16)
    return (layer_out[None], ssm_now[None], conv_x_new[None], conv_bc_new[None])


def solution(mesh):
    return jax.shard_map(
        shards,
        mesh=mesh,
        in_specs=(
            P("req", ("groups", "head"), None),
            P("req", "groups", "head", None, None),
            P("req", "groups", None, "head"),
            P("req", "groups", None, "head"),
            P("req", ("groups", "head"), None),
            P(),
            P(None, "head"),
            P(None, "head"),
            P(None, "head"),
            P("head"),
            P("head"),
            P("head"),
            P(None, "head"),
            P("head"),
            P(None, "head"),
            P("head"),
            P("head"),
            P("head", None),
            P(),
            P(),
            P(None, "head"),
            P("head", None),
        ),
        out_specs=(
            P("req", ("groups", "head"), None),
            P("req", "groups", "head", None, None),
            P("req", "groups", None, "head"),
            P("req", "groups", None, "head"),
        ),
        check_vma=False,
    )
```

```python
import jax
import jax.numpy as jnp
from jax import lax
from jax.experimental import pallas as pl
from jax.sharding import PartitionSpec as P

HEADS = 128
G = 8
EXPERTS = 8
TOP = 2
STEPS = 8
CAP = 2


eps = 1e-05
highest = lax.Precision.HIGHEST


def norm_rows(values, gain):
    mean_square = jnp.mean(values * values, axis=-1, keepdims=True)
    return values * lax.rsqrt(mean_square + eps) * gain


def causal_conv(past_rows, fresh_rows, kernel, offset):
    window = jnp.concatenate([past_rows, fresh_rows], axis=1)
    window_wide = window.astype(jnp.float32)
    fresh_count = fresh_rows.shape[1]
    running = offset + kernel[0] * window_wide[:, 0:fresh_count]
    for tap_index in range(1, kernel.shape[0]):
        running = running + kernel[tap_index] * window_wide[:, tap_index : tap_index + fresh_count]
    return (jax.nn.silu(running), window[:, fresh_count:])


def route_share(ffn_in, router_weight, chosen_ids):
    logits = jnp.dot(ffn_in, router_weight, preferred_element_type=jnp.float32)
    match_table = (chosen_ids[:, :, None] == jnp.arange(EXPERTS)[None, None, :]).astype(jnp.float32)
    picked = jnp.einsum("mke,me->mk", match_table, logits, precision=highest)
    first_weight = jax.nn.sigmoid(picked[:, 0] - picked[:, 1])
    return jnp.stack([first_weight, 1.0 - first_weight], axis=1)


def expert_hidden(rows_in, weight_up):
    return jnp.square(
        jnp.maximum(jnp.dot(rows_in, weight_up, preferred_element_type=jnp.float32), 0.0)
    ).astype(jnp.bfloat16)


def column_matmul_kernel(a_ref, w_ref, o_ref):
    o_ref[...] = jnp.dot(a_ref[...], w_ref[...], preferred_element_type=jnp.float32)


def column_matmul(rows, weight):
    m, k = rows.shape
    cols = weight.shape[1]
    block = min(512, cols)
    return pl.pallas_call(
        column_matmul_kernel,
        grid=(cols // block,),
        in_specs=[
            pl.BlockSpec((m, k), lambda j: (0, 0)),
            pl.BlockSpec((k, block), lambda j: (0, j)),
        ],
        out_specs=pl.BlockSpec((m, block), lambda j: (0, j)),
        out_shape=jax.ShapeDtypeStruct((m, cols), jnp.float32),
    )(rows, weight)


def ssm_scan_kernel(s_ref, dec_ref, dx_ref, b_ref, c_ref, s_out_ref, read_ref):
    tiles = s_ref.shape[1]
    steps = dec_ref.shape[2]

    def tile(j, carry):
        state = s_ref[0, j].astype(jnp.float32)
        b_all = b_ref[0, j]
        c_all = c_ref[0, j]
        dec_all = dec_ref[0, j]
        dx_all = dx_ref[0, j]
        for t in range(steps):
            fresh = dec_all[t : t + 1, :] * state + dx_all[t : t + 1, :] * b_all[:, t : t + 1]
            read_ref[0, j, t : t + 1, :] = jnp.sum(fresh * c_all[:, t : t + 1], axis=0, keepdims=True)
            state = fresh.astype(jnp.bfloat16).astype(jnp.float32)
        s_out_ref[0, j] = state.astype(jnp.bfloat16)
        return carry

    lax.fori_loop(0, tiles, tile, 0)


def ssm_scan(state_tiles, decay_tiles, dx_tiles, b_tiles, c_tiles):
    requests, tiles, state_dim, lanes = state_tiles.shape
    steps = decay_tiles.shape[2]
    big = pl.BlockSpec((1, tiles, state_dim, lanes), lambda r: (r, 0, 0, 0))
    per_step = pl.BlockSpec((1, tiles, steps, lanes), lambda r: (r, 0, 0, 0))
    columns = pl.BlockSpec((1, tiles, state_dim, steps), lambda r: (r, 0, 0, 0))
    return pl.pallas_call(
        ssm_scan_kernel,
        grid=(requests,),
        in_specs=[big, per_step, per_step, columns, columns],
        out_specs=[big, per_step],
        out_shape=[
            jax.ShapeDtypeStruct(state_tiles.shape, jnp.bfloat16),
            jax.ShapeDtypeStruct(decay_tiles.shape, jnp.float32),
        ],
    )(state_tiles, decay_tiles, dx_tiles, b_tiles, c_tiles)


def broadcast_gather(block, count):
    copies = jnp.broadcast_to(block[None], (count,) + block.shape)
    return lax.all_to_all(copies, "head", 0, 0, tiled=True)


def shards(
    tokens,
    ssm_state,
    conv_x_state,
    conv_bc_state,
    expert_ids,
    mixer_gain,
    weight_xz,
    weight_bc,
    weight_delta,
    delta_bias,
    decay_log,
    skip_gain,
    conv_x_kernel,
    conv_x_bias,
    conv_bc_kernel,
    conv_bc_bias,
    gated_gain,
    weight_out,
    ffn_gain,
    router_weight,
    weight_up,
    weight_down,
):
    head_count = lax.axis_size("head")
    my_index = lax.axis_index("head")
    tok_local = tokens.shape[1]
    width = tokens.shape[2]
    requests = ssm_state.shape[1]
    heads_local = ssm_state.shape[2]
    head_dim = ssm_state.shape[3]
    state_dim = ssm_state.shape[4]
    gathered = broadcast_gather(tokens[0], head_count)
    inputs = gathered.reshape(requests * STEPS, width)
    normed = norm_rows(inputs.astype(jnp.float32), mixer_gain).astype(jnp.bfloat16)
    proj_xz = column_matmul(normed, weight_xz).reshape(
        requests, STEPS, heads_local, 2, head_dim
    )
    x_fresh = (
        proj_xz[:, :, :, 0, :].reshape(requests, STEPS, heads_local * head_dim).astype(jnp.bfloat16)
    )
    z_gate = proj_xz[:, :, :, 1, :]
    bc_fresh = (
        jnp.dot(normed, weight_bc, preferred_element_type=jnp.float32)
        .reshape(requests, STEPS, -1)
        .astype(jnp.bfloat16)
    )
    delta = jax.nn.softplus(
        jnp.dot(normed, weight_delta, preferred_element_type=jnp.float32).reshape(
            requests, STEPS, heads_local
        )
        + delta_bias
    )
    x_conv, conv_x_new = causal_conv(conv_x_state[0], x_fresh, conv_x_kernel, conv_x_bias)
    bc_conv, conv_bc_new = causal_conv(conv_bc_state[0], bc_fresh, conv_bc_kernel, conv_bc_bias)
    bc_conv = bc_conv.astype(jnp.bfloat16)
    bc_all = jnp.moveaxis(broadcast_gather(bc_conv, head_count), 0, 2).reshape(
        requests, STEPS, -1
    )
    x_heads = x_conv.reshape(requests, STEPS, heads_local, head_dim)
    decay_rate = jnp.exp(delta * -jnp.exp(decay_log))
    pack = 2 if heads_local % 2 == 0 else 1
    tiles = heads_local // pack
    lanes = pack * head_dim

    def to_tiles(per_head):
        return per_head.reshape(requests, STEPS, tiles, lanes).transpose(0, 2, 1, 3)

    decay_tiles = to_tiles(
        jnp.broadcast_to(decay_rate[..., None], (requests, STEPS, heads_local, head_dim))
    )
    dx_tiles = to_tiles(delta[..., None] * x_heads)
    tile_group = (my_index * heads_local + jnp.arange(tiles) * pack) // (HEADS // G)
    bc_values = bc_all.astype(jnp.float32).reshape(requests, STEPS, 2, G, state_dim)
    b_tiles = jnp.take(bc_values[:, :, 0], tile_group, axis=2).transpose(0, 2, 3, 1)
    c_tiles = jnp.take(bc_values[:, :, 1], tile_group, axis=2).transpose(0, 2, 3, 1)
    state_tiles = (
        ssm_state[0]
        .reshape(requests, tiles, pack, head_dim, state_dim)
        .transpose(0, 1, 4, 2, 3)
        .reshape(requests, tiles, state_dim, lanes)
    )
    state_out, read_tiles = ssm_scan(state_tiles, decay_tiles, dx_tiles, b_tiles, c_tiles)
    ssm_now = (
        state_out.reshape(requests, tiles, state_dim, pack, head_dim)
        .transpose(0, 1, 3, 4, 2)
        .reshape(requests, heads_local, head_dim, state_dim)
    )
    scan_read = read_tiles.transpose(0, 2, 1, 3).reshape(requests, STEPS, heads_local, head_dim)
    readings = scan_read + skip_gain[:, None] * x_heads
    gated_out = readings * jax.nn.silu(z_gate)
    group_normed = (
        norm_rows(gated_out, gated_gain.reshape(heads_local, head_dim))
        .astype(jnp.bfloat16)
        .reshape(requests * STEPS, heads_local * head_dim)
    )
    per_expert = head_count // EXPERTS
    mixer_part = jnp.dot(group_normed, weight_out, preferred_element_type=jnp.float32)
    mixer_out = lax.all_to_all(
        mixer_part.reshape(head_count, tok_local, width), "head", 0, 0, tiled=True
    ).sum(axis=0)
    residual = (tokens[0].astype(jnp.float32) + mixer_out).astype(jnp.bfloat16)
    ffn_in = norm_rows(residual.astype(jnp.float32), ffn_gain).astype(jnp.bfloat16)
    share = route_share(ffn_in, router_weight, expert_ids[0])
    chosen = expert_ids[0].reshape(-1)
    onehot = (chosen[:, None] == jnp.arange(EXPERTS)[None, :]).astype(jnp.int32)
    earlier = jnp.cumsum(onehot, axis=0) - onehot
    position = jnp.sum(earlier * onehot, axis=1)
    slot_index = chosen * CAP + position
    place = (jnp.arange(EXPERTS * CAP)[:, None] == slot_index[None, :]).astype(jnp.bfloat16)
    routed_rows = jnp.repeat(ffn_in, TOP, axis=0)
    packed = jnp.dot(place, routed_rows, preferred_element_type=jnp.float32).astype(jnp.bfloat16)
    outgoing = jnp.repeat(packed.reshape(EXPERTS, CAP, width), per_expert, axis=0)
    received = lax.all_to_all(outgoing, "head", split_axis=0, concat_axis=0, tiled=True)
    flat_rows = received.reshape(-1, width)
    hidden = expert_hidden(flat_rows, weight_up)
    computed = jnp.dot(hidden, weight_down, preferred_element_type=jnp.float32).reshape(
        received.shape[0], received.shape[1], width
    )
    returned = lax.all_to_all(
        computed.astype(jnp.bfloat16), "head", split_axis=0, concat_axis=0, tiled=True
    ).astype(computed.dtype)
    summed = (
        returned.reshape(EXPERTS, per_expert, CAP, width).sum(axis=1).reshape(EXPERTS * CAP, width)
    )
    per_route = jnp.dot(place.astype(jnp.float32).T, summed, precision=highest).reshape(
        tok_local, TOP, width
    )
    combined = jnp.sum(share[:, :, None] * per_route, axis=1)
    layer_out = (residual.astype(jnp.float32) + combined).astype(jnp.bfloat16)
    return (layer_out[None], ssm_now[None], conv_x_new[None], conv_bc_new[None])


def solution(mesh):
    return jax.shard_map(
        shards,
        mesh=mesh,
        in_specs=(
            P("req", ("groups", "head"), None),
            P("req", "groups", "head", None, None),
            P("req", "groups", None, "head"),
            P("req", "groups", None, "head"),
            P("req", ("groups", "head"), None),
            P(),
            P(None, "head"),
            P(None, "head"),
            P(None, "head"),
            P("head"),
            P("head"),
            P("head"),
            P(None, "head"),
            P("head"),
            P(None, "head"),
            P("head"),
            P("head"),
            P("head", None),
            P(),
            P(),
            P(None, "head"),
            P("head", None),
        ),
        out_specs=(
            P("req", ("groups", "head"), None),
            P("req", "groups", "head", None, None),
            P("req", "groups", None, "head"),
            P("req", "groups", None, "head"),
        ),
        check_vma=False,
    )
```

```python
import jax
import jax.numpy as jnp
from jax import lax
from jax.experimental import pallas as pl
from jax.sharding import PartitionSpec as P

HEADS = 128
G = 8
EXPERTS = 8
TOP = 2
STEPS = 8
CAP = 2


eps = 1e-05
highest = lax.Precision.HIGHEST


def norm_rows(values, gain):
    mean_square = jnp.mean(values * values, axis=-1, keepdims=True)
    return values * lax.rsqrt(mean_square + eps) * gain


def causal_conv(past_rows, fresh_rows, kernel, offset):
    window = jnp.concatenate([past_rows, fresh_rows], axis=1)
    window_wide = window.astype(jnp.float32)
    fresh_count = fresh_rows.shape[1]
    running = offset + kernel[0] * window_wide[:, 0:fresh_count]
    for tap_index in range(1, kernel.shape[0]):
        running = running + kernel[tap_index] * window_wide[:, tap_index : tap_index + fresh_count]
    return (jax.nn.silu(running), window[:, fresh_count:])


def route_share(ffn_in, router_weight, chosen_ids):
    logits = jnp.dot(ffn_in, router_weight, preferred_element_type=jnp.float32)
    match_table = (chosen_ids[:, :, None] == jnp.arange(EXPERTS)[None, None, :]).astype(jnp.float32)
    picked = jnp.einsum("mke,me->mk", match_table, logits, precision=highest)
    first_weight = jax.nn.sigmoid(picked[:, 0] - picked[:, 1])
    return jnp.stack([first_weight, 1.0 - first_weight], axis=1)


def expert_hidden(rows_in, weight_up):
    return jnp.square(
        jnp.maximum(jnp.dot(rows_in, weight_up, preferred_element_type=jnp.float32), 0.0)
    ).astype(jnp.bfloat16)


def column_matmul_kernel(a_ref, w_ref, o_ref):
    o_ref[...] = jnp.dot(a_ref[...], w_ref[...], preferred_element_type=jnp.float32)


def column_matmul(rows, weight):
    m, k = rows.shape
    cols = weight.shape[1]
    block = min(512, cols)
    return pl.pallas_call(
        column_matmul_kernel,
        grid=(cols // block,),
        in_specs=[
            pl.BlockSpec((m, k), lambda j: (0, 0)),
            pl.BlockSpec((k, block), lambda j: (0, j)),
        ],
        out_specs=pl.BlockSpec((m, block), lambda j: (0, j)),
        out_shape=jax.ShapeDtypeStruct((m, cols), jnp.float32),
    )(rows, weight)


def ssm_scan_kernel(s_ref, dec_ref, dx_ref, b_ref, c_ref, s_out_ref, read_ref):
    tiles = s_ref.shape[1]
    steps = dec_ref.shape[2]

    def tile(j, carry):
        state = s_ref[0, j].astype(jnp.float32)
        b_all = b_ref[0, j]
        c_all = c_ref[0, j]
        dec_all = dec_ref[0, j]
        dx_all = dx_ref[0, j]
        for t in range(steps):
            fresh = dec_all[t : t + 1, :] * state + dx_all[t : t + 1, :] * b_all[:, t : t + 1]
            read_ref[0, j, t : t + 1, :] = jnp.sum(fresh * c_all[:, t : t + 1], axis=0, keepdims=True)
            state = fresh.astype(jnp.bfloat16).astype(jnp.float32)
        s_out_ref[0, j] = state.astype(jnp.bfloat16)
        return carry

    lax.fori_loop(0, tiles, tile, 0)


def ssm_scan(state_tiles, decay_tiles, dx_tiles, b_tiles, c_tiles):
    requests, tiles, state_dim, lanes = state_tiles.shape
    steps = decay_tiles.shape[2]
    big = pl.BlockSpec((1, tiles, state_dim, lanes), lambda r: (r, 0, 0, 0))
    per_step = pl.BlockSpec((1, tiles, steps, lanes), lambda r: (r, 0, 0, 0))
    columns = pl.BlockSpec((1, tiles, state_dim, steps), lambda r: (r, 0, 0, 0))
    return pl.pallas_call(
        ssm_scan_kernel,
        grid=(requests,),
        in_specs=[big, per_step, per_step, columns, columns],
        out_specs=[big, per_step],
        out_shape=[
            jax.ShapeDtypeStruct(state_tiles.shape, jnp.bfloat16),
            jax.ShapeDtypeStruct(decay_tiles.shape, jnp.float32),
        ],
    )(state_tiles, decay_tiles, dx_tiles, b_tiles, c_tiles)


def broadcast_gather(block, count):
    copies = jnp.broadcast_to(block[None], (count,) + block.shape)
    return lax.all_to_all(copies, "head", 0, 0, tiled=True)


def shards(
    tokens,
    ssm_state,
    conv_x_state,
    conv_bc_state,
    expert_ids,
    mixer_gain,
    weight_xz,
    weight_bc,
    weight_delta,
    delta_bias,
    decay_log,
    skip_gain,
    conv_x_kernel,
    conv_x_bias,
    conv_bc_kernel,
    conv_bc_bias,
    gated_gain,
    weight_out,
    ffn_gain,
    router_weight,
    weight_up,
    weight_down,
):
    head_count = lax.axis_size("head")
    my_index = lax.axis_index("head")
    tok_local = tokens.shape[1]
    width = tokens.shape[2]
    requests = ssm_state.shape[1]
    heads_local = ssm_state.shape[2]
    head_dim = ssm_state.shape[3]
    state_dim = ssm_state.shape[4]
    top = expert_ids.shape[2]
    broadcast_sum = head_count * requests * STEPS * width * 4 <= (8 << 20)
    if broadcast_sum:
        id_cols = jnp.zeros((tok_local, 128), jnp.bfloat16).at[:, :top].set(
            expert_ids[0].astype(jnp.bfloat16)
        )
        gathered_all = broadcast_gather(jnp.concatenate([tokens[0], id_cols], axis=1), head_count)
        gathered = gathered_all[..., :width]
        ids_all = (
            gathered_all[..., width : width + top].astype(jnp.int32).reshape(requests * STEPS, top)
        )
    else:
        gathered = broadcast_gather(tokens[0], head_count)
    inputs = gathered.reshape(requests * STEPS, width)
    normed = norm_rows(inputs.astype(jnp.float32), mixer_gain).astype(jnp.bfloat16)
    proj_xz = column_matmul(normed, weight_xz).reshape(
        requests, STEPS, heads_local, 2, head_dim
    )
    x_fresh = (
        proj_xz[:, :, :, 0, :].reshape(requests, STEPS, heads_local * head_dim).astype(jnp.bfloat16)
    )
    z_gate = proj_xz[:, :, :, 1, :]
    bc_fresh = (
        jnp.dot(normed, weight_bc, preferred_element_type=jnp.float32)
        .reshape(requests, STEPS, -1)
        .astype(jnp.bfloat16)
    )
    delta = jax.nn.softplus(
        jnp.dot(normed, weight_delta, preferred_element_type=jnp.float32).reshape(
            requests, STEPS, heads_local
        )
        + delta_bias
    )
    x_conv, conv_x_new = causal_conv(conv_x_state[0], x_fresh, conv_x_kernel, conv_x_bias)
    bc_conv, conv_bc_new = causal_conv(conv_bc_state[0], bc_fresh, conv_bc_kernel, conv_bc_bias)
    bc_conv = bc_conv.astype(jnp.bfloat16)
    bc_all = jnp.moveaxis(broadcast_gather(bc_conv, head_count), 0, 2).reshape(
        requests, STEPS, -1
    )
    x_heads = x_conv.reshape(requests, STEPS, heads_local, head_dim)
    decay_rate = jnp.exp(delta * -jnp.exp(decay_log))
    pack = 2 if heads_local % 2 == 0 else 1
    tiles = heads_local // pack
    lanes = pack * head_dim

    def to_tiles(per_head):
        return per_head.reshape(requests, STEPS, tiles, lanes).transpose(0, 2, 1, 3)

    decay_tiles = to_tiles(
        jnp.broadcast_to(decay_rate[..., None], (requests, STEPS, heads_local, head_dim))
    )
    dx_tiles = to_tiles(delta[..., None] * x_heads)
    tile_group = (my_index * heads_local + jnp.arange(tiles) * pack) // (HEADS // G)
    bc_values = bc_all.astype(jnp.float32).reshape(requests, STEPS, 2, G, state_dim)
    b_tiles = jnp.take(bc_values[:, :, 0], tile_group, axis=2).transpose(0, 2, 3, 1)
    c_tiles = jnp.take(bc_values[:, :, 1], tile_group, axis=2).transpose(0, 2, 3, 1)
    state_tiles = (
        ssm_state[0]
        .reshape(requests, tiles, pack, head_dim, state_dim)
        .transpose(0, 1, 4, 2, 3)
        .reshape(requests, tiles, state_dim, lanes)
    )
    state_out, read_tiles = ssm_scan(state_tiles, decay_tiles, dx_tiles, b_tiles, c_tiles)
    ssm_now = (
        state_out.reshape(requests, tiles, state_dim, pack, head_dim)
        .transpose(0, 1, 3, 4, 2)
        .reshape(requests, heads_local, head_dim, state_dim)
    )
    scan_read = read_tiles.transpose(0, 2, 1, 3).reshape(requests, STEPS, heads_local, head_dim)
    readings = scan_read + skip_gain[:, None] * x_heads
    gated_out = readings * jax.nn.silu(z_gate)
    group_normed = (
        norm_rows(gated_out, gated_gain.reshape(heads_local, head_dim))
        .astype(jnp.bfloat16)
        .reshape(requests * STEPS, heads_local * head_dim)
    )
    per_expert = head_count // EXPERTS
    mixer_part = jnp.dot(group_normed, weight_out, preferred_element_type=jnp.float32)
    if broadcast_sum:
        mixer_all = broadcast_gather(mixer_part, head_count).sum(axis=0)
        residual_all = (inputs.astype(jnp.float32) + mixer_all).astype(jnp.bfloat16)
        ffn_all = norm_rows(residual_all.astype(jnp.float32), ffn_gain).astype(jnp.bfloat16)
        share_all = route_share(ffn_all, router_weight, ids_all)
        my_expert = my_index // per_expert
        row_weight = jnp.sum(share_all * (ids_all == my_expert).astype(jnp.float32), axis=1)
        hidden = expert_hidden(ffn_all, weight_up)
        computed = jnp.dot(hidden, weight_down, preferred_element_type=jnp.float32)
        contrib = row_weight[:, None] * computed
        combined = lax.all_to_all(
            contrib.reshape(head_count, tok_local, width), "head", 0, 0, tiled=True
        ).sum(axis=0)
        residual = lax.dynamic_slice_in_dim(residual_all, my_index * tok_local, tok_local, axis=0)
        layer_out = (residual.astype(jnp.float32) + combined).astype(jnp.bfloat16)
        return (layer_out[None], ssm_now[None], conv_x_new[None], conv_bc_new[None])
    mixer_out = lax.all_to_all(
        mixer_part.reshape(head_count, tok_local, width), "head", 0, 0, tiled=True
    ).sum(axis=0)
    residual = (tokens[0].astype(jnp.float32) + mixer_out).astype(jnp.bfloat16)
    ffn_in = norm_rows(residual.astype(jnp.float32), ffn_gain).astype(jnp.bfloat16)
    share = route_share(ffn_in, router_weight, expert_ids[0])
    chosen = expert_ids[0].reshape(-1)
    onehot = (chosen[:, None] == jnp.arange(EXPERTS)[None, :]).astype(jnp.int32)
    earlier = jnp.cumsum(onehot, axis=0) - onehot
    position = jnp.sum(earlier * onehot, axis=1)
    slot_index = chosen * CAP + position
    place = (jnp.arange(EXPERTS * CAP)[:, None] == slot_index[None, :]).astype(jnp.bfloat16)
    routed_rows = jnp.repeat(ffn_in, TOP, axis=0)
    packed = jnp.dot(place, routed_rows, preferred_element_type=jnp.float32).astype(jnp.bfloat16)
    outgoing = jnp.repeat(packed.reshape(EXPERTS, CAP, width), per_expert, axis=0)
    received = lax.all_to_all(outgoing, "head", split_axis=0, concat_axis=0, tiled=True)
    flat_rows = received.reshape(-1, width)
    hidden = expert_hidden(flat_rows, weight_up)
    computed = jnp.dot(hidden, weight_down, preferred_element_type=jnp.float32).reshape(
        received.shape[0], received.shape[1], width
    )
    returned = lax.all_to_all(
        computed.astype(jnp.bfloat16), "head", split_axis=0, concat_axis=0, tiled=True
    ).astype(computed.dtype)
    summed = (
        returned.reshape(EXPERTS, per_expert, CAP, width).sum(axis=1).reshape(EXPERTS * CAP, width)
    )
    per_route = jnp.dot(place.astype(jnp.float32).T, summed, precision=highest).reshape(
        tok_local, TOP, width
    )
    combined = jnp.sum(share[:, :, None] * per_route, axis=1)
    layer_out = (residual.astype(jnp.float32) + combined).astype(jnp.bfloat16)
    return (layer_out[None], ssm_now[None], conv_x_new[None], conv_bc_new[None])


def solution(mesh):
    return jax.shard_map(
        shards,
        mesh=mesh,
        in_specs=(
            P("req", ("groups", "head"), None),
            P("req", "groups", "head", None, None),
            P("req", "groups", None, "head"),
            P("req", "groups", None, "head"),
            P("req", ("groups", "head"), None),
            P(),
            P(None, "head"),
            P(None, "head"),
            P(None, "head"),
            P("head"),
            P("head"),
            P("head"),
            P(None, "head"),
            P("head"),
            P(None, "head"),
            P("head"),
            P("head"),
            P("head", None),
            P(),
            P(),
            P(None, "head"),
            P("head", None),
        ),
        out_specs=(
            P("req", ("groups", "head"), None),
            P("req", "groups", "head", None, None),
            P("req", "groups", None, "head"),
            P("req", "groups", None, "head"),
        ),
        check_vma=False,
    )
```

```python
import jax
import jax.numpy as jnp
from jax import lax
from jax.experimental import pallas as pl
from jax.sharding import PartitionSpec as P

HEADS = 128
G = 8
EXPERTS = 8
TOP = 2
STEPS = 8
CAP = 2


eps = 1e-05
highest = lax.Precision.HIGHEST


def norm_rows(values, gain):
    mean_square = jnp.mean(values * values, axis=-1, keepdims=True)
    return values * lax.rsqrt(mean_square + eps) * gain


def causal_conv(past_rows, fresh_rows, kernel, offset):
    window = jnp.concatenate([past_rows, fresh_rows], axis=1)
    window_wide = window.astype(jnp.float32)
    fresh_count = fresh_rows.shape[1]
    running = offset + kernel[0] * window_wide[:, 0:fresh_count]
    for tap_index in range(1, kernel.shape[0]):
        running = running + kernel[tap_index] * window_wide[:, tap_index : tap_index + fresh_count]
    return (jax.nn.silu(running), window[:, fresh_count:])


def route_share(ffn_in, router_weight, chosen_ids):
    logits = jnp.dot(ffn_in, router_weight, preferred_element_type=jnp.float32)
    match_table = (chosen_ids[:, :, None] == jnp.arange(EXPERTS)[None, None, :]).astype(jnp.float32)
    picked = jnp.einsum("mke,me->mk", match_table, logits, precision=highest)
    first_weight = jax.nn.sigmoid(picked[:, 0] - picked[:, 1])
    return jnp.stack([first_weight, 1.0 - first_weight], axis=1)


def expert_hidden(rows_in, weight_up):
    return jnp.square(
        jnp.maximum(jnp.dot(rows_in, weight_up, preferred_element_type=jnp.float32), 0.0)
    ).astype(jnp.bfloat16)


def column_matmul_kernel(a_ref, w_ref, o_ref):
    o_ref[...] = jnp.dot(a_ref[...], w_ref[...], preferred_element_type=jnp.float32)


def column_matmul(rows, weight):
    m, k = rows.shape
    cols = weight.shape[1]
    block = min(512, cols)
    return pl.pallas_call(
        column_matmul_kernel,
        grid=(cols // block,),
        in_specs=[
            pl.BlockSpec((m, k), lambda j: (0, 0)),
            pl.BlockSpec((k, block), lambda j: (0, j)),
        ],
        out_specs=pl.BlockSpec((m, block), lambda j: (0, j)),
        out_shape=jax.ShapeDtypeStruct((m, cols), jnp.float32),
    )(rows, weight)


def ssm_scan_kernel(s_ref, dec_ref, dx_ref, b_ref, c_ref, s_out_ref, read_ref):
    tiles = s_ref.shape[1]
    lanes = s_ref.shape[3]
    steps = dec_ref.shape[1]
    for j in range(tiles):
        cols = slice(j * lanes, (j + 1) * lanes)
        state = s_ref[0, j].astype(jnp.float32)
        b_all = b_ref[0, j].T
        c_all = c_ref[0, j].T
        dec_all = dec_ref[0, :, cols]
        dx_all = dx_ref[0, :, cols]
        for t in range(steps):
            fresh = dec_all[t : t + 1, :] * state + dx_all[t : t + 1, :] * b_all[:, t : t + 1]
            read_ref[0, t : t + 1, cols] = jnp.sum(fresh * c_all[:, t : t + 1], axis=0, keepdims=True)
            state = fresh.astype(jnp.bfloat16).astype(jnp.float32)
        s_out_ref[0, j] = state.astype(jnp.bfloat16)


def ssm_scan(state_tiles, decay_rows, dx_rows, b_rows, c_rows):
    requests, tiles, state_dim, lanes = state_tiles.shape
    steps = decay_rows.shape[1]
    big = pl.BlockSpec((1, tiles, state_dim, lanes), lambda r: (r, 0, 0, 0))
    per_step = pl.BlockSpec((1, steps, tiles * lanes), lambda r: (r, 0, 0))
    rows = pl.BlockSpec((1, tiles, steps, state_dim), lambda r: (r, 0, 0, 0))
    return pl.pallas_call(
        ssm_scan_kernel,
        grid=(requests,),
        in_specs=[big, per_step, per_step, rows, rows],
        out_specs=[big, per_step],
        out_shape=[
            jax.ShapeDtypeStruct(state_tiles.shape, jnp.bfloat16),
            jax.ShapeDtypeStruct(decay_rows.shape, jnp.float32),
        ],
    )(state_tiles, decay_rows, dx_rows, b_rows, c_rows)


def broadcast_gather(block, count):
    copies = jnp.broadcast_to(block[None], (count,) + block.shape)
    return lax.all_to_all(copies, "head", 0, 0, tiled=True)


def shards(
    tokens,
    ssm_state,
    conv_x_state,
    conv_bc_state,
    expert_ids,
    mixer_gain,
    weight_xz,
    weight_bc,
    weight_delta,
    delta_bias,
    decay_log,
    skip_gain,
    conv_x_kernel,
    conv_x_bias,
    conv_bc_kernel,
    conv_bc_bias,
    gated_gain,
    weight_out,
    ffn_gain,
    router_weight,
    weight_up,
    weight_down,
):
    head_count = lax.axis_size("head")
    my_index = lax.axis_index("head")
    tok_local = tokens.shape[1]
    width = tokens.shape[2]
    requests = ssm_state.shape[1]
    heads_local = ssm_state.shape[2]
    head_dim = ssm_state.shape[3]
    state_dim = ssm_state.shape[4]
    gathered = broadcast_gather(tokens[0], head_count)
    inputs = gathered.reshape(requests * STEPS, width)
    normed = norm_rows(inputs.astype(jnp.float32), mixer_gain).astype(jnp.bfloat16)
    proj_xz = column_matmul(normed, weight_xz).reshape(
        requests, STEPS, heads_local, 2, head_dim
    )
    x_fresh = (
        proj_xz[:, :, :, 0, :].reshape(requests, STEPS, heads_local * head_dim).astype(jnp.bfloat16)
    )
    z_gate = proj_xz[:, :, :, 1, :]
    bc_fresh = (
        jnp.dot(normed, weight_bc, preferred_element_type=jnp.float32)
        .reshape(requests, STEPS, -1)
        .astype(jnp.bfloat16)
    )
    delta = jax.nn.softplus(
        jnp.dot(normed, weight_delta, preferred_element_type=jnp.float32).reshape(
            requests, STEPS, heads_local
        )
        + delta_bias
    )
    x_conv, conv_x_new = causal_conv(conv_x_state[0], x_fresh, conv_x_kernel, conv_x_bias)
    bc_conv, conv_bc_new = causal_conv(conv_bc_state[0], bc_fresh, conv_bc_kernel, conv_bc_bias)
    bc_conv = bc_conv.astype(jnp.bfloat16)
    bc_all = jnp.moveaxis(broadcast_gather(bc_conv, head_count), 0, 2).reshape(
        requests, STEPS, -1
    )
    x_heads = x_conv.reshape(requests, STEPS, heads_local, head_dim)
    decay_rate = jnp.exp(delta * -jnp.exp(decay_log))
    pack = 2 if heads_local % 2 == 0 else 1
    tiles = heads_local // pack
    lanes = pack * head_dim

    decay_rows = jnp.broadcast_to(
        decay_rate[..., None], (requests, STEPS, heads_local, head_dim)
    ).reshape(requests, STEPS, heads_local * head_dim)
    dx_rows = (delta[..., None] * x_heads).reshape(requests, STEPS, heads_local * head_dim)
    tile_group = (my_index * heads_local + jnp.arange(tiles) * pack) // (HEADS // G)
    bc_values = bc_all.astype(jnp.float32).reshape(requests, STEPS, 2, G, state_dim)
    b_rows = jnp.take(bc_values[:, :, 0], tile_group, axis=2).transpose(0, 2, 1, 3)
    c_rows = jnp.take(bc_values[:, :, 1], tile_group, axis=2).transpose(0, 2, 1, 3)
    state_tiles = (
        ssm_state[0]
        .reshape(requests, tiles, pack, head_dim, state_dim)
        .transpose(0, 1, 4, 2, 3)
        .reshape(requests, tiles, state_dim, lanes)
    )
    state_out, read_rows = ssm_scan(state_tiles, decay_rows, dx_rows, b_rows, c_rows)
    ssm_now = (
        state_out.reshape(requests, tiles, state_dim, pack, head_dim)
        .transpose(0, 1, 3, 4, 2)
        .reshape(requests, heads_local, head_dim, state_dim)
    )
    scan_read = read_rows.reshape(requests, STEPS, heads_local, head_dim)
    readings = scan_read + skip_gain[:, None] * x_heads
    gated_out = readings * jax.nn.silu(z_gate)
    group_normed = (
        norm_rows(gated_out, gated_gain.reshape(heads_local, head_dim))
        .astype(jnp.bfloat16)
        .reshape(requests * STEPS, heads_local * head_dim)
    )
    per_expert = head_count // EXPERTS
    mixer_part = jnp.dot(group_normed, weight_out, preferred_element_type=jnp.float32)
    mixer_out = lax.all_to_all(
        mixer_part.reshape(head_count, tok_local, width), "head", 0, 0, tiled=True
    ).sum(axis=0)
    residual = (tokens[0].astype(jnp.float32) + mixer_out).astype(jnp.bfloat16)
    ffn_in = norm_rows(residual.astype(jnp.float32), ffn_gain).astype(jnp.bfloat16)
    share = route_share(ffn_in, router_weight, expert_ids[0])
    chosen = expert_ids[0].reshape(-1)
    onehot = (chosen[:, None] == jnp.arange(EXPERTS)[None, :]).astype(jnp.int32)
    earlier = jnp.cumsum(onehot, axis=0) - onehot
    position = jnp.sum(earlier * onehot, axis=1)
    slot_index = chosen * CAP + position
    place = (jnp.arange(EXPERTS * CAP)[:, None] == slot_index[None, :]).astype(jnp.bfloat16)
    routed_rows = jnp.repeat(ffn_in, TOP, axis=0)
    packed = jnp.dot(place, routed_rows, preferred_element_type=jnp.float32).astype(jnp.bfloat16)
    outgoing = jnp.repeat(packed.reshape(EXPERTS, CAP, width), per_expert, axis=0)
    received = lax.all_to_all(outgoing, "head", split_axis=0, concat_axis=0, tiled=True)
    flat_rows = received.reshape(-1, width)
    hidden = expert_hidden(flat_rows, weight_up)
    computed = jnp.dot(hidden, weight_down, preferred_element_type=jnp.float32).reshape(
        received.shape[0], received.shape[1], width
    )
    returned = lax.all_to_all(
        computed.astype(jnp.bfloat16), "head", split_axis=0, concat_axis=0, tiled=True
    ).astype(computed.dtype)
    summed = (
        returned.reshape(EXPERTS, per_expert, CAP, width).sum(axis=1).reshape(EXPERTS * CAP, width)
    )
    per_route = jnp.dot(place.astype(jnp.float32).T, summed, precision=highest).reshape(
        tok_local, TOP, width
    )
    combined = jnp.sum(share[:, :, None] * per_route, axis=1)
    layer_out = (residual.astype(jnp.float32) + combined).astype(jnp.bfloat16)
    return (layer_out[None], ssm_now[None], conv_x_new[None], conv_bc_new[None])


def solution(mesh):
    return jax.shard_map(
        shards,
        mesh=mesh,
        in_specs=(
            P("req", ("groups", "head"), None),
            P("req", "groups", "head", None, None),
            P("req", "groups", None, "head"),
            P("req", "groups", None, "head"),
            P("req", ("groups", "head"), None),
            P(),
            P(None, "head"),
            P(None, "head"),
            P(None, "head"),
            P("head"),
            P("head"),
            P("head"),
            P(None, "head"),
            P("head"),
            P(None, "head"),
            P("head"),
            P("head"),
            P("head", None),
            P(),
            P(),
            P(None, "head"),
            P("head", None),
        ),
        out_specs=(
            P("req", ("groups", "head"), None),
            P("req", "groups", "head", None, None),
            P("req", "groups", None, "head"),
            P("req", "groups", None, "head"),
        ),
        check_vma=False,
    )
```

```python
import jax
import jax.numpy as jnp
from jax import lax
from jax.experimental import pallas as pl
from jax.sharding import PartitionSpec as P

HEADS = 128
G = 8
EXPERTS = 8
TOP = 2
STEPS = 8
CAP = 2


eps = 1e-05
highest = lax.Precision.HIGHEST


def norm_rows(values, gain):
    mean_square = jnp.mean(values * values, axis=-1, keepdims=True)
    return values * lax.rsqrt(mean_square + eps) * gain


def causal_conv(past_rows, fresh_rows, kernel, offset):
    window = jnp.concatenate([past_rows, fresh_rows], axis=1)
    window_wide = window.astype(jnp.float32)
    fresh_count = fresh_rows.shape[1]
    running = offset + kernel[0] * window_wide[:, 0:fresh_count]
    for tap_index in range(1, kernel.shape[0]):
        running = running + kernel[tap_index] * window_wide[:, tap_index : tap_index + fresh_count]
    return (jax.nn.silu(running), window[:, fresh_count:])


def route_share(ffn_in, router_weight, chosen_ids):
    logits = jnp.dot(ffn_in, router_weight, preferred_element_type=jnp.float32)
    match_table = (chosen_ids[:, :, None] == jnp.arange(EXPERTS)[None, None, :]).astype(jnp.float32)
    picked = jnp.einsum("mke,me->mk", match_table, logits, precision=highest)
    first_weight = jax.nn.sigmoid(picked[:, 0] - picked[:, 1])
    return jnp.stack([first_weight, 1.0 - first_weight], axis=1)


def expert_hidden(rows_in, weight_up):
    return jnp.square(
        jnp.maximum(jnp.dot(rows_in, weight_up, preferred_element_type=jnp.float32), 0.0)
    ).astype(jnp.bfloat16)


def column_matmul_kernel(a_ref, w_ref, o_ref):
    o_ref[...] = jnp.dot(a_ref[...], w_ref[...], preferred_element_type=jnp.float32)


def column_matmul(rows, weight):
    m, k = rows.shape
    cols = weight.shape[1]
    block = min(512, cols)
    return pl.pallas_call(
        column_matmul_kernel,
        grid=(cols // block,),
        in_specs=[
            pl.BlockSpec((m, k), lambda j: (0, 0)),
            pl.BlockSpec((k, block), lambda j: (0, j)),
        ],
        out_specs=pl.BlockSpec((m, block), lambda j: (0, j)),
        out_shape=jax.ShapeDtypeStruct((m, cols), jnp.float32),
        cost_estimate=pl.CostEstimate(
            flops=2 * m * k * cols,
            transcendentals=0,
            bytes_accessed=2 * (m * k + k * cols) + 4 * m * cols,
        ),
    )(rows, weight)


def ssm_scan_kernel(s_ref, dec_ref, dx_ref, b_ref, c_ref, s_out_ref, read_ref):
    tiles = s_ref.shape[1]
    lanes = s_ref.shape[3]
    steps = dec_ref.shape[1]
    for j in range(tiles):
        cols = slice(j * lanes, (j + 1) * lanes)
        state = s_ref[0, j].astype(jnp.float32)
        b_all = b_ref[0, j].T
        c_all = c_ref[0, j].T
        dec_all = dec_ref[0, :, cols]
        dx_all = dx_ref[0, :, cols]
        for t in range(steps):
            fresh = dec_all[t : t + 1, :] * state + dx_all[t : t + 1, :] * b_all[:, t : t + 1]
            read_ref[0, t : t + 1, cols] = jnp.sum(fresh * c_all[:, t : t + 1], axis=0, keepdims=True)
            state = fresh.astype(jnp.bfloat16).astype(jnp.float32)
        s_out_ref[0, j] = state.astype(jnp.bfloat16)


def ssm_scan(state_tiles, decay_rows, dx_rows, b_rows, c_rows):
    requests, tiles, state_dim, lanes = state_tiles.shape
    steps = decay_rows.shape[1]
    big = pl.BlockSpec((1, tiles, state_dim, lanes), lambda r: (r, 0, 0, 0))
    per_step = pl.BlockSpec((1, steps, tiles * lanes), lambda r: (r, 0, 0))
    rows = pl.BlockSpec((1, tiles, steps, state_dim), lambda r: (r, 0, 0, 0))
    return pl.pallas_call(
        ssm_scan_kernel,
        grid=(requests,),
        in_specs=[big, per_step, per_step, rows, rows],
        out_specs=[big, per_step],
        out_shape=[
            jax.ShapeDtypeStruct(state_tiles.shape, jnp.bfloat16),
            jax.ShapeDtypeStruct(decay_rows.shape, jnp.float32),
        ],
    )(state_tiles, decay_rows, dx_rows, b_rows, c_rows)


def broadcast_gather(block, count):
    copies = jnp.broadcast_to(block[None], (count,) + block.shape)
    return lax.all_to_all(copies, "head", 0, 0, tiled=True)


def shards(
    tokens,
    ssm_state,
    conv_x_state,
    conv_bc_state,
    expert_ids,
    mixer_gain,
    weight_xz,
    weight_bc,
    weight_delta,
    delta_bias,
    decay_log,
    skip_gain,
    conv_x_kernel,
    conv_x_bias,
    conv_bc_kernel,
    conv_bc_bias,
    gated_gain,
    weight_out,
    ffn_gain,
    router_weight,
    weight_up,
    weight_down,
):
    head_count = lax.axis_size("head")
    my_index = lax.axis_index("head")
    tok_local = tokens.shape[1]
    width = tokens.shape[2]
    requests = ssm_state.shape[1]
    heads_local = ssm_state.shape[2]
    head_dim = ssm_state.shape[3]
    state_dim = ssm_state.shape[4]
    gathered = broadcast_gather(tokens[0], head_count)
    inputs = gathered.reshape(requests * STEPS, width)
    normed = norm_rows(inputs.astype(jnp.float32), mixer_gain).astype(jnp.bfloat16)
    bc_fresh = (
        jnp.dot(normed, weight_bc, preferred_element_type=jnp.float32)
        .reshape(requests, STEPS, -1)
        .astype(jnp.bfloat16)
    )
    bc_conv, conv_bc_new = causal_conv(conv_bc_state[0], bc_fresh, conv_bc_kernel, conv_bc_bias)
    bc_conv = bc_conv.astype(jnp.bfloat16)
    bc_all = jnp.moveaxis(broadcast_gather(bc_conv, head_count), 0, 2).reshape(
        requests, STEPS, -1
    )
    proj_xz = column_matmul(normed, weight_xz).reshape(
        requests, STEPS, heads_local, 2 * head_dim
    )
    x_fresh = (
        proj_xz[..., :head_dim].reshape(requests, STEPS, heads_local * head_dim).astype(jnp.bfloat16)
    )
    z_gate = proj_xz[..., head_dim:]
    delta = jax.nn.softplus(
        jnp.dot(normed, weight_delta, preferred_element_type=jnp.float32).reshape(
            requests, STEPS, heads_local
        )
        + delta_bias
    )
    x_conv, conv_x_new = causal_conv(conv_x_state[0], x_fresh, conv_x_kernel, conv_x_bias)
    x_heads = x_conv.reshape(requests, STEPS, heads_local, head_dim)
    decay_rate = jnp.exp(delta * -jnp.exp(decay_log))
    pack = 2 if heads_local % 2 == 0 else 1
    tiles = heads_local // pack
    lanes = pack * head_dim

    decay_rows = jnp.broadcast_to(
        decay_rate[..., None], (requests, STEPS, heads_local, head_dim)
    ).reshape(requests, STEPS, heads_local * head_dim)
    dx_rows = (delta[..., None] * x_heads).reshape(requests, STEPS, heads_local * head_dim)
    tile_group = (my_index * heads_local + jnp.arange(tiles) * pack) // (HEADS // G)
    bc_values = bc_all.astype(jnp.float32).reshape(requests, STEPS, 2, G, state_dim)
    b_rows = jnp.take(bc_values[:, :, 0], tile_group, axis=2).transpose(0, 2, 1, 3)
    c_rows = jnp.take(bc_values[:, :, 1], tile_group, axis=2).transpose(0, 2, 1, 3)
    state_tiles = (
        ssm_state[0]
        .reshape(requests, tiles, pack, head_dim, state_dim)
        .transpose(0, 1, 4, 2, 3)
        .reshape(requests, tiles, state_dim, lanes)
    )
    state_out, read_rows = ssm_scan(state_tiles, decay_rows, dx_rows, b_rows, c_rows)
    ssm_now = (
        state_out.reshape(requests, tiles, state_dim, pack, head_dim)
        .transpose(0, 1, 3, 4, 2)
        .reshape(requests, heads_local, head_dim, state_dim)
    )
    scan_read = read_rows.reshape(requests, STEPS, heads_local, head_dim)
    readings = scan_read + skip_gain[:, None] * x_heads
    gated_out = readings * jax.nn.silu(z_gate)
    group_normed = (
        norm_rows(gated_out, gated_gain.reshape(heads_local, head_dim))
        .astype(jnp.bfloat16)
        .reshape(requests * STEPS, heads_local * head_dim)
    )
    per_expert = head_count // EXPERTS
    mixer_part = jnp.dot(group_normed, weight_out, preferred_element_type=jnp.float32)
    mixer_out = lax.all_to_all(
        mixer_part.reshape(head_count, tok_local, width), "head", 0, 0, tiled=True
    ).sum(axis=0)
    residual = (tokens[0].astype(jnp.float32) + mixer_out).astype(jnp.bfloat16)
    ffn_in = norm_rows(residual.astype(jnp.float32), ffn_gain).astype(jnp.bfloat16)
    share = route_share(ffn_in, router_weight, expert_ids[0])
    chosen = expert_ids[0].reshape(-1)
    onehot = (chosen[:, None] == jnp.arange(EXPERTS)[None, :]).astype(jnp.int32)
    earlier = jnp.cumsum(onehot, axis=0) - onehot
    position = jnp.sum(earlier * onehot, axis=1)
    slot_index = chosen * CAP + position
    place = (jnp.arange(EXPERTS * CAP)[:, None] == slot_index[None, :]).astype(jnp.bfloat16)
    routed_rows = jnp.repeat(ffn_in, TOP, axis=0)
    packed = jnp.dot(place, routed_rows, preferred_element_type=jnp.float32).astype(jnp.bfloat16)
    outgoing = jnp.repeat(packed.reshape(EXPERTS, CAP, width), per_expert, axis=0)
    received = lax.all_to_all(outgoing, "head", split_axis=0, concat_axis=0, tiled=True)
    flat_rows = received.reshape(-1, width)
    hidden = expert_hidden(flat_rows, weight_up)
    computed = jnp.dot(hidden, weight_down, preferred_element_type=jnp.float32).reshape(
        received.shape[0], received.shape[1], width
    )
    returned = lax.all_to_all(
        computed.astype(jnp.bfloat16), "head", split_axis=0, concat_axis=0, tiled=True
    ).astype(computed.dtype)
    summed = (
        returned.reshape(EXPERTS, per_expert, CAP, width).sum(axis=1).reshape(EXPERTS * CAP, width)
    )
    per_route = jnp.dot(place.astype(jnp.float32).T, summed, precision=highest).reshape(
        tok_local, TOP, width
    )
    combined = jnp.sum(share[:, :, None] * per_route, axis=1)
    layer_out = (residual.astype(jnp.float32) + combined).astype(jnp.bfloat16)
    return (layer_out[None], ssm_now[None], conv_x_new[None], conv_bc_new[None])


def solution(mesh):
    return jax.shard_map(
        shards,
        mesh=mesh,
        in_specs=(
            P("req", ("groups", "head"), None),
            P("req", "groups", "head", None, None),
            P("req", "groups", None, "head"),
            P("req", "groups", None, "head"),
            P("req", ("groups", "head"), None),
            P(),
            P(None, "head"),
            P(None, "head"),
            P(None, "head"),
            P("head"),
            P("head"),
            P("head"),
            P(None, "head"),
            P("head"),
            P(None, "head"),
            P("head"),
            P("head"),
            P("head", None),
            P(),
            P(),
            P(None, "head"),
            P("head", None),
        ),
        out_specs=(
            P("req", ("groups", "head"), None),
            P("req", "groups", "head", None, None),
            P("req", "groups", None, "head"),
            P("req", "groups", None, "head"),
        ),
        check_vma=False,
    )
```

```python
import jax
import jax.numpy as jnp
from jax import lax
from jax.experimental import pallas as pl
from jax.experimental.pallas import tpu as pltpu
from jax.sharding import PartitionSpec as P

HEADS = 128
G = 8
EXPERTS = 8
TOP = 2
STEPS = 8
CAP = 2


eps = 1e-05
highest = lax.Precision.HIGHEST


def norm_rows(values, gain):
    mean_square = jnp.mean(values * values, axis=-1, keepdims=True)
    return values * lax.rsqrt(mean_square + eps) * gain


def causal_conv(past_rows, fresh_rows, kernel, offset):
    window = jnp.concatenate([past_rows, fresh_rows], axis=1)
    window_wide = window.astype(jnp.float32)
    fresh_count = fresh_rows.shape[1]
    running = offset + kernel[0] * window_wide[:, 0:fresh_count]
    for tap_index in range(1, kernel.shape[0]):
        running = running + kernel[tap_index] * window_wide[:, tap_index : tap_index + fresh_count]
    return (jax.nn.silu(running), window[:, fresh_count:])


def route_share(ffn_in, router_weight, chosen_ids):
    logits = jnp.dot(ffn_in, router_weight, preferred_element_type=jnp.float32)
    match_table = (chosen_ids[:, :, None] == jnp.arange(EXPERTS)[None, None, :]).astype(jnp.float32)
    picked = jnp.einsum("mke,me->mk", match_table, logits, precision=highest)
    first_weight = jax.nn.sigmoid(picked[:, 0] - picked[:, 1])
    return jnp.stack([first_weight, 1.0 - first_weight], axis=1)


def expert_hidden(rows_in, weight_up):
    return jnp.square(
        jnp.maximum(jnp.dot(rows_in, weight_up, preferred_element_type=jnp.float32), 0.0)
    ).astype(jnp.bfloat16)


def column_matmul_kernel(a_ref, w_ref, o_ref):
    o_ref[...] = jnp.dot(a_ref[...], w_ref[...], preferred_element_type=jnp.float32)


def column_matmul(rows, weight):
    m, k = rows.shape
    cols = weight.shape[1]
    block = min(512, cols)
    return pl.pallas_call(
        column_matmul_kernel,
        grid=(cols // block,),
        in_specs=[
            pl.BlockSpec((m, k), lambda j: (0, 0)),
            pl.BlockSpec((k, block), lambda j: (0, j)),
        ],
        out_specs=pl.BlockSpec((m, block), lambda j: (0, j)),
        out_shape=jax.ShapeDtypeStruct((m, cols), jnp.float32),
        cost_estimate=pl.CostEstimate(
            flops=2 * m * k * cols,
            transcendentals=0,
            bytes_accessed=2 * (m * k + k * cols) + 4 * m * cols,
        ),
    )(rows, weight)


def expert_ffn_kernel(x_ref, up_ref, down_ref, o_ref, acc_ref):
    j = pl.program_id(0)
    hidden = jnp.dot(x_ref[...], up_ref[...], preferred_element_type=jnp.float32)
    hidden = jnp.square(jnp.maximum(hidden, 0.0)).astype(jnp.bfloat16)
    part = jnp.dot(hidden, down_ref[...], preferred_element_type=jnp.float32)

    @pl.when(j == 0)
    def _():
        acc_ref[...] = part

    @pl.when(j > 0)
    def _():
        acc_ref[...] += part

    @pl.when(j == pl.num_programs(0) - 1)
    def _():
        o_ref[...] = acc_ref[...].astype(o_ref.dtype)


def expert_ffn(rows, weight_up, weight_down):
    m, width = rows.shape
    hidden_units = weight_up.shape[1]
    block = min(512, hidden_units)
    return pl.pallas_call(
        expert_ffn_kernel,
        grid=(hidden_units // block,),
        in_specs=[
            pl.BlockSpec((m, width), lambda j: (0, 0)),
            pl.BlockSpec((width, block), lambda j: (0, j)),
            pl.BlockSpec((block, width), lambda j: (j, 0)),
        ],
        out_specs=pl.BlockSpec((m, width), lambda j: (0, 0)),
        out_shape=jax.ShapeDtypeStruct((m, width), jnp.bfloat16),
        scratch_shapes=[pltpu.VMEM((m, width), jnp.float32)],
        cost_estimate=pl.CostEstimate(
            flops=4 * m * width * hidden_units,
            transcendentals=0,
            bytes_accessed=4 * width * hidden_units + 4 * m * width,
        ),
    )(rows, weight_up, weight_down)


def ssm_scan_kernel(s_ref, dec_ref, dx_ref, b_ref, c_ref, s_out_ref, read_ref):
    tiles = s_ref.shape[1]
    lanes = s_ref.shape[3]
    steps = dec_ref.shape[1]
    for j in range(tiles):
        cols = slice(j * lanes, (j + 1) * lanes)
        state = s_ref[0, j].astype(jnp.float32)
        b_all = b_ref[0, j].T
        c_all = c_ref[0, j].T
        dec_all = dec_ref[0, :, cols]
        dx_all = dx_ref[0, :, cols]
        for t in range(steps):
            fresh = dec_all[t : t + 1, :] * state + dx_all[t : t + 1, :] * b_all[:, t : t + 1]
            read_ref[0, t : t + 1, cols] = jnp.sum(fresh * c_all[:, t : t + 1], axis=0, keepdims=True)
            state = fresh.astype(jnp.bfloat16).astype(jnp.float32)
        s_out_ref[0, j] = state.astype(jnp.bfloat16)


def ssm_scan(state_tiles, decay_rows, dx_rows, b_rows, c_rows):
    requests, tiles, state_dim, lanes = state_tiles.shape
    steps = decay_rows.shape[1]
    big = pl.BlockSpec((1, tiles, state_dim, lanes), lambda r: (r, 0, 0, 0))
    per_step = pl.BlockSpec((1, steps, tiles * lanes), lambda r: (r, 0, 0))
    rows = pl.BlockSpec((1, tiles, steps, state_dim), lambda r: (r, 0, 0, 0))
    return pl.pallas_call(
        ssm_scan_kernel,
        grid=(requests,),
        in_specs=[big, per_step, per_step, rows, rows],
        out_specs=[big, per_step],
        out_shape=[
            jax.ShapeDtypeStruct(state_tiles.shape, jnp.bfloat16),
            jax.ShapeDtypeStruct(decay_rows.shape, jnp.float32),
        ],
    )(state_tiles, decay_rows, dx_rows, b_rows, c_rows)


def broadcast_gather(block, count):
    copies = jnp.broadcast_to(block[None], (count,) + block.shape)
    return lax.all_to_all(copies, "head", 0, 0, tiled=True)


def shards(
    tokens,
    ssm_state,
    conv_x_state,
    conv_bc_state,
    expert_ids,
    mixer_gain,
    weight_xz,
    weight_bc,
    weight_delta,
    delta_bias,
    decay_log,
    skip_gain,
    conv_x_kernel,
    conv_x_bias,
    conv_bc_kernel,
    conv_bc_bias,
    gated_gain,
    weight_out,
    ffn_gain,
    router_weight,
    weight_up,
    weight_down,
):
    head_count = lax.axis_size("head")
    my_index = lax.axis_index("head")
    tok_local = tokens.shape[1]
    width = tokens.shape[2]
    requests = ssm_state.shape[1]
    heads_local = ssm_state.shape[2]
    head_dim = ssm_state.shape[3]
    state_dim = ssm_state.shape[4]
    gathered = broadcast_gather(tokens[0], head_count)
    inputs = gathered.reshape(requests * STEPS, width)
    normed = norm_rows(inputs.astype(jnp.float32), mixer_gain).astype(jnp.bfloat16)
    bc_fresh = (
        jnp.dot(normed, weight_bc, preferred_element_type=jnp.float32)
        .reshape(requests, STEPS, -1)
        .astype(jnp.bfloat16)
    )
    bc_conv, conv_bc_new = causal_conv(conv_bc_state[0], bc_fresh, conv_bc_kernel, conv_bc_bias)
    bc_conv = bc_conv.astype(jnp.bfloat16)
    bc_all = jnp.moveaxis(broadcast_gather(bc_conv, head_count), 0, 2).reshape(
        requests, STEPS, -1
    )
    proj_xz = column_matmul(normed, weight_xz).reshape(
        requests, STEPS, heads_local, 2 * head_dim
    )
    x_fresh = (
        proj_xz[..., :head_dim].reshape(requests, STEPS, heads_local * head_dim).astype(jnp.bfloat16)
    )
    z_gate = proj_xz[..., head_dim:]
    delta = jax.nn.softplus(
        jnp.dot(normed, weight_delta, preferred_element_type=jnp.float32).reshape(
            requests, STEPS, heads_local
        )
        + delta_bias
    )
    x_conv, conv_x_new = causal_conv(conv_x_state[0], x_fresh, conv_x_kernel, conv_x_bias)
    x_heads = x_conv.reshape(requests, STEPS, heads_local, head_dim)
    decay_rate = jnp.exp(delta * -jnp.exp(decay_log))
    pack = 2 if heads_local % 2 == 0 else 1
    tiles = heads_local // pack
    lanes = pack * head_dim

    decay_rows = jnp.broadcast_to(
        decay_rate[..., None], (requests, STEPS, heads_local, head_dim)
    ).reshape(requests, STEPS, heads_local * head_dim)
    dx_rows = (delta[..., None] * x_heads).reshape(requests, STEPS, heads_local * head_dim)
    tile_group = (my_index * heads_local + jnp.arange(tiles) * pack) // (HEADS // G)
    bc_values = bc_all.astype(jnp.float32).reshape(requests, STEPS, 2, G, state_dim)
    b_rows = jnp.take(bc_values[:, :, 0], tile_group, axis=2).transpose(0, 2, 1, 3)
    c_rows = jnp.take(bc_values[:, :, 1], tile_group, axis=2).transpose(0, 2, 1, 3)
    state_tiles = (
        ssm_state[0]
        .reshape(requests, tiles, pack, head_dim, state_dim)
        .transpose(0, 1, 4, 2, 3)
        .reshape(requests, tiles, state_dim, lanes)
    )
    state_out, read_rows = ssm_scan(state_tiles, decay_rows, dx_rows, b_rows, c_rows)
    ssm_now = (
        state_out.reshape(requests, tiles, state_dim, pack, head_dim)
        .transpose(0, 1, 3, 4, 2)
        .reshape(requests, heads_local, head_dim, state_dim)
    )
    scan_read = read_rows.reshape(requests, STEPS, heads_local, head_dim)
    readings = scan_read + skip_gain[:, None] * x_heads
    gated_out = readings * jax.nn.silu(z_gate)
    group_normed = (
        norm_rows(gated_out, gated_gain.reshape(heads_local, head_dim))
        .astype(jnp.bfloat16)
        .reshape(requests * STEPS, heads_local * head_dim)
    )
    per_expert = head_count // EXPERTS
    mixer_part = column_matmul(group_normed, weight_out)
    mixer_out = lax.all_to_all(
        mixer_part.reshape(head_count, tok_local, width), "head", 0, 0, tiled=True
    ).sum(axis=0)
    residual = (tokens[0].astype(jnp.float32) + mixer_out).astype(jnp.bfloat16)
    ffn_in = norm_rows(residual.astype(jnp.float32), ffn_gain).astype(jnp.bfloat16)
    share = route_share(ffn_in, router_weight, expert_ids[0])
    chosen = expert_ids[0].reshape(-1)
    onehot = (chosen[:, None] == jnp.arange(EXPERTS)[None, :]).astype(jnp.int32)
    earlier = jnp.cumsum(onehot, axis=0) - onehot
    position = jnp.sum(earlier * onehot, axis=1)
    slot_index = chosen * CAP + position
    place = (jnp.arange(EXPERTS * CAP)[:, None] == slot_index[None, :]).astype(jnp.bfloat16)
    routed_rows = jnp.repeat(ffn_in, TOP, axis=0)
    packed = jnp.dot(place, routed_rows, preferred_element_type=jnp.float32).astype(jnp.bfloat16)
    outgoing = jnp.repeat(packed.reshape(EXPERTS, CAP, width), per_expert, axis=0)
    received = lax.all_to_all(outgoing, "head", split_axis=0, concat_axis=0, tiled=True)
    flat_rows = received.reshape(-1, width)
    computed = expert_ffn(flat_rows, weight_up, weight_down).reshape(
        received.shape[0], received.shape[1], width
    )
    returned = lax.all_to_all(
        computed, "head", split_axis=0, concat_axis=0, tiled=True
    ).astype(jnp.float32)
    summed = (
        returned.reshape(EXPERTS, per_expert, CAP, width).sum(axis=1).reshape(EXPERTS * CAP, width)
    )
    per_route = jnp.dot(place.astype(jnp.float32).T, summed, precision=highest).reshape(
        tok_local, TOP, width
    )
    combined = jnp.sum(share[:, :, None] * per_route, axis=1)
    layer_out = (residual.astype(jnp.float32) + combined).astype(jnp.bfloat16)
    return (layer_out[None], ssm_now[None], conv_x_new[None], conv_bc_new[None])


def solution(mesh):
    return jax.shard_map(
        shards,
        mesh=mesh,
        in_specs=(
            P("req", ("groups", "head"), None),
            P("req", "groups", "head", None, None),
            P("req", "groups", None, "head"),
            P("req", "groups", None, "head"),
            P("req", ("groups", "head"), None),
            P(),
            P(None, "head"),
            P(None, "head"),
            P(None, "head"),
            P("head"),
            P("head"),
            P("head"),
            P(None, "head"),
            P("head"),
            P(None, "head"),
            P("head"),
            P("head"),
            P("head", None),
            P(),
            P(),
            P(None, "head"),
            P("head", None),
        ),
        out_specs=(
            P("req", ("groups", "head"), None),
            P("req", "groups", "head", None, None),
            P("req", "groups", None, "head"),
            P("req", "groups", None, "head"),
        ),
        check_vma=False,
    )
```

```python
import jax
import jax.numpy as jnp
from jax import lax
from jax.experimental import pallas as pl
from jax.experimental.pallas import tpu as pltpu
from jax.sharding import PartitionSpec as P

HEADS = 128
G = 8
EXPERTS = 8
TOP = 2
STEPS = 8
CAP = 2


eps = 1e-05
highest = lax.Precision.HIGHEST


def norm_rows(values, gain):
    mean_square = jnp.mean(values * values, axis=-1, keepdims=True)
    return values * lax.rsqrt(mean_square + eps) * gain


def causal_conv(past_rows, fresh_rows, kernel, offset):
    window = jnp.concatenate([past_rows, fresh_rows], axis=1)
    window_wide = window.astype(jnp.float32)
    fresh_count = fresh_rows.shape[1]
    running = offset + kernel[0] * window_wide[:, 0:fresh_count]
    for tap_index in range(1, kernel.shape[0]):
        running = running + kernel[tap_index] * window_wide[:, tap_index : tap_index + fresh_count]
    return (jax.nn.silu(running), window[:, fresh_count:])


def route_share(ffn_in, router_weight, chosen_ids):
    logits = jnp.dot(ffn_in, router_weight, preferred_element_type=jnp.float32)
    match_table = (chosen_ids[:, :, None] == jnp.arange(EXPERTS)[None, None, :]).astype(jnp.float32)
    picked = jnp.einsum("mke,me->mk", match_table, logits, precision=highest)
    first_weight = jax.nn.sigmoid(picked[:, 0] - picked[:, 1])
    return jnp.stack([first_weight, 1.0 - first_weight], axis=1)


def expert_hidden(rows_in, weight_up):
    return jnp.square(
        jnp.maximum(jnp.dot(rows_in, weight_up, preferred_element_type=jnp.float32), 0.0)
    ).astype(jnp.bfloat16)


def column_matmul_kernel(a_ref, w_ref, o_ref):
    o_ref[...] = jnp.dot(a_ref[...], w_ref[...], preferred_element_type=jnp.float32)


def column_matmul(rows, weight):
    m, k = rows.shape
    cols = weight.shape[1]
    block = min(512, cols)
    return pl.pallas_call(
        column_matmul_kernel,
        grid=(cols // block,),
        in_specs=[
            pl.BlockSpec((m, k), lambda j: (0, 0)),
            pl.BlockSpec((k, block), lambda j: (0, j)),
        ],
        out_specs=pl.BlockSpec((m, block), lambda j: (0, j)),
        out_shape=jax.ShapeDtypeStruct((m, cols), jnp.float32),
        cost_estimate=pl.CostEstimate(
            flops=2 * m * k * cols,
            transcendentals=0,
            bytes_accessed=2 * (m * k + k * cols) + 4 * m * cols,
        ),
    )(rows, weight)


def ssm_scan_kernel(s_ref, dec_ref, dx_ref, b_ref, c_ref, s_out_ref, read_ref, bb_ref, cb_ref):
    tiles = s_ref.shape[1]
    state_dim = s_ref.shape[2]
    lanes = s_ref.shape[3]
    steps = dec_ref.shape[1]
    shared = b_ref.shape[1] == 1

    def fill(jb):
        b_cols = b_ref[0, jb].T
        c_cols = c_ref[0, jb].T
        for t in range(steps):
            bb_ref[t] = jnp.broadcast_to(b_cols[:, t : t + 1], (state_dim, lanes))
            cb_ref[t] = jnp.broadcast_to(c_cols[:, t : t + 1], (state_dim, lanes))

    if shared:
        fill(0)
    for j in range(tiles):
        if not shared:
            fill(j)
        cols = slice(j * lanes, (j + 1) * lanes)
        state = s_ref[0, j].astype(jnp.float32)
        dec_all = dec_ref[0, :, cols]
        dx_all = dx_ref[0, :, cols]
        for t in range(steps):
            fresh = dec_all[t : t + 1, :] * state + dx_all[t : t + 1, :] * bb_ref[t]
            read_ref[0, t : t + 1, cols] = jnp.sum(fresh * cb_ref[t], axis=0, keepdims=True)
            state = fresh.astype(jnp.bfloat16).astype(jnp.float32)
        s_out_ref[0, j] = state.astype(jnp.bfloat16)


def ssm_scan(state_tiles, decay_rows, dx_rows, b_rows, c_rows):
    requests, tiles, state_dim, lanes = state_tiles.shape
    steps = decay_rows.shape[1]
    big = pl.BlockSpec((1, tiles, state_dim, lanes), lambda r: (r, 0, 0, 0))
    per_step = pl.BlockSpec((1, steps, tiles * lanes), lambda r: (r, 0, 0))
    rows = pl.BlockSpec((1,) + b_rows.shape[1:], lambda r: (r, 0, 0, 0))
    return pl.pallas_call(
        ssm_scan_kernel,
        grid=(requests,),
        in_specs=[big, per_step, per_step, rows, rows],
        out_specs=[big, per_step],
        out_shape=[
            jax.ShapeDtypeStruct(state_tiles.shape, jnp.bfloat16),
            jax.ShapeDtypeStruct(decay_rows.shape, jnp.float32),
        ],
        scratch_shapes=[
            pltpu.VMEM((steps, state_dim, lanes), jnp.float32),
            pltpu.VMEM((steps, state_dim, lanes), jnp.float32),
        ],
    )(state_tiles, decay_rows, dx_rows, b_rows, c_rows)


def broadcast_gather(block, count):
    copies = jnp.broadcast_to(block[None], (count,) + block.shape)
    return lax.all_to_all(copies, "head", 0, 0, tiled=True)


def shards(
    tokens,
    ssm_state,
    conv_x_state,
    conv_bc_state,
    expert_ids,
    mixer_gain,
    weight_xz,
    weight_bc,
    weight_delta,
    delta_bias,
    decay_log,
    skip_gain,
    conv_x_kernel,
    conv_x_bias,
    conv_bc_kernel,
    conv_bc_bias,
    gated_gain,
    weight_out,
    ffn_gain,
    router_weight,
    weight_up,
    weight_down,
):
    head_count = lax.axis_size("head")
    my_index = lax.axis_index("head")
    tok_local = tokens.shape[1]
    width = tokens.shape[2]
    requests = ssm_state.shape[1]
    heads_local = ssm_state.shape[2]
    head_dim = ssm_state.shape[3]
    state_dim = ssm_state.shape[4]
    gathered = broadcast_gather(tokens[0], head_count)
    inputs = gathered.reshape(requests * STEPS, width)
    normed = norm_rows(inputs.astype(jnp.float32), mixer_gain).astype(jnp.bfloat16)
    bc_fresh = (
        jnp.dot(normed, weight_bc, preferred_element_type=jnp.float32)
        .reshape(requests, STEPS, -1)
        .astype(jnp.bfloat16)
    )
    bc_conv, conv_bc_new = causal_conv(conv_bc_state[0], bc_fresh, conv_bc_kernel, conv_bc_bias)
    bc_conv = bc_conv.astype(jnp.bfloat16)
    bc_all = jnp.moveaxis(broadcast_gather(bc_conv, head_count), 0, 2).reshape(
        requests, STEPS, -1
    )
    proj_xz = column_matmul(normed, weight_xz).reshape(
        requests, STEPS, heads_local, 2 * head_dim
    )
    x_fresh = (
        proj_xz[..., :head_dim].reshape(requests, STEPS, heads_local * head_dim).astype(jnp.bfloat16)
    )
    z_gate = proj_xz[..., head_dim:]
    delta = jax.nn.softplus(
        jnp.dot(normed, weight_delta, preferred_element_type=jnp.float32).reshape(
            requests, STEPS, heads_local
        )
        + delta_bias
    )
    x_conv, conv_x_new = causal_conv(conv_x_state[0], x_fresh, conv_x_kernel, conv_x_bias)
    x_heads = x_conv.reshape(requests, STEPS, heads_local, head_dim)
    decay_rate = jnp.exp(delta * -jnp.exp(decay_log))
    pack = 2 if heads_local % 2 == 0 else 1
    tiles = heads_local // pack
    lanes = pack * head_dim

    decay_rows = jnp.broadcast_to(
        decay_rate[..., None], (requests, STEPS, heads_local, head_dim)
    ).reshape(requests, STEPS, heads_local * head_dim)
    dx_rows = (delta[..., None] * x_heads).reshape(requests, STEPS, heads_local * head_dim)
    shared_group = (HEADS // G) % heads_local == 0
    tile_group = (my_index * heads_local + jnp.arange(1 if shared_group else tiles) * pack) // (
        HEADS // G
    )
    bc_values = bc_all.astype(jnp.float32).reshape(requests, STEPS, 2, G, state_dim)
    b_rows = jnp.take(bc_values[:, :, 0], tile_group, axis=2).transpose(0, 2, 1, 3)
    c_rows = jnp.take(bc_values[:, :, 1], tile_group, axis=2).transpose(0, 2, 1, 3)
    state_tiles = (
        ssm_state[0]
        .reshape(requests, tiles, pack, head_dim, state_dim)
        .transpose(0, 1, 4, 2, 3)
        .reshape(requests, tiles, state_dim, lanes)
    )
    state_out, read_rows = ssm_scan(state_tiles, decay_rows, dx_rows, b_rows, c_rows)
    ssm_now = (
        state_out.reshape(requests, tiles, state_dim, pack, head_dim)
        .transpose(0, 1, 3, 4, 2)
        .reshape(requests, heads_local, head_dim, state_dim)
    )
    scan_read = read_rows.reshape(requests, STEPS, heads_local, head_dim)
    readings = scan_read + skip_gain[:, None] * x_heads
    gated_out = readings * jax.nn.silu(z_gate)
    group_normed = (
        norm_rows(gated_out, gated_gain.reshape(heads_local, head_dim))
        .astype(jnp.bfloat16)
        .reshape(requests * STEPS, heads_local * head_dim)
    )
    per_expert = head_count // EXPERTS
    mixer_part = jnp.dot(group_normed, weight_out, preferred_element_type=jnp.float32)
    mixer_out = lax.all_to_all(
        mixer_part.reshape(head_count, tok_local, width), "head", 0, 0, tiled=True
    ).sum(axis=0)
    residual = (tokens[0].astype(jnp.float32) + mixer_out).astype(jnp.bfloat16)
    ffn_in = norm_rows(residual.astype(jnp.float32), ffn_gain).astype(jnp.bfloat16)
    share = route_share(ffn_in, router_weight, expert_ids[0])
    chosen = expert_ids[0].reshape(-1)
    onehot = (chosen[:, None] == jnp.arange(EXPERTS)[None, :]).astype(jnp.int32)
    earlier = jnp.cumsum(onehot, axis=0) - onehot
    position = jnp.sum(earlier * onehot, axis=1)
    slot_index = chosen * CAP + position
    place = (jnp.arange(EXPERTS * CAP)[:, None] == slot_index[None, :]).astype(jnp.bfloat16)
    routed_rows = jnp.repeat(ffn_in, TOP, axis=0)
    packed = jnp.dot(place, routed_rows, preferred_element_type=jnp.float32).astype(jnp.bfloat16)
    outgoing = jnp.repeat(packed.reshape(EXPERTS, CAP, width), per_expert, axis=0)
    received = lax.all_to_all(outgoing, "head", split_axis=0, concat_axis=0, tiled=True)
    flat_rows = received.reshape(-1, width)
    hidden = expert_hidden(flat_rows, weight_up)
    computed = jnp.dot(hidden, weight_down, preferred_element_type=jnp.float32).reshape(
        received.shape[0], received.shape[1], width
    )
    returned = lax.all_to_all(
        computed.astype(jnp.bfloat16), "head", split_axis=0, concat_axis=0, tiled=True
    ).astype(computed.dtype)
    summed = (
        returned.reshape(EXPERTS, per_expert, CAP, width).sum(axis=1).reshape(EXPERTS * CAP, width)
    )
    per_route = jnp.dot(place.astype(jnp.float32).T, summed, precision=highest).reshape(
        tok_local, TOP, width
    )
    combined = jnp.sum(share[:, :, None] * per_route, axis=1)
    layer_out = (residual.astype(jnp.float32) + combined).astype(jnp.bfloat16)
    return (layer_out[None], ssm_now[None], conv_x_new[None], conv_bc_new[None])


def solution(mesh):
    return jax.shard_map(
        shards,
        mesh=mesh,
        in_specs=(
            P("req", ("groups", "head"), None),
            P("req", "groups", "head", None, None),
            P("req", "groups", None, "head"),
            P("req", "groups", None, "head"),
            P("req", ("groups", "head"), None),
            P(),
            P(None, "head"),
            P(None, "head"),
            P(None, "head"),
            P("head"),
            P("head"),
            P("head"),
            P(None, "head"),
            P("head"),
            P(None, "head"),
            P("head"),
            P("head"),
            P("head", None),
            P(),
            P(),
            P(None, "head"),
            P("head", None),
        ),
        out_specs=(
            P("req", ("groups", "head"), None),
            P("req", "groups", "head", None, None),
            P("req", "groups", None, "head"),
            P("req", "groups", None, "head"),
        ),
        check_vma=False,
    )
```

```python
import functools

import jax
import jax.numpy as jnp
from jax import lax
from jax.experimental import pallas as pl
from jax.experimental.pallas import tpu as pltpu
from jax.sharding import PartitionSpec as P

HEADS = 128
G = 8
EXPERTS = 8
TOP = 2
STEPS = 8
CAP = 2


eps = 1e-05
highest = lax.Precision.HIGHEST


def norm_rows(values, gain):
    mean_square = jnp.mean(values * values, axis=-1, keepdims=True)
    return values * lax.rsqrt(mean_square + eps) * gain


def causal_conv(past_rows, fresh_rows, kernel, offset):
    window = jnp.concatenate([past_rows, fresh_rows], axis=1)
    window_wide = window.astype(jnp.float32)
    fresh_count = fresh_rows.shape[1]
    running = offset + kernel[0] * window_wide[:, 0:fresh_count]
    for tap_index in range(1, kernel.shape[0]):
        running = running + kernel[tap_index] * window_wide[:, tap_index : tap_index + fresh_count]
    return (jax.nn.silu(running), window[:, fresh_count:])


def route_share(ffn_in, router_weight, chosen_ids):
    logits = jnp.dot(ffn_in, router_weight, preferred_element_type=jnp.float32)
    match_table = (chosen_ids[:, :, None] == jnp.arange(EXPERTS)[None, None, :]).astype(jnp.float32)
    picked = jnp.einsum("mke,me->mk", match_table, logits, precision=highest)
    first_weight = jax.nn.sigmoid(picked[:, 0] - picked[:, 1])
    return jnp.stack([first_weight, 1.0 - first_weight], axis=1)


def expert_hidden(rows_in, weight_up):
    return jnp.square(
        jnp.maximum(jnp.dot(rows_in, weight_up, preferred_element_type=jnp.float32), 0.0)
    ).astype(jnp.bfloat16)


def column_matmul_kernel(a_ref, w_ref, o_ref):
    o_ref[...] = jnp.dot(a_ref[...], w_ref[...], preferred_element_type=jnp.float32)


def column_matmul(rows, weight):
    m, k = rows.shape
    cols = weight.shape[1]
    block = min(512, cols)
    return pl.pallas_call(
        column_matmul_kernel,
        grid=(cols // block,),
        in_specs=[
            pl.BlockSpec((m, k), lambda j: (0, 0)),
            pl.BlockSpec((k, block), lambda j: (0, j)),
        ],
        out_specs=pl.BlockSpec((m, block), lambda j: (0, j)),
        out_shape=jax.ShapeDtypeStruct((m, cols), jnp.float32),
        cost_estimate=pl.CostEstimate(
            flops=2 * m * k * cols,
            transcendentals=0,
            bytes_accessed=2 * (m * k + k * cols) + 4 * m * cols,
        ),
    )(rows, weight)


def xz_matmul_kernel(head_dim, a_ref, w_ref, x_ref, z_ref):
    product = jnp.dot(a_ref[...], w_ref[...], preferred_element_type=jnp.float32)
    width = z_ref.shape[1]
    for h in range(width // head_dim):
        x_ref[:, h * head_dim : (h + 1) * head_dim] = product[
            :, 2 * h * head_dim : (2 * h + 1) * head_dim
        ].astype(x_ref.dtype)
        z_ref[:, h * head_dim : (h + 1) * head_dim] = product[
            :, (2 * h + 1) * head_dim : (2 * h + 2) * head_dim
        ]


def xz_matmul(rows, weight, head_dim):
    m, k = rows.shape
    cols = weight.shape[1]
    block = min(512, cols)
    return pl.pallas_call(
        functools.partial(xz_matmul_kernel, head_dim),
        grid=(cols // block,),
        in_specs=[
            pl.BlockSpec((m, k), lambda j: (0, 0)),
            pl.BlockSpec((k, block), lambda j: (0, j)),
        ],
        out_specs=[
            pl.BlockSpec((m, block // 2), lambda j: (0, j)),
            pl.BlockSpec((m, block // 2), lambda j: (0, j)),
        ],
        out_shape=[
            jax.ShapeDtypeStruct((m, cols // 2), jnp.bfloat16),
            jax.ShapeDtypeStruct((m, cols // 2), jnp.float32),
        ],
        cost_estimate=pl.CostEstimate(
            flops=2 * m * k * cols,
            transcendentals=0,
            bytes_accessed=2 * (m * k + k * cols) + 3 * m * cols,
        ),
    )(rows, weight)


def ssm_scan_kernel(s_ref, dec_ref, dx_ref, b_ref, c_ref, s_out_ref, read_ref, bb_ref, cb_ref):
    tiles = s_ref.shape[1]
    state_dim = s_ref.shape[2]
    lanes = s_ref.shape[3]
    steps = dec_ref.shape[1]
    shared = b_ref.shape[1] == 1

    def fill(jb):
        b_cols = b_ref[0, jb].T
        c_cols = c_ref[0, jb].T
        for t in range(steps):
            bb_ref[t] = jnp.broadcast_to(b_cols[:, t : t + 1], (state_dim, lanes))
            cb_ref[t] = jnp.broadcast_to(c_cols[:, t : t + 1], (state_dim, lanes))

    if shared:
        fill(0)
    for j in range(tiles):
        if not shared:
            fill(j)
        cols = slice(j * lanes, (j + 1) * lanes)
        state = s_ref[0, j].astype(jnp.float32)
        dec_all = dec_ref[0, :, cols]
        dx_all = dx_ref[0, :, cols]
        for t in range(steps):
            fresh = dec_all[t : t + 1, :] * state + dx_all[t : t + 1, :] * bb_ref[t]
            read_ref[0, t : t + 1, cols] = jnp.sum(fresh * cb_ref[t], axis=0, keepdims=True)
            state = fresh.astype(jnp.bfloat16).astype(jnp.float32)
        s_out_ref[0, j] = state.astype(jnp.bfloat16)


def ssm_scan(state_tiles, decay_rows, dx_rows, b_rows, c_rows):
    requests, tiles, state_dim, lanes = state_tiles.shape
    steps = decay_rows.shape[1]
    big = pl.BlockSpec((1, tiles, state_dim, lanes), lambda r: (r, 0, 0, 0))
    per_step = pl.BlockSpec((1, steps, tiles * lanes), lambda r: (r, 0, 0))
    rows = pl.BlockSpec((1,) + b_rows.shape[1:], lambda r: (r, 0, 0, 0))
    return pl.pallas_call(
        ssm_scan_kernel,
        grid=(requests,),
        in_specs=[big, per_step, per_step, rows, rows],
        out_specs=[big, per_step],
        out_shape=[
            jax.ShapeDtypeStruct(state_tiles.shape, jnp.bfloat16),
            jax.ShapeDtypeStruct(decay_rows.shape, jnp.float32),
        ],
        scratch_shapes=[
            pltpu.VMEM((steps, state_dim, lanes), jnp.float32),
            pltpu.VMEM((steps, state_dim, lanes), jnp.float32),
        ],
    )(state_tiles, decay_rows, dx_rows, b_rows, c_rows)


def broadcast_gather(block, count):
    copies = jnp.broadcast_to(block[None], (count,) + block.shape)
    return lax.all_to_all(copies, "head", 0, 0, tiled=True)


def shards(
    tokens,
    ssm_state,
    conv_x_state,
    conv_bc_state,
    expert_ids,
    mixer_gain,
    weight_xz,
    weight_bc,
    weight_delta,
    delta_bias,
    decay_log,
    skip_gain,
    conv_x_kernel,
    conv_x_bias,
    conv_bc_kernel,
    conv_bc_bias,
    gated_gain,
    weight_out,
    ffn_gain,
    router_weight,
    weight_up,
    weight_down,
):
    head_count = lax.axis_size("head")
    my_index = lax.axis_index("head")
    tok_local = tokens.shape[1]
    width = tokens.shape[2]
    requests = ssm_state.shape[1]
    heads_local = ssm_state.shape[2]
    head_dim = ssm_state.shape[3]
    state_dim = ssm_state.shape[4]
    gathered = broadcast_gather(tokens[0], head_count)
    inputs = gathered.reshape(requests * STEPS, width)
    normed = norm_rows(inputs.astype(jnp.float32), mixer_gain).astype(jnp.bfloat16)
    bc_fresh = (
        jnp.dot(normed, weight_bc, preferred_element_type=jnp.float32)
        .reshape(requests, STEPS, -1)
        .astype(jnp.bfloat16)
    )
    bc_conv, conv_bc_new = causal_conv(conv_bc_state[0], bc_fresh, conv_bc_kernel, conv_bc_bias)
    bc_conv = bc_conv.astype(jnp.bfloat16)
    bc_all = jnp.moveaxis(broadcast_gather(bc_conv, head_count), 0, 2).reshape(
        requests, STEPS, -1
    )
    x_rows, z_rows = xz_matmul(normed, weight_xz, head_dim)
    x_fresh = x_rows.reshape(requests, STEPS, heads_local * head_dim)
    z_gate = z_rows.reshape(requests, STEPS, heads_local, head_dim)
    delta = jax.nn.softplus(
        jnp.dot(normed, weight_delta, preferred_element_type=jnp.float32).reshape(
            requests, STEPS, heads_local
        )
        + delta_bias
    )
    x_conv, conv_x_new = causal_conv(conv_x_state[0], x_fresh, conv_x_kernel, conv_x_bias)
    x_heads = x_conv.reshape(requests, STEPS, heads_local, head_dim)
    decay_rate = jnp.exp(delta * -jnp.exp(decay_log))
    pack = 2 if heads_local % 2 == 0 else 1
    tiles = heads_local // pack
    lanes = pack * head_dim

    decay_rows = jnp.broadcast_to(
        decay_rate[..., None], (requests, STEPS, heads_local, head_dim)
    ).reshape(requests, STEPS, heads_local * head_dim)
    dx_rows = (delta[..., None] * x_heads).reshape(requests, STEPS, heads_local * head_dim)
    shared_group = (HEADS // G) % heads_local == 0
    tile_group = (my_index * heads_local + jnp.arange(1 if shared_group else tiles) * pack) // (
        HEADS // G
    )
    bc_values = bc_all.astype(jnp.float32).reshape(requests, STEPS, 2, G, state_dim)
    b_rows = jnp.take(bc_values[:, :, 0], tile_group, axis=2).transpose(0, 2, 1, 3)
    c_rows = jnp.take(bc_values[:, :, 1], tile_group, axis=2).transpose(0, 2, 1, 3)
    state_tiles = (
        ssm_state[0]
        .reshape(requests, tiles, pack, head_dim, state_dim)
        .transpose(0, 1, 4, 2, 3)
        .reshape(requests, tiles, state_dim, lanes)
    )
    state_out, read_rows = ssm_scan(state_tiles, decay_rows, dx_rows, b_rows, c_rows)
    ssm_now = (
        state_out.reshape(requests, tiles, state_dim, pack, head_dim)
        .transpose(0, 1, 3, 4, 2)
        .reshape(requests, heads_local, head_dim, state_dim)
    )
    scan_read = read_rows.reshape(requests, STEPS, heads_local, head_dim)
    readings = scan_read + skip_gain[:, None] * x_heads
    gated_out = readings * jax.nn.silu(z_gate)
    group_normed = (
        norm_rows(gated_out, gated_gain.reshape(heads_local, head_dim))
        .astype(jnp.bfloat16)
        .reshape(requests * STEPS, heads_local * head_dim)
    )
    per_expert = head_count // EXPERTS
    mixer_part = jnp.dot(group_normed, weight_out, preferred_element_type=jnp.float32)
    mixer_out = lax.all_to_all(
        mixer_part.reshape(head_count, tok_local, width), "head", 0, 0, tiled=True
    ).sum(axis=0)
    residual = (tokens[0].astype(jnp.float32) + mixer_out).astype(jnp.bfloat16)
    ffn_in = norm_rows(residual.astype(jnp.float32), ffn_gain).astype(jnp.bfloat16)
    share = route_share(ffn_in, router_weight, expert_ids[0])
    chosen = expert_ids[0].reshape(-1)
    onehot = (chosen[:, None] == jnp.arange(EXPERTS)[None, :]).astype(jnp.int32)
    earlier = jnp.cumsum(onehot, axis=0) - onehot
    position = jnp.sum(earlier * onehot, axis=1)
    slot_index = chosen * CAP + position
    place = (jnp.arange(EXPERTS * CAP)[:, None] == slot_index[None, :]).astype(jnp.bfloat16)
    routed_rows = jnp.repeat(ffn_in, TOP, axis=0)
    packed = jnp.dot(place, routed_rows, preferred_element_type=jnp.float32).astype(jnp.bfloat16)
    outgoing = jnp.repeat(packed.reshape(EXPERTS, CAP, width), per_expert, axis=0)
    received = lax.all_to_all(outgoing, "head", split_axis=0, concat_axis=0, tiled=True)
    flat_rows = received.reshape(-1, width)
    hidden = expert_hidden(flat_rows, weight_up)
    computed = jnp.dot(hidden, weight_down, preferred_element_type=jnp.float32).reshape(
        received.shape[0], received.shape[1], width
    )
    returned = lax.all_to_all(
        computed.astype(jnp.bfloat16), "head", split_axis=0, concat_axis=0, tiled=True
    ).astype(computed.dtype)
    summed = (
        returned.reshape(EXPERTS, per_expert, CAP, width).sum(axis=1).reshape(EXPERTS * CAP, width)
    )
    per_route = jnp.dot(place.astype(jnp.float32).T, summed, precision=highest).reshape(
        tok_local, TOP, width
    )
    combined = jnp.sum(share[:, :, None] * per_route, axis=1)
    layer_out = (residual.astype(jnp.float32) + combined).astype(jnp.bfloat16)
    return (layer_out[None], ssm_now[None], conv_x_new[None], conv_bc_new[None])


def solution(mesh):
    return jax.shard_map(
        shards,
        mesh=mesh,
        in_specs=(
            P("req", ("groups", "head"), None),
            P("req", "groups", "head", None, None),
            P("req", "groups", None, "head"),
            P("req", "groups", None, "head"),
            P("req", ("groups", "head"), None),
            P(),
            P(None, "head"),
            P(None, "head"),
            P(None, "head"),
            P("head"),
            P("head"),
            P("head"),
            P(None, "head"),
            P("head"),
            P(None, "head"),
            P("head"),
            P("head"),
            P("head", None),
            P(),
            P(),
            P(None, "head"),
            P("head", None),
        ),
        out_specs=(
            P("req", ("groups", "head"), None),
            P("req", "groups", "head", None, None),
            P("req", "groups", None, "head"),
            P("req", "groups", None, "head"),
        ),
        check_vma=False,
    )
```

```python
import jax
import jax.numpy as jnp
from jax import lax
from jax.experimental import pallas as pl
from jax.experimental.pallas import tpu as pltpu
from jax.sharding import PartitionSpec as P

HEADS = 128
G = 8
EXPERTS = 8
TOP = 2
STEPS = 8
CAP = 2


eps = 1e-05
highest = lax.Precision.HIGHEST


def norm_rows(values, gain):
    mean_square = jnp.mean(values * values, axis=-1, keepdims=True)
    return values * lax.rsqrt(mean_square + eps) * gain


def causal_conv(past_rows, fresh_rows, kernel, offset):
    window = jnp.concatenate([past_rows, fresh_rows], axis=1)
    window_wide = window.astype(jnp.float32)
    fresh_count = fresh_rows.shape[1]
    running = offset + kernel[0] * window_wide[:, 0:fresh_count]
    for tap_index in range(1, kernel.shape[0]):
        running = running + kernel[tap_index] * window_wide[:, tap_index : tap_index + fresh_count]
    return (jax.nn.silu(running), window[:, fresh_count:])


def route_share(ffn_in, router_weight, chosen_ids):
    logits = jnp.dot(ffn_in, router_weight, preferred_element_type=jnp.float32)
    match_table = (chosen_ids[:, :, None] == jnp.arange(EXPERTS)[None, None, :]).astype(jnp.float32)
    picked = jnp.einsum("mke,me->mk", match_table, logits, precision=highest)
    first_weight = jax.nn.sigmoid(picked[:, 0] - picked[:, 1])
    return jnp.stack([first_weight, 1.0 - first_weight], axis=1)


def expert_hidden(rows_in, weight_up):
    return jnp.square(
        jnp.maximum(jnp.dot(rows_in, weight_up, preferred_element_type=jnp.float32), 0.0)
    ).astype(jnp.bfloat16)


def column_matmul_kernel(a_ref, w_ref, o_ref):
    o_ref[...] = jnp.dot(a_ref[...], w_ref[...], preferred_element_type=jnp.float32)


def column_matmul(rows, weight):
    m, k = rows.shape
    cols = weight.shape[1]
    block = min(512, cols)
    return pl.pallas_call(
        column_matmul_kernel,
        grid=(cols // block,),
        in_specs=[
            pl.BlockSpec((m, k), lambda j: (0, 0)),
            pl.BlockSpec((k, block), lambda j: (0, j)),
        ],
        out_specs=pl.BlockSpec((m, block), lambda j: (0, j)),
        out_shape=jax.ShapeDtypeStruct((m, cols), jnp.float32),
        cost_estimate=pl.CostEstimate(
            flops=2 * m * k * cols,
            transcendentals=0,
            bytes_accessed=2 * (m * k + k * cols) + 4 * m * cols,
        ),
    )(rows, weight)


def ssm_scan_kernel(s_ref, dec_ref, dx_ref, b_ref, c_ref, s_out_ref, read_ref, bb_ref, cb_ref):
    tiles = s_ref.shape[1]
    state_dim = s_ref.shape[2]
    lanes = s_ref.shape[3]
    steps = dec_ref.shape[1]
    shared = b_ref.shape[1] == 1

    def fill(jb):
        b_cols = b_ref[0, jb].T
        c_cols = c_ref[0, jb].T
        for t in range(steps):
            bb_ref[t] = jnp.broadcast_to(b_cols[:, t : t + 1], (state_dim, lanes))
            cb_ref[t] = jnp.broadcast_to(c_cols[:, t : t + 1], (state_dim, lanes))

    if shared:
        fill(0)
    for j in range(tiles):
        if not shared:
            fill(j)
        cols = slice(j * lanes, (j + 1) * lanes)
        state = s_ref[0, j].astype(jnp.float32)
        dec_all = dec_ref[0, :, cols]
        dx_all = dx_ref[0, :, cols]
        for t in range(steps):
            fresh = dec_all[t : t + 1, :] * state + dx_all[t : t + 1, :] * bb_ref[t]
            read_ref[0, t : t + 1, cols] = jnp.sum(fresh * cb_ref[t], axis=0, keepdims=True)
            state = fresh.astype(jnp.bfloat16).astype(jnp.float32)
        s_out_ref[0, j] = state.astype(jnp.bfloat16)


def ssm_scan(state_tiles, decay_rows, dx_rows, b_rows, c_rows):
    requests, tiles, state_dim, lanes = state_tiles.shape
    steps = decay_rows.shape[1]
    big = pl.BlockSpec((1, tiles, state_dim, lanes), lambda r: (r, 0, 0, 0))
    per_step = pl.BlockSpec((1, steps, tiles * lanes), lambda r: (r, 0, 0))
    rows = pl.BlockSpec((1,) + b_rows.shape[1:], lambda r: (r, 0, 0, 0))
    return pl.pallas_call(
        ssm_scan_kernel,
        grid=(requests,),
        in_specs=[big, per_step, per_step, rows, rows],
        out_specs=[big, per_step],
        out_shape=[
            jax.ShapeDtypeStruct(state_tiles.shape, jnp.bfloat16),
            jax.ShapeDtypeStruct(decay_rows.shape, jnp.float32),
        ],
        scratch_shapes=[
            pltpu.VMEM((steps, state_dim, lanes), jnp.float32),
            pltpu.VMEM((steps, state_dim, lanes), jnp.float32),
        ],
    )(state_tiles, decay_rows, dx_rows, b_rows, c_rows)


def broadcast_gather(block, count):
    copies = jnp.broadcast_to(block[None], (count,) + block.shape)
    return lax.all_to_all(copies, "head", 0, 0, tiled=True)


def shards(
    tokens,
    ssm_state,
    conv_x_state,
    conv_bc_state,
    expert_ids,
    mixer_gain,
    weight_xz,
    weight_bc,
    weight_delta,
    delta_bias,
    decay_log,
    skip_gain,
    conv_x_kernel,
    conv_x_bias,
    conv_bc_kernel,
    conv_bc_bias,
    gated_gain,
    weight_out,
    ffn_gain,
    router_weight,
    weight_up,
    weight_down,
):
    head_count = lax.axis_size("head")
    my_index = lax.axis_index("head")
    tok_local = tokens.shape[1]
    width = tokens.shape[2]
    requests = ssm_state.shape[1]
    heads_local = ssm_state.shape[2]
    head_dim = ssm_state.shape[3]
    state_dim = ssm_state.shape[4]
    gathered = broadcast_gather(tokens[0], head_count)
    inputs = gathered.reshape(requests * STEPS, width)
    normed = norm_rows(inputs.astype(jnp.float32), mixer_gain).astype(jnp.bfloat16)
    bc_fresh = (
        jnp.dot(normed, weight_bc, preferred_element_type=jnp.float32)
        .reshape(requests, STEPS, -1)
        .astype(jnp.bfloat16)
    )
    bc_conv, conv_bc_new = causal_conv(conv_bc_state[0], bc_fresh, conv_bc_kernel, conv_bc_bias)
    bc_conv = bc_conv.astype(jnp.bfloat16)
    bc_all = jnp.moveaxis(broadcast_gather(bc_conv, head_count), 0, 2).reshape(
        requests, STEPS, -1
    )
    proj_xz = column_matmul(normed, weight_xz).reshape(
        requests, STEPS, heads_local, 2 * head_dim
    )
    x_fresh = (
        proj_xz[..., :head_dim].reshape(requests, STEPS, heads_local * head_dim).astype(jnp.bfloat16)
    )
    z_gate = proj_xz[..., head_dim:]
    delta = jax.nn.softplus(
        jnp.dot(normed, weight_delta, preferred_element_type=jnp.float32).reshape(
            requests, STEPS, heads_local
        )
        + delta_bias
    )
    x_conv, conv_x_new = causal_conv(conv_x_state[0], x_fresh, conv_x_kernel, conv_x_bias)
    x_heads = x_conv.reshape(requests, STEPS, heads_local, head_dim)
    decay_rate = jnp.exp(delta * -jnp.exp(decay_log))
    pack = 2 if heads_local % 2 == 0 else 1
    tiles = heads_local // pack
    lanes = pack * head_dim

    decay_rows = jnp.broadcast_to(
        decay_rate[..., None], (requests, STEPS, heads_local, head_dim)
    ).reshape(requests, STEPS, heads_local * head_dim)
    dx_rows = (delta[..., None] * x_heads).reshape(requests, STEPS, heads_local * head_dim)
    shared_group = (HEADS // G) % heads_local == 0
    tile_group = (my_index * heads_local + jnp.arange(1 if shared_group else tiles) * pack) // (
        HEADS // G
    )
    bc_values = bc_all.astype(jnp.float32).reshape(requests, STEPS, 2, G, state_dim)
    b_rows = jnp.take(bc_values[:, :, 0], tile_group, axis=2).transpose(0, 2, 1, 3)
    c_rows = jnp.take(bc_values[:, :, 1], tile_group, axis=2).transpose(0, 2, 1, 3)
    state_tiles = (
        ssm_state[0]
        .reshape(requests, tiles, pack, head_dim, state_dim)
        .transpose(0, 1, 4, 2, 3)
        .reshape(requests, tiles, state_dim, lanes)
    )
    state_out, read_rows = ssm_scan(state_tiles, decay_rows, dx_rows, b_rows, c_rows)
    ssm_now = (
        state_out.reshape(requests, tiles, state_dim, pack, head_dim)
        .transpose(0, 1, 3, 4, 2)
        .reshape(requests, heads_local, head_dim, state_dim)
    )
    scan_read = read_rows.reshape(requests, STEPS, heads_local, head_dim)
    readings = scan_read + skip_gain[:, None] * x_heads
    gated_out = readings * jax.nn.silu(z_gate)
    group_normed = (
        norm_rows(gated_out, gated_gain.reshape(heads_local, head_dim))
        .astype(jnp.bfloat16)
        .reshape(requests * STEPS, heads_local * head_dim)
    )
    per_expert = head_count // EXPERTS
    mixer_part = jnp.dot(group_normed, weight_out, preferred_element_type=jnp.float32)
    mixer_out = lax.all_to_all(
        mixer_part.reshape(head_count, tok_local, width), "head", 0, 0, tiled=True
    ).sum(axis=0)
    residual = (tokens[0].astype(jnp.float32) + mixer_out).astype(jnp.bfloat16)
    ffn_in = norm_rows(residual.astype(jnp.float32), ffn_gain).astype(jnp.bfloat16)
    share = route_share(ffn_in, router_weight, expert_ids[0])
    chosen = expert_ids[0].reshape(-1)
    onehot = (chosen[:, None] == jnp.arange(EXPERTS)[None, :]).astype(jnp.int32)
    earlier = jnp.cumsum(onehot, axis=0) - onehot
    position = jnp.sum(earlier * onehot, axis=1)
    slot_index = chosen * CAP + position
    place = (jnp.arange(EXPERTS * CAP)[:, None] == slot_index[None, :]).astype(jnp.bfloat16)
    routed_rows = jnp.repeat(ffn_in, TOP, axis=0)
    packed = jnp.dot(place, routed_rows, preferred_element_type=jnp.float32).astype(jnp.bfloat16)
    outgoing = jnp.repeat(packed.reshape(EXPERTS, CAP, width), per_expert, axis=0)
    received = lax.all_to_all(outgoing, "head", split_axis=0, concat_axis=0, tiled=True)
    flat_rows = received.reshape(-1, width)
    hidden = expert_hidden(flat_rows, weight_up)
    computed = jnp.dot(hidden, weight_down, preferred_element_type=jnp.float32).reshape(
        received.shape[0], received.shape[1], width
    )
    returned = lax.all_to_all(computed, "head", split_axis=0, concat_axis=0, tiled=True)
    summed = (
        returned.reshape(EXPERTS, per_expert, CAP, width).sum(axis=1).reshape(EXPERTS * CAP, width)
    )
    per_route = jnp.dot(place.astype(jnp.float32).T, summed, precision=highest).reshape(
        tok_local, TOP, width
    )
    combined = jnp.sum(share[:, :, None] * per_route, axis=1)
    layer_out = (residual.astype(jnp.float32) + combined).astype(jnp.bfloat16)
    return (layer_out[None], ssm_now[None], conv_x_new[None], conv_bc_new[None])


def solution(mesh):
    return jax.shard_map(
        shards,
        mesh=mesh,
        in_specs=(
            P("req", ("groups", "head"), None),
            P("req", "groups", "head", None, None),
            P("req", "groups", None, "head"),
            P("req", "groups", None, "head"),
            P("req", ("groups", "head"), None),
            P(),
            P(None, "head"),
            P(None, "head"),
            P(None, "head"),
            P("head"),
            P("head"),
            P("head"),
            P(None, "head"),
            P("head"),
            P(None, "head"),
            P("head"),
            P("head"),
            P("head", None),
            P(),
            P(),
            P(None, "head"),
            P("head", None),
        ),
        out_specs=(
            P("req", ("groups", "head"), None),
            P("req", "groups", "head", None, None),
            P("req", "groups", None, "head"),
            P("req", "groups", None, "head"),
        ),
        check_vma=False,
    )
```

```python
import jax
import jax.numpy as jnp
from jax import lax
from jax.experimental import pallas as pl
from jax.experimental.pallas import tpu as pltpu
from jax.sharding import PartitionSpec as P

HEADS = 128
G = 8
EXPERTS = 8
TOP = 2
STEPS = 8
CAP = 2


eps = 1e-05
highest = lax.Precision.HIGHEST


def norm_rows(values, gain):
    mean_square = jnp.mean(values * values, axis=-1, keepdims=True)
    return values * lax.rsqrt(mean_square + eps) * gain


def causal_conv(past_rows, fresh_rows, kernel, offset):
    window = jnp.concatenate([past_rows, fresh_rows], axis=1)
    window_wide = window.astype(jnp.float32)
    fresh_count = fresh_rows.shape[1]
    running = offset + kernel[0] * window_wide[:, 0:fresh_count]
    for tap_index in range(1, kernel.shape[0]):
        running = running + kernel[tap_index] * window_wide[:, tap_index : tap_index + fresh_count]
    return (jax.nn.silu(running), window[:, fresh_count:])


def route_share(ffn_in, router_weight, chosen_ids):
    logits = jnp.dot(ffn_in, router_weight, preferred_element_type=jnp.float32)
    match_table = (chosen_ids[:, :, None] == jnp.arange(EXPERTS)[None, None, :]).astype(jnp.float32)
    picked = jnp.einsum("mke,me->mk", match_table, logits, precision=highest)
    first_weight = jax.nn.sigmoid(picked[:, 0] - picked[:, 1])
    return jnp.stack([first_weight, 1.0 - first_weight], axis=1)


def expert_hidden(rows_in, weight_up):
    return jnp.square(
        jnp.maximum(jnp.dot(rows_in, weight_up, preferred_element_type=jnp.float32), 0.0)
    ).astype(jnp.bfloat16)


def column_matmul_kernel(a_ref, w_ref, o_ref):
    o_ref[...] = jnp.dot(a_ref[...], w_ref[...], preferred_element_type=jnp.float32)


def column_matmul(rows, weight):
    m, k = rows.shape
    cols = weight.shape[1]
    block = min(512, cols)
    return pl.pallas_call(
        column_matmul_kernel,
        grid=(cols // block,),
        in_specs=[
            pl.BlockSpec((m, k), lambda j: (0, 0)),
            pl.BlockSpec((k, block), lambda j: (0, j)),
        ],
        out_specs=pl.BlockSpec((m, block), lambda j: (0, j)),
        out_shape=jax.ShapeDtypeStruct((m, cols), jnp.float32),
        cost_estimate=pl.CostEstimate(
            flops=2 * m * k * cols,
            transcendentals=0,
            bytes_accessed=2 * (m * k + k * cols) + 4 * m * cols,
        ),
    )(rows, weight)


def ssm_scan_kernel(s_ref, dec_ref, dx_ref, b_ref, c_ref, s_out_ref, read_ref, bb_ref, cb_ref):
    tiles = s_ref.shape[1]
    state_dim = s_ref.shape[2]
    lanes = s_ref.shape[3]
    steps = dec_ref.shape[1]
    shared = b_ref.shape[1] == 1

    def fill(jb):
        b_cols = b_ref[0, jb].astype(jnp.float32).T
        c_cols = c_ref[0, jb].astype(jnp.float32).T
        for t in range(steps):
            bb_ref[t] = jnp.broadcast_to(b_cols[:, t : t + 1], (state_dim, lanes))
            cb_ref[t] = jnp.broadcast_to(c_cols[:, t : t + 1], (state_dim, lanes))

    if shared:
        fill(0)
    for j in range(tiles):
        if not shared:
            fill(j)
        cols = slice(j * lanes, (j + 1) * lanes)
        state = s_ref[0, j].astype(jnp.float32)
        dec_all = dec_ref[0, :, cols]
        dx_all = dx_ref[0, :, cols]
        for t in range(steps):
            fresh = dec_all[t : t + 1, :] * state + dx_all[t : t + 1, :] * bb_ref[t]
            read_ref[0, t : t + 1, cols] = jnp.sum(fresh * cb_ref[t], axis=0, keepdims=True)
            state = fresh.astype(jnp.bfloat16).astype(jnp.float32)
        s_out_ref[0, j] = state.astype(jnp.bfloat16)


def ssm_scan(state_tiles, decay_rows, dx_rows, b_rows, c_rows):
    requests, tiles, state_dim, lanes = state_tiles.shape
    steps = decay_rows.shape[1]
    big = pl.BlockSpec((1, tiles, state_dim, lanes), lambda r: (r, 0, 0, 0))
    per_step = pl.BlockSpec((1, steps, tiles * lanes), lambda r: (r, 0, 0))
    rows = pl.BlockSpec((1,) + b_rows.shape[1:], lambda r: (r, 0, 0, 0))
    return pl.pallas_call(
        ssm_scan_kernel,
        grid=(requests,),
        in_specs=[big, per_step, per_step, rows, rows],
        out_specs=[big, per_step],
        out_shape=[
            jax.ShapeDtypeStruct(state_tiles.shape, jnp.bfloat16),
            jax.ShapeDtypeStruct(decay_rows.shape, jnp.float32),
        ],
        scratch_shapes=[
            pltpu.VMEM((steps, state_dim, lanes), jnp.float32),
            pltpu.VMEM((steps, state_dim, lanes), jnp.float32),
        ],
    )(state_tiles, decay_rows, dx_rows, b_rows, c_rows)


def ssm_scan_direct_kernel(group_ref, *refs):
    ssm_scan_kernel(*refs)


def ssm_scan_direct(state_tiles, decay_rows, dx_rows, bc_blocks, group, group_count):
    requests, tiles, state_dim, lanes = state_tiles.shape
    steps = decay_rows.shape[1]
    cols_local = bc_blocks.shape[3]
    c_start = group_count * state_dim

    def b_map(r, g):
        first = g[0] * state_dim
        return (first // cols_local, r, 0, (first % cols_local) // state_dim)

    def c_map(r, g):
        first = c_start + g[0] * state_dim
        return (first // cols_local, r, 0, (first % cols_local) // state_dim)

    big = pl.BlockSpec((1, tiles, state_dim, lanes), lambda r, g: (r, 0, 0, 0))
    per_step = pl.BlockSpec((1, steps, tiles * lanes), lambda r, g: (r, 0, 0))
    return pl.pallas_call(
        ssm_scan_direct_kernel,
        grid_spec=pltpu.PrefetchScalarGridSpec(
            num_scalar_prefetch=1,
            grid=(requests,),
            in_specs=[
                big,
                per_step,
                per_step,
                pl.BlockSpec((1, 1, steps, state_dim), b_map),
                pl.BlockSpec((1, 1, steps, state_dim), c_map),
            ],
            out_specs=[big, per_step],
            scratch_shapes=[
                pltpu.VMEM((steps, state_dim, lanes), jnp.float32),
                pltpu.VMEM((steps, state_dim, lanes), jnp.float32),
            ],
        ),
        out_shape=[
            jax.ShapeDtypeStruct(state_tiles.shape, jnp.bfloat16),
            jax.ShapeDtypeStruct(decay_rows.shape, jnp.float32),
        ],
    )(group, state_tiles, decay_rows, dx_rows, bc_blocks, bc_blocks)


def broadcast_gather(block, count):
    copies = jnp.broadcast_to(block[None], (count,) + block.shape)
    return lax.all_to_all(copies, "head", 0, 0, tiled=True)


def shards(
    tokens,
    ssm_state,
    conv_x_state,
    conv_bc_state,
    expert_ids,
    mixer_gain,
    weight_xz,
    weight_bc,
    weight_delta,
    delta_bias,
    decay_log,
    skip_gain,
    conv_x_kernel,
    conv_x_bias,
    conv_bc_kernel,
    conv_bc_bias,
    gated_gain,
    weight_out,
    ffn_gain,
    router_weight,
    weight_up,
    weight_down,
):
    head_count = lax.axis_size("head")
    my_index = lax.axis_index("head")
    tok_local = tokens.shape[1]
    width = tokens.shape[2]
    requests = ssm_state.shape[1]
    heads_local = ssm_state.shape[2]
    head_dim = ssm_state.shape[3]
    state_dim = ssm_state.shape[4]
    gathered = broadcast_gather(tokens[0], head_count)
    inputs = gathered.reshape(requests * STEPS, width)
    normed = norm_rows(inputs.astype(jnp.float32), mixer_gain).astype(jnp.bfloat16)
    bc_fresh = (
        jnp.dot(normed, weight_bc, preferred_element_type=jnp.float32)
        .reshape(requests, STEPS, -1)
        .astype(jnp.bfloat16)
    )
    bc_conv, conv_bc_new = causal_conv(conv_bc_state[0], bc_fresh, conv_bc_kernel, conv_bc_bias)
    bc_conv = bc_conv.astype(jnp.bfloat16)
    bc_blocks = broadcast_gather(bc_conv, head_count)
    proj_xz = column_matmul(normed, weight_xz).reshape(
        requests, STEPS, heads_local, 2 * head_dim
    )
    x_fresh = (
        proj_xz[..., :head_dim].reshape(requests, STEPS, heads_local * head_dim).astype(jnp.bfloat16)
    )
    z_gate = proj_xz[..., head_dim:]
    delta = jax.nn.softplus(
        jnp.dot(normed, weight_delta, preferred_element_type=jnp.float32).reshape(
            requests, STEPS, heads_local
        )
        + delta_bias
    )
    x_conv, conv_x_new = causal_conv(conv_x_state[0], x_fresh, conv_x_kernel, conv_x_bias)
    x_heads = x_conv.reshape(requests, STEPS, heads_local, head_dim)
    decay_rate = jnp.exp(delta * -jnp.exp(decay_log))
    pack = 2 if heads_local % 2 == 0 else 1
    tiles = heads_local // pack
    lanes = pack * head_dim

    decay_rows = jnp.broadcast_to(
        decay_rate[..., None], (requests, STEPS, heads_local, head_dim)
    ).reshape(requests, STEPS, heads_local * head_dim)
    dx_rows = (delta[..., None] * x_heads).reshape(requests, STEPS, heads_local * head_dim)
    shared_group = (HEADS // G) % heads_local == 0
    tile_group = (my_index * heads_local + jnp.arange(1 if shared_group else tiles) * pack) // (
        HEADS // G
    )
    state_tiles = (
        ssm_state[0]
        .reshape(requests, tiles, pack, head_dim, state_dim)
        .transpose(0, 1, 4, 2, 3)
        .reshape(requests, tiles, state_dim, lanes)
    )
    if shared_group and bc_blocks.shape[3] % state_dim == 0:
        state_out, read_rows = ssm_scan_direct(
            state_tiles, decay_rows, dx_rows, bc_blocks, tile_group.astype(jnp.int32), G
        )
    else:
        bc_all = jnp.moveaxis(bc_blocks, 0, 2).reshape(requests, STEPS, -1)
        bc_values = bc_all.astype(jnp.float32).reshape(requests, STEPS, 2, G, state_dim)
        b_rows = jnp.take(bc_values[:, :, 0], tile_group, axis=2).transpose(0, 2, 1, 3)
        c_rows = jnp.take(bc_values[:, :, 1], tile_group, axis=2).transpose(0, 2, 1, 3)
        state_out, read_rows = ssm_scan(state_tiles, decay_rows, dx_rows, b_rows, c_rows)
    ssm_now = (
        state_out.reshape(requests, tiles, state_dim, pack, head_dim)
        .transpose(0, 1, 3, 4, 2)
        .reshape(requests, heads_local, head_dim, state_dim)
    )
    scan_read = read_rows.reshape(requests, STEPS, heads_local, head_dim)
    readings = scan_read + skip_gain[:, None] * x_heads
    gated_out = readings * jax.nn.silu(z_gate)
    group_normed = (
        norm_rows(gated_out, gated_gain.reshape(heads_local, head_dim))
        .astype(jnp.bfloat16)
        .reshape(requests * STEPS, heads_local * head_dim)
    )
    per_expert = head_count // EXPERTS
    mixer_part = jnp.dot(group_normed, weight_out, preferred_element_type=jnp.float32)
    mixer_out = lax.all_to_all(
        mixer_part.reshape(head_count, tok_local, width), "head", 0, 0, tiled=True
    ).sum(axis=0)
    residual = (tokens[0].astype(jnp.float32) + mixer_out).astype(jnp.bfloat16)
    ffn_in = norm_rows(residual.astype(jnp.float32), ffn_gain).astype(jnp.bfloat16)
    share = route_share(ffn_in, router_weight, expert_ids[0])
    chosen = expert_ids[0].reshape(-1)
    onehot = (chosen[:, None] == jnp.arange(EXPERTS)[None, :]).astype(jnp.int32)
    earlier = jnp.cumsum(onehot, axis=0) - onehot
    position = jnp.sum(earlier * onehot, axis=1)
    slot_index = chosen * CAP + position
    place = (jnp.arange(EXPERTS * CAP)[:, None] == slot_index[None, :]).astype(jnp.bfloat16)
    routed_rows = jnp.repeat(ffn_in, TOP, axis=0)
    packed = jnp.dot(place, routed_rows, preferred_element_type=jnp.float32).astype(jnp.bfloat16)
    outgoing = jnp.repeat(packed.reshape(EXPERTS, CAP, width), per_expert, axis=0)
    received = lax.all_to_all(outgoing, "head", split_axis=0, concat_axis=0, tiled=True)
    flat_rows = received.reshape(-1, width)
    hidden = expert_hidden(flat_rows, weight_up)
    computed = jnp.dot(hidden, weight_down, preferred_element_type=jnp.float32).reshape(
        received.shape[0], received.shape[1], width
    )
    returned = lax.all_to_all(
        computed.astype(jnp.bfloat16), "head", split_axis=0, concat_axis=0, tiled=True
    ).astype(computed.dtype)
    summed = (
        returned.reshape(EXPERTS, per_expert, CAP, width).sum(axis=1).reshape(EXPERTS * CAP, width)
    )
    per_route = jnp.dot(place.astype(jnp.float32).T, summed, precision=highest).reshape(
        tok_local, TOP, width
    )
    combined = jnp.sum(share[:, :, None] * per_route, axis=1)
    layer_out = (residual.astype(jnp.float32) + combined).astype(jnp.bfloat16)
    return (layer_out[None], ssm_now[None], conv_x_new[None], conv_bc_new[None])


def solution(mesh):
    return jax.shard_map(
        shards,
        mesh=mesh,
        in_specs=(
            P("req", ("groups", "head"), None),
            P("req", "groups", "head", None, None),
            P("req", "groups", None, "head"),
            P("req", "groups", None, "head"),
            P("req", ("groups", "head"), None),
            P(),
            P(None, "head"),
            P(None, "head"),
            P(None, "head"),
            P("head"),
            P("head"),
            P("head"),
            P(None, "head"),
            P("head"),
            P(None, "head"),
            P("head"),
            P("head"),
            P("head", None),
            P(),
            P(),
            P(None, "head"),
            P("head", None),
        ),
        out_specs=(
            P("req", ("groups", "head"), None),
            P("req", "groups", "head", None, None),
            P("req", "groups", None, "head"),
            P("req", "groups", None, "head"),
        ),
        check_vma=False,
    )
```

```python
import jax
import jax.numpy as jnp
from jax import lax
from jax.experimental import pallas as pl
from jax.experimental.pallas import tpu as pltpu
from jax.sharding import PartitionSpec as P

HEADS = 128
G = 8
EXPERTS = 8
TOP = 2
STEPS = 8
CAP = 2


eps = 1e-05
highest = lax.Precision.HIGHEST


def norm_rows(values, gain):
    mean_square = jnp.mean(values * values, axis=-1, keepdims=True)
    return values * lax.rsqrt(mean_square + eps) * gain


def causal_conv(past_rows, fresh_rows, kernel, offset):
    window = jnp.concatenate([past_rows, fresh_rows], axis=1)
    window_wide = window.astype(jnp.float32)
    fresh_count = fresh_rows.shape[1]
    running = offset + kernel[0] * window_wide[:, 0:fresh_count]
    for tap_index in range(1, kernel.shape[0]):
        running = running + kernel[tap_index] * window_wide[:, tap_index : tap_index + fresh_count]
    return (jax.nn.silu(running), window[:, fresh_count:])


def route_share(ffn_in, router_weight, chosen_ids):
    logits = jnp.dot(ffn_in, router_weight, preferred_element_type=jnp.float32)
    match_table = (chosen_ids[:, :, None] == jnp.arange(EXPERTS)[None, None, :]).astype(jnp.float32)
    picked = jnp.einsum("mke,me->mk", match_table, logits, precision=highest)
    first_weight = jax.nn.sigmoid(picked[:, 0] - picked[:, 1])
    return jnp.stack([first_weight, 1.0 - first_weight], axis=1)


def expert_hidden(rows_in, weight_up):
    return jnp.square(
        jnp.maximum(jnp.dot(rows_in, weight_up, preferred_element_type=jnp.float32), 0.0)
    ).astype(jnp.bfloat16)


def column_matmul_kernel(a_ref, w_ref, o_ref):
    o_ref[...] = jnp.dot(a_ref[...], w_ref[...], preferred_element_type=jnp.float32)


def column_matmul(rows, weight):
    m, k = rows.shape
    cols = weight.shape[1]
    block = min(1024, cols)
    return pl.pallas_call(
        column_matmul_kernel,
        grid=(cols // block,),
        in_specs=[
            pl.BlockSpec((m, k), lambda j: (0, 0)),
            pl.BlockSpec((k, block), lambda j: (0, j)),
        ],
        out_specs=pl.BlockSpec((m, block), lambda j: (0, j)),
        out_shape=jax.ShapeDtypeStruct((m, cols), jnp.float32),
        cost_estimate=pl.CostEstimate(
            flops=2 * m * k * cols,
            transcendentals=0,
            bytes_accessed=2 * (m * k + k * cols) + 4 * m * cols,
        ),
    )(rows, weight)


def ssm_scan_kernel(s_ref, dec_ref, dx_ref, b_ref, c_ref, s_out_ref, read_ref, bb_ref, cb_ref):
    tiles = s_ref.shape[1]
    state_dim = s_ref.shape[2]
    lanes = s_ref.shape[3]
    steps = dec_ref.shape[1]
    shared = b_ref.shape[1] == 1

    def fill(jb):
        b_cols = b_ref[0, jb].astype(jnp.float32).T
        c_cols = c_ref[0, jb].astype(jnp.float32).T
        for t in range(steps):
            bb_ref[t] = jnp.broadcast_to(b_cols[:, t : t + 1], (state_dim, lanes))
            cb_ref[t] = jnp.broadcast_to(c_cols[:, t : t + 1], (state_dim, lanes))

    if shared:
        fill(0)
    for j in range(tiles):
        if not shared:
            fill(j)
        cols = slice(j * lanes, (j + 1) * lanes)
        state = s_ref[0, j].astype(jnp.float32)
        dec_all = dec_ref[0, :, cols]
        dx_all = dx_ref[0, :, cols]
        for t in range(steps):
            fresh = dec_all[t : t + 1, :] * state + dx_all[t : t + 1, :] * bb_ref[t]
            read_ref[0, t : t + 1, cols] = jnp.sum(fresh * cb_ref[t], axis=0, keepdims=True)
            state = fresh.astype(jnp.bfloat16).astype(jnp.float32)
        s_out_ref[0, j] = state.astype(jnp.bfloat16)


def ssm_scan(state_tiles, decay_rows, dx_rows, b_rows, c_rows):
    requests, tiles, state_dim, lanes = state_tiles.shape
    steps = decay_rows.shape[1]
    big = pl.BlockSpec((1, tiles, state_dim, lanes), lambda r: (r, 0, 0, 0))
    per_step = pl.BlockSpec((1, steps, tiles * lanes), lambda r: (r, 0, 0))
    rows = pl.BlockSpec((1,) + b_rows.shape[1:], lambda r: (r, 0, 0, 0))
    return pl.pallas_call(
        ssm_scan_kernel,
        grid=(requests,),
        in_specs=[big, per_step, per_step, rows, rows],
        out_specs=[big, per_step],
        out_shape=[
            jax.ShapeDtypeStruct(state_tiles.shape, jnp.bfloat16),
            jax.ShapeDtypeStruct(decay_rows.shape, jnp.float32),
        ],
        scratch_shapes=[
            pltpu.VMEM((steps, state_dim, lanes), jnp.float32),
            pltpu.VMEM((steps, state_dim, lanes), jnp.float32),
        ],
    )(state_tiles, decay_rows, dx_rows, b_rows, c_rows)


def ssm_scan_direct_kernel(group_ref, *refs):
    ssm_scan_kernel(*refs)


def ssm_scan_direct(state_tiles, decay_rows, dx_rows, bc_blocks, group, group_count):
    requests, tiles, state_dim, lanes = state_tiles.shape
    steps = decay_rows.shape[1]
    cols_local = bc_blocks.shape[3]
    c_start = group_count * state_dim

    def b_map(r, g):
        first = g[0] * state_dim
        return (first // cols_local, r, 0, (first % cols_local) // state_dim)

    def c_map(r, g):
        first = c_start + g[0] * state_dim
        return (first // cols_local, r, 0, (first % cols_local) // state_dim)

    big = pl.BlockSpec((1, tiles, state_dim, lanes), lambda r, g: (r, 0, 0, 0))
    per_step = pl.BlockSpec((1, steps, tiles * lanes), lambda r, g: (r, 0, 0))
    return pl.pallas_call(
        ssm_scan_direct_kernel,
        grid_spec=pltpu.PrefetchScalarGridSpec(
            num_scalar_prefetch=1,
            grid=(requests,),
            in_specs=[
                big,
                per_step,
                per_step,
                pl.BlockSpec((1, 1, steps, state_dim), b_map),
                pl.BlockSpec((1, 1, steps, state_dim), c_map),
            ],
            out_specs=[big, per_step],
            scratch_shapes=[
                pltpu.VMEM((steps, state_dim, lanes), jnp.float32),
                pltpu.VMEM((steps, state_dim, lanes), jnp.float32),
            ],
        ),
        out_shape=[
            jax.ShapeDtypeStruct(state_tiles.shape, jnp.bfloat16),
            jax.ShapeDtypeStruct(decay_rows.shape, jnp.float32),
        ],
    )(group, state_tiles, decay_rows, dx_rows, bc_blocks, bc_blocks)


def broadcast_gather(block, count):
    copies = jnp.broadcast_to(block[None], (count,) + block.shape)
    return lax.all_to_all(copies, "head", 0, 0, tiled=True)


def shards(
    tokens,
    ssm_state,
    conv_x_state,
    conv_bc_state,
    expert_ids,
    mixer_gain,
    weight_xz,
    weight_bc,
    weight_delta,
    delta_bias,
    decay_log,
    skip_gain,
    conv_x_kernel,
    conv_x_bias,
    conv_bc_kernel,
    conv_bc_bias,
    gated_gain,
    weight_out,
    ffn_gain,
    router_weight,
    weight_up,
    weight_down,
):
    head_count = lax.axis_size("head")
    my_index = lax.axis_index("head")
    tok_local = tokens.shape[1]
    width = tokens.shape[2]
    requests = ssm_state.shape[1]
    heads_local = ssm_state.shape[2]
    head_dim = ssm_state.shape[3]
    state_dim = ssm_state.shape[4]
    gathered = broadcast_gather(tokens[0], head_count)
    inputs = gathered.reshape(requests * STEPS, width)
    normed = norm_rows(inputs.astype(jnp.float32), mixer_gain).astype(jnp.bfloat16)
    bc_fresh = (
        jnp.dot(normed, weight_bc, preferred_element_type=jnp.float32)
        .reshape(requests, STEPS, -1)
        .astype(jnp.bfloat16)
    )
    bc_conv, conv_bc_new = causal_conv(conv_bc_state[0], bc_fresh, conv_bc_kernel, conv_bc_bias)
    bc_conv = bc_conv.astype(jnp.bfloat16)
    bc_blocks = broadcast_gather(bc_conv, head_count)
    proj_xz = column_matmul(normed, weight_xz).reshape(
        requests, STEPS, heads_local, 2 * head_dim
    )
    x_fresh = (
        proj_xz[..., :head_dim].reshape(requests, STEPS, heads_local * head_dim).astype(jnp.bfloat16)
    )
    z_gate = proj_xz[..., head_dim:]
    delta = jax.nn.softplus(
        jnp.dot(normed, weight_delta, preferred_element_type=jnp.float32).reshape(
            requests, STEPS, heads_local
        )
        + delta_bias
    )
    x_conv, conv_x_new = causal_conv(conv_x_state[0], x_fresh, conv_x_kernel, conv_x_bias)
    x_heads = x_conv.reshape(requests, STEPS, heads_local, head_dim)
    decay_rate = jnp.exp(delta * -jnp.exp(decay_log))
    pack = 2 if heads_local % 2 == 0 else 1
    tiles = heads_local // pack
    lanes = pack * head_dim

    decay_rows = jnp.broadcast_to(
        decay_rate[..., None], (requests, STEPS, heads_local, head_dim)
    ).reshape(requests, STEPS, heads_local * head_dim)
    dx_rows = (delta[..., None] * x_heads).reshape(requests, STEPS, heads_local * head_dim)
    shared_group = (HEADS // G) % heads_local == 0
    tile_group = (my_index * heads_local + jnp.arange(1 if shared_group else tiles) * pack) // (
        HEADS // G
    )
    state_tiles = (
        ssm_state[0]
        .reshape(requests, tiles, pack, head_dim, state_dim)
        .transpose(0, 1, 4, 2, 3)
        .reshape(requests, tiles, state_dim, lanes)
    )
    if shared_group and bc_blocks.shape[3] % state_dim == 0:
        state_out, read_rows = ssm_scan_direct(
            state_tiles, decay_rows, dx_rows, bc_blocks, tile_group.astype(jnp.int32), G
        )
    else:
        bc_all = jnp.moveaxis(bc_blocks, 0, 2).reshape(requests, STEPS, -1)
        bc_values = bc_all.astype(jnp.float32).reshape(requests, STEPS, 2, G, state_dim)
        b_rows = jnp.take(bc_values[:, :, 0], tile_group, axis=2).transpose(0, 2, 1, 3)
        c_rows = jnp.take(bc_values[:, :, 1], tile_group, axis=2).transpose(0, 2, 1, 3)
        state_out, read_rows = ssm_scan(state_tiles, decay_rows, dx_rows, b_rows, c_rows)
    ssm_now = (
        state_out.reshape(requests, tiles, state_dim, pack, head_dim)
        .transpose(0, 1, 3, 4, 2)
        .reshape(requests, heads_local, head_dim, state_dim)
    )
    scan_read = read_rows.reshape(requests, STEPS, heads_local, head_dim)
    readings = scan_read + skip_gain[:, None] * x_heads
    gated_out = readings * jax.nn.silu(z_gate)
    group_normed = (
        norm_rows(gated_out, gated_gain.reshape(heads_local, head_dim))
        .astype(jnp.bfloat16)
        .reshape(requests * STEPS, heads_local * head_dim)
    )
    per_expert = head_count // EXPERTS
    mixer_part = jnp.dot(group_normed, weight_out, preferred_element_type=jnp.float32)
    mixer_out = lax.all_to_all(
        mixer_part.reshape(head_count, tok_local, width), "head", 0, 0, tiled=True
    ).sum(axis=0)
    residual = (tokens[0].astype(jnp.float32) + mixer_out).astype(jnp.bfloat16)
    ffn_in = norm_rows(residual.astype(jnp.float32), ffn_gain).astype(jnp.bfloat16)
    share = route_share(ffn_in, router_weight, expert_ids[0])
    chosen = expert_ids[0].reshape(-1)
    onehot = (chosen[:, None] == jnp.arange(EXPERTS)[None, :]).astype(jnp.int32)
    earlier = jnp.cumsum(onehot, axis=0) - onehot
    position = jnp.sum(earlier * onehot, axis=1)
    slot_index = chosen * CAP + position
    place = (jnp.arange(EXPERTS * CAP)[:, None] == slot_index[None, :]).astype(jnp.bfloat16)
    routed_rows = jnp.repeat(ffn_in, TOP, axis=0)
    packed = jnp.dot(place, routed_rows, preferred_element_type=jnp.float32).astype(jnp.bfloat16)
    outgoing = jnp.repeat(packed.reshape(EXPERTS, CAP, width), per_expert, axis=0)
    received = lax.all_to_all(outgoing, "head", split_axis=0, concat_axis=0, tiled=True)
    flat_rows = received.reshape(-1, width)
    hidden = expert_hidden(flat_rows, weight_up)
    computed = jnp.dot(hidden, weight_down, preferred_element_type=jnp.float32).reshape(
        received.shape[0], received.shape[1], width
    )
    returned = lax.all_to_all(
        computed.astype(jnp.bfloat16), "head", split_axis=0, concat_axis=0, tiled=True
    ).astype(computed.dtype)
    summed = (
        returned.reshape(EXPERTS, per_expert, CAP, width).sum(axis=1).reshape(EXPERTS * CAP, width)
    )
    per_route = jnp.dot(place.astype(jnp.float32).T, summed, precision=highest).reshape(
        tok_local, TOP, width
    )
    combined = jnp.sum(share[:, :, None] * per_route, axis=1)
    layer_out = (residual.astype(jnp.float32) + combined).astype(jnp.bfloat16)
    return (layer_out[None], ssm_now[None], conv_x_new[None], conv_bc_new[None])


def solution(mesh):
    return jax.shard_map(
        shards,
        mesh=mesh,
        in_specs=(
            P("req", ("groups", "head"), None),
            P("req", "groups", "head", None, None),
            P("req", "groups", None, "head"),
            P("req", "groups", None, "head"),
            P("req", ("groups", "head"), None),
            P(),
            P(None, "head"),
            P(None, "head"),
            P(None, "head"),
            P("head"),
            P("head"),
            P("head"),
            P(None, "head"),
            P("head"),
            P(None, "head"),
            P("head"),
            P("head"),
            P("head", None),
            P(),
            P(),
            P(None, "head"),
            P("head", None),
        ),
        out_specs=(
            P("req", ("groups", "head"), None),
            P("req", "groups", "head", None, None),
            P("req", "groups", None, "head"),
            P("req", "groups", None, "head"),
        ),
        check_vma=False,
    )
```

```python
import functools

import jax
import jax.numpy as jnp
from jax import lax
from jax.experimental import pallas as pl
from jax.experimental.pallas import tpu as pltpu
from jax.sharding import PartitionSpec as P

HEADS = 128
G = 8
EXPERTS = 8
TOP = 2
STEPS = 8
CAP = 2


eps = 1e-05
highest = lax.Precision.HIGHEST


def norm_rows(values, gain):
    mean_square = jnp.mean(values * values, axis=-1, keepdims=True)
    return values * lax.rsqrt(mean_square + eps) * gain


def causal_conv(past_rows, fresh_rows, kernel, offset):
    window = jnp.concatenate([past_rows, fresh_rows], axis=1)
    window_wide = window.astype(jnp.float32)
    fresh_count = fresh_rows.shape[1]
    running = offset + kernel[0] * window_wide[:, 0:fresh_count]
    for tap_index in range(1, kernel.shape[0]):
        running = running + kernel[tap_index] * window_wide[:, tap_index : tap_index + fresh_count]
    return (jax.nn.silu(running), window[:, fresh_count:])


def route_share(ffn_in, router_weight, chosen_ids):
    logits = jnp.dot(ffn_in, router_weight, preferred_element_type=jnp.float32)
    match_table = (chosen_ids[:, :, None] == jnp.arange(EXPERTS)[None, None, :]).astype(jnp.float32)
    picked = jnp.einsum("mke,me->mk", match_table, logits, precision=highest)
    first_weight = jax.nn.sigmoid(picked[:, 0] - picked[:, 1])
    return jnp.stack([first_weight, 1.0 - first_weight], axis=1)


def expert_hidden(rows_in, weight_up):
    return jnp.square(
        jnp.maximum(jnp.dot(rows_in, weight_up, preferred_element_type=jnp.float32), 0.0)
    ).astype(jnp.bfloat16)


def column_matmul_kernel(a_ref, w_ref, o_ref):
    o_ref[...] = jnp.dot(a_ref[...], w_ref[...], preferred_element_type=jnp.float32)


def column_matmul(rows, weight):
    m, k = rows.shape
    cols = weight.shape[1]
    block = min(1024, cols)
    return pl.pallas_call(
        column_matmul_kernel,
        grid=(cols // block,),
        in_specs=[
            pl.BlockSpec((m, k), lambda j: (0, 0)),
            pl.BlockSpec((k, block), lambda j: (0, j)),
        ],
        out_specs=pl.BlockSpec((m, block), lambda j: (0, j)),
        out_shape=jax.ShapeDtypeStruct((m, cols), jnp.float32),
        cost_estimate=pl.CostEstimate(
            flops=2 * m * k * cols,
            transcendentals=0,
            bytes_accessed=2 * (m * k + k * cols) + 4 * m * cols,
        ),
    )(rows, weight)


def ssm_scan_kernel(s_ref, dec_ref, dx_ref, b_ref, c_ref, s_out_ref, read_ref, bb_ref, cb_ref):
    tiles = s_ref.shape[1]
    state_dim = s_ref.shape[2]
    lanes = s_ref.shape[3]
    steps = dec_ref.shape[1]
    shared = b_ref.shape[1] == 1

    def fill(jb):
        b_cols = b_ref[0, jb].astype(jnp.float32).T
        c_cols = c_ref[0, jb].astype(jnp.float32).T
        for t in range(steps):
            bb_ref[t] = jnp.broadcast_to(b_cols[:, t : t + 1], (state_dim, lanes))
            cb_ref[t] = jnp.broadcast_to(c_cols[:, t : t + 1], (state_dim, lanes))

    if shared:
        fill(0)
    for j in range(tiles):
        if not shared:
            fill(j)
        cols = slice(j * lanes, (j + 1) * lanes)
        state = s_ref[0, j].astype(jnp.float32)
        dec_all = dec_ref[0, :, cols]
        dx_all = dx_ref[0, :, cols]
        for t in range(steps):
            fresh = dec_all[t : t + 1, :] * state + dx_all[t : t + 1, :] * bb_ref[t]
            read_ref[0, t : t + 1, cols] = jnp.sum(fresh * cb_ref[t], axis=0, keepdims=True)
            state = fresh.astype(jnp.bfloat16).astype(jnp.float32)
        s_out_ref[0, j] = state.astype(jnp.bfloat16)


def ssm_scan(state_tiles, decay_rows, dx_rows, b_rows, c_rows):
    requests, tiles, state_dim, lanes = state_tiles.shape
    steps = decay_rows.shape[1]
    big = pl.BlockSpec((1, tiles, state_dim, lanes), lambda r: (r, 0, 0, 0))
    per_step = pl.BlockSpec((1, steps, tiles * lanes), lambda r: (r, 0, 0))
    rows = pl.BlockSpec((1,) + b_rows.shape[1:], lambda r: (r, 0, 0, 0))
    return pl.pallas_call(
        ssm_scan_kernel,
        grid=(requests,),
        in_specs=[big, per_step, per_step, rows, rows],
        out_specs=[big, per_step],
        out_shape=[
            jax.ShapeDtypeStruct(state_tiles.shape, jnp.bfloat16),
            jax.ShapeDtypeStruct(decay_rows.shape, jnp.float32),
        ],
        scratch_shapes=[
            pltpu.VMEM((steps, state_dim, lanes), jnp.float32),
            pltpu.VMEM((steps, state_dim, lanes), jnp.float32),
        ],
    )(state_tiles, decay_rows, dx_rows, b_rows, c_rows)


def ssm_scan_direct_kernel(
    head_dim, group_ref, s_ref, dec_ref, dx_ref, b_ref, c_ref, z_ref, sx_ref, gain_ref,
    s_out_ref, read_ref, gn_ref, bb_ref, cb_ref,
):
    ssm_scan_kernel(s_ref, dec_ref, dx_ref, b_ref, c_ref, s_out_ref, read_ref, bb_ref, cb_ref)
    reading = read_ref[0] + sx_ref[0]
    z = z_ref[0]
    gated = reading * (z * jax.nn.sigmoid(z))
    steps, width = gated.shape
    lane = lax.broadcasted_iota(jnp.int32, (steps, width), 1)
    scale = jnp.zeros_like(gated)
    for h in range(width // head_dim):
        inside = (lane >= h * head_dim) & (lane < (h + 1) * head_dim)
        square_sum = jnp.sum(jnp.where(inside, gated * gated, 0.0), axis=1, keepdims=True)
        scale = jnp.where(inside, lax.rsqrt(square_sum * (1.0 / head_dim) + eps), scale)
    gn_ref[0] = (gated * scale * gain_ref[...]).astype(gn_ref.dtype)


def ssm_scan_direct(
    state_tiles, decay_rows, dx_rows, bc_blocks, group, group_count, z_rows, skip_rows, gain_row, head_dim
):
    requests, tiles, state_dim, lanes = state_tiles.shape
    steps = decay_rows.shape[1]
    cols_local = bc_blocks.shape[3]
    c_start = group_count * state_dim

    def b_map(r, g):
        first = g[0] * state_dim
        return (first // cols_local, r, 0, (first % cols_local) // state_dim)

    def c_map(r, g):
        first = c_start + g[0] * state_dim
        return (first // cols_local, r, 0, (first % cols_local) // state_dim)

    big = pl.BlockSpec((1, tiles, state_dim, lanes), lambda r, g: (r, 0, 0, 0))
    per_step = pl.BlockSpec((1, steps, tiles * lanes), lambda r, g: (r, 0, 0))
    return pl.pallas_call(
        functools.partial(ssm_scan_direct_kernel, head_dim),
        grid_spec=pltpu.PrefetchScalarGridSpec(
            num_scalar_prefetch=1,
            grid=(requests,),
            in_specs=[
                big,
                per_step,
                per_step,
                pl.BlockSpec((1, 1, steps, state_dim), b_map),
                pl.BlockSpec((1, 1, steps, state_dim), c_map),
                per_step,
                per_step,
                pl.BlockSpec((1, tiles * lanes), lambda r, g: (0, 0)),
            ],
            out_specs=[big, per_step, per_step],
            scratch_shapes=[
                pltpu.VMEM((steps, state_dim, lanes), jnp.float32),
                pltpu.VMEM((steps, state_dim, lanes), jnp.float32),
            ],
        ),
        out_shape=[
            jax.ShapeDtypeStruct(state_tiles.shape, jnp.bfloat16),
            jax.ShapeDtypeStruct(decay_rows.shape, jnp.float32),
            jax.ShapeDtypeStruct(decay_rows.shape, jnp.bfloat16),
        ],
    )(group, state_tiles, decay_rows, dx_rows, bc_blocks, bc_blocks, z_rows, skip_rows, gain_row)


def broadcast_gather(block, count):
    copies = jnp.broadcast_to(block[None], (count,) + block.shape)
    return lax.all_to_all(copies, "head", 0, 0, tiled=True)


def shards(
    tokens,
    ssm_state,
    conv_x_state,
    conv_bc_state,
    expert_ids,
    mixer_gain,
    weight_xz,
    weight_bc,
    weight_delta,
    delta_bias,
    decay_log,
    skip_gain,
    conv_x_kernel,
    conv_x_bias,
    conv_bc_kernel,
    conv_bc_bias,
    gated_gain,
    weight_out,
    ffn_gain,
    router_weight,
    weight_up,
    weight_down,
):
    head_count = lax.axis_size("head")
    my_index = lax.axis_index("head")
    tok_local = tokens.shape[1]
    width = tokens.shape[2]
    requests = ssm_state.shape[1]
    heads_local = ssm_state.shape[2]
    head_dim = ssm_state.shape[3]
    state_dim = ssm_state.shape[4]
    gathered = broadcast_gather(tokens[0], head_count)
    inputs = gathered.reshape(requests * STEPS, width)
    normed = norm_rows(inputs.astype(jnp.float32), mixer_gain).astype(jnp.bfloat16)
    bc_fresh = (
        jnp.dot(normed, weight_bc, preferred_element_type=jnp.float32)
        .reshape(requests, STEPS, -1)
        .astype(jnp.bfloat16)
    )
    bc_conv, conv_bc_new = causal_conv(conv_bc_state[0], bc_fresh, conv_bc_kernel, conv_bc_bias)
    bc_conv = bc_conv.astype(jnp.bfloat16)
    bc_blocks = broadcast_gather(bc_conv, head_count)
    proj_xz = column_matmul(normed, weight_xz).reshape(
        requests, STEPS, heads_local, 2 * head_dim
    )
    x_fresh = (
        proj_xz[..., :head_dim].reshape(requests, STEPS, heads_local * head_dim).astype(jnp.bfloat16)
    )
    z_gate = proj_xz[..., head_dim:]
    delta = jax.nn.softplus(
        jnp.dot(normed, weight_delta, preferred_element_type=jnp.float32).reshape(
            requests, STEPS, heads_local
        )
        + delta_bias
    )
    x_conv, conv_x_new = causal_conv(conv_x_state[0], x_fresh, conv_x_kernel, conv_x_bias)
    x_heads = x_conv.reshape(requests, STEPS, heads_local, head_dim)
    decay_rate = jnp.exp(delta * -jnp.exp(decay_log))
    pack = 2 if heads_local % 2 == 0 else 1
    tiles = heads_local // pack
    lanes = pack * head_dim

    decay_rows = jnp.broadcast_to(
        decay_rate[..., None], (requests, STEPS, heads_local, head_dim)
    ).reshape(requests, STEPS, heads_local * head_dim)
    dx_rows = (delta[..., None] * x_heads).reshape(requests, STEPS, heads_local * head_dim)
    shared_group = (HEADS // G) % heads_local == 0
    tile_group = (my_index * heads_local + jnp.arange(1 if shared_group else tiles) * pack) // (
        HEADS // G
    )
    state_tiles = (
        ssm_state[0]
        .reshape(requests, tiles, pack, head_dim, state_dim)
        .transpose(0, 1, 4, 2, 3)
        .reshape(requests, tiles, state_dim, lanes)
    )
    fused_gate = shared_group and bc_blocks.shape[3] % state_dim == 0
    if fused_gate:
        skip_rows = (skip_gain[:, None] * x_heads).reshape(requests, STEPS, heads_local * head_dim)
        state_out, read_rows, gn_rows = ssm_scan_direct(
            state_tiles,
            decay_rows,
            dx_rows,
            bc_blocks,
            tile_group.astype(jnp.int32),
            G,
            z_gate.reshape(requests, STEPS, heads_local * head_dim),
            skip_rows,
            gated_gain.reshape(1, heads_local * head_dim),
            head_dim,
        )
    else:
        bc_all = jnp.moveaxis(bc_blocks, 0, 2).reshape(requests, STEPS, -1)
        bc_values = bc_all.astype(jnp.float32).reshape(requests, STEPS, 2, G, state_dim)
        b_rows = jnp.take(bc_values[:, :, 0], tile_group, axis=2).transpose(0, 2, 1, 3)
        c_rows = jnp.take(bc_values[:, :, 1], tile_group, axis=2).transpose(0, 2, 1, 3)
        state_out, read_rows = ssm_scan(state_tiles, decay_rows, dx_rows, b_rows, c_rows)
    ssm_now = (
        state_out.reshape(requests, tiles, state_dim, pack, head_dim)
        .transpose(0, 1, 3, 4, 2)
        .reshape(requests, heads_local, head_dim, state_dim)
    )
    if fused_gate:
        group_normed = gn_rows.reshape(requests * STEPS, heads_local * head_dim)
    else:
        scan_read = read_rows.reshape(requests, STEPS, heads_local, head_dim)
        readings = scan_read + skip_gain[:, None] * x_heads
        gated_out = readings * jax.nn.silu(z_gate)
        group_normed = (
            norm_rows(gated_out, gated_gain.reshape(heads_local, head_dim))
            .astype(jnp.bfloat16)
            .reshape(requests * STEPS, heads_local * head_dim)
        )
    per_expert = head_count // EXPERTS
    mixer_part = jnp.dot(group_normed, weight_out, preferred_element_type=jnp.float32)
    mixer_out = lax.all_to_all(
        mixer_part.reshape(head_count, tok_local, width), "head", 0, 0, tiled=True
    ).sum(axis=0)
    residual = (tokens[0].astype(jnp.float32) + mixer_out).astype(jnp.bfloat16)
    ffn_in = norm_rows(residual.astype(jnp.float32), ffn_gain).astype(jnp.bfloat16)
    share = route_share(ffn_in, router_weight, expert_ids[0])
    chosen = expert_ids[0].reshape(-1)
    onehot = (chosen[:, None] == jnp.arange(EXPERTS)[None, :]).astype(jnp.int32)
    earlier = jnp.cumsum(onehot, axis=0) - onehot
    position = jnp.sum(earlier * onehot, axis=1)
    slot_index = chosen * CAP + position
    place = (jnp.arange(EXPERTS * CAP)[:, None] == slot_index[None, :]).astype(jnp.bfloat16)
    routed_rows = jnp.repeat(ffn_in, TOP, axis=0)
    packed = jnp.dot(place, routed_rows, preferred_element_type=jnp.float32).astype(jnp.bfloat16)
    outgoing = jnp.repeat(packed.reshape(EXPERTS, CAP, width), per_expert, axis=0)
    received = lax.all_to_all(outgoing, "head", split_axis=0, concat_axis=0, tiled=True)
    flat_rows = received.reshape(-1, width)
    hidden = expert_hidden(flat_rows, weight_up)
    computed = jnp.dot(hidden, weight_down, preferred_element_type=jnp.float32).reshape(
        received.shape[0], received.shape[1], width
    )
    returned = lax.all_to_all(
        computed.astype(jnp.bfloat16), "head", split_axis=0, concat_axis=0, tiled=True
    ).astype(computed.dtype)
    summed = (
        returned.reshape(EXPERTS, per_expert, CAP, width).sum(axis=1).reshape(EXPERTS * CAP, width)
    )
    per_route = jnp.dot(place.astype(jnp.float32).T, summed, precision=highest).reshape(
        tok_local, TOP, width
    )
    combined = jnp.sum(share[:, :, None] * per_route, axis=1)
    layer_out = (residual.astype(jnp.float32) + combined).astype(jnp.bfloat16)
    return (layer_out[None], ssm_now[None], conv_x_new[None], conv_bc_new[None])


def solution(mesh):
    return jax.shard_map(
        shards,
        mesh=mesh,
        in_specs=(
            P("req", ("groups", "head"), None),
            P("req", "groups", "head", None, None),
            P("req", "groups", None, "head"),
            P("req", "groups", None, "head"),
            P("req", ("groups", "head"), None),
            P(),
            P(None, "head"),
            P(None, "head"),
            P(None, "head"),
            P("head"),
            P("head"),
            P("head"),
            P(None, "head"),
            P("head"),
            P(None, "head"),
            P("head"),
            P("head"),
            P("head", None),
            P(),
            P(),
            P(None, "head"),
            P("head", None),
        ),
        out_specs=(
            P("req", ("groups", "head"), None),
            P("req", "groups", "head", None, None),
            P("req", "groups", None, "head"),
            P("req", "groups", None, "head"),
        ),
        check_vma=False,
    )
```

```python
import functools

import jax
import jax.numpy as jnp
from jax import lax
from jax.experimental import pallas as pl
from jax.experimental.pallas import tpu as pltpu
from jax.sharding import PartitionSpec as P

HEADS = 128
G = 8
EXPERTS = 8
TOP = 2
STEPS = 8
CAP = 2


eps = 1e-05
highest = lax.Precision.HIGHEST


def norm_rows(values, gain):
    mean_square = jnp.mean(values * values, axis=-1, keepdims=True)
    return values * lax.rsqrt(mean_square + eps) * gain


def causal_conv(past_rows, fresh_rows, kernel, offset):
    window = jnp.concatenate([past_rows, fresh_rows], axis=1)
    window_wide = window.astype(jnp.float32)
    fresh_count = fresh_rows.shape[1]
    running = offset + kernel[0] * window_wide[:, 0:fresh_count]
    for tap_index in range(1, kernel.shape[0]):
        running = running + kernel[tap_index] * window_wide[:, tap_index : tap_index + fresh_count]
    return (jax.nn.silu(running), window[:, fresh_count:])


def route_share(ffn_in, router_weight, chosen_ids):
    logits = jnp.dot(ffn_in, router_weight, preferred_element_type=jnp.float32)
    match_table = (chosen_ids[:, :, None] == jnp.arange(EXPERTS)[None, None, :]).astype(jnp.float32)
    picked = jnp.einsum("mke,me->mk", match_table, logits, precision=highest)
    first_weight = jax.nn.sigmoid(picked[:, 0] - picked[:, 1])
    return jnp.stack([first_weight, 1.0 - first_weight], axis=1)


def expert_hidden(rows_in, weight_up):
    return jnp.square(
        jnp.maximum(jnp.dot(rows_in, weight_up, preferred_element_type=jnp.float32), 0.0)
    ).astype(jnp.bfloat16)


def column_matmul_kernel(a_ref, w_ref, o_ref):
    o_ref[...] = jnp.dot(a_ref[...], w_ref[...], preferred_element_type=jnp.float32)


def column_matmul(rows, weight):
    m, k = rows.shape
    cols = weight.shape[1]
    block = min(1024, cols)
    return pl.pallas_call(
        column_matmul_kernel,
        grid=(cols // block,),
        in_specs=[
            pl.BlockSpec((m, k), lambda j: (0, 0)),
            pl.BlockSpec((k, block), lambda j: (0, j)),
        ],
        out_specs=pl.BlockSpec((m, block), lambda j: (0, j)),
        out_shape=jax.ShapeDtypeStruct((m, cols), jnp.float32),
        cost_estimate=pl.CostEstimate(
            flops=2 * m * k * cols,
            transcendentals=0,
            bytes_accessed=2 * (m * k + k * cols) + 4 * m * cols,
        ),
    )(rows, weight)


def xz_matmul_kernel(head_dim, a_ref, w_ref, x_ref, z_ref):
    product = jnp.dot(a_ref[...], w_ref[...], preferred_element_type=jnp.float32)
    width = z_ref.shape[1]
    for h in range(width // head_dim):
        x_ref[:, h * head_dim : (h + 1) * head_dim] = product[
            :, 2 * h * head_dim : (2 * h + 1) * head_dim
        ].astype(x_ref.dtype)
        z_ref[:, h * head_dim : (h + 1) * head_dim] = product[
            :, (2 * h + 1) * head_dim : (2 * h + 2) * head_dim
        ]


def xz_matmul(rows, weight, head_dim):
    m, k = rows.shape
    cols = weight.shape[1]
    block = min(512, cols)
    return pl.pallas_call(
        functools.partial(xz_matmul_kernel, head_dim),
        grid=(cols // block,),
        in_specs=[
            pl.BlockSpec((m, k), lambda j: (0, 0)),
            pl.BlockSpec((k, block), lambda j: (0, j)),
        ],
        out_specs=[
            pl.BlockSpec((m, block // 2), lambda j: (0, j)),
            pl.BlockSpec((m, block // 2), lambda j: (0, j)),
        ],
        out_shape=[
            jax.ShapeDtypeStruct((m, cols // 2), jnp.bfloat16),
            jax.ShapeDtypeStruct((m, cols // 2), jnp.float32),
        ],
        cost_estimate=pl.CostEstimate(
            flops=2 * m * k * cols,
            transcendentals=0,
            bytes_accessed=2 * (m * k + k * cols) + 3 * m * cols,
        ),
    )(rows, weight)


def ssm_scan_kernel(s_ref, dec_ref, dx_ref, b_ref, c_ref, s_out_ref, read_ref, bb_ref, cb_ref):
    tiles = s_ref.shape[1]
    state_dim = s_ref.shape[2]
    lanes = s_ref.shape[3]
    steps = dec_ref.shape[1]
    shared = b_ref.shape[1] == 1

    def fill(jb):
        b_cols = b_ref[0, jb].astype(jnp.float32).T
        c_cols = c_ref[0, jb].astype(jnp.float32).T
        for t in range(steps):
            bb_ref[t] = jnp.broadcast_to(b_cols[:, t : t + 1], (state_dim, lanes))
            cb_ref[t] = jnp.broadcast_to(c_cols[:, t : t + 1], (state_dim, lanes))

    if shared:
        fill(0)
    for j in range(tiles):
        if not shared:
            fill(j)
        cols = slice(j * lanes, (j + 1) * lanes)
        state = s_ref[0, j].astype(jnp.float32)
        dec_all = dec_ref[0, :, cols]
        dx_all = dx_ref[0, :, cols]
        for t in range(steps):
            fresh = dec_all[t : t + 1, :] * state + dx_all[t : t + 1, :] * bb_ref[t]
            read_ref[0, t : t + 1, cols] = jnp.sum(fresh * cb_ref[t], axis=0, keepdims=True)
            state = fresh.astype(jnp.bfloat16).astype(jnp.float32)
        s_out_ref[0, j] = state.astype(jnp.bfloat16)


def ssm_scan(state_tiles, decay_rows, dx_rows, b_rows, c_rows):
    requests, tiles, state_dim, lanes = state_tiles.shape
    steps = decay_rows.shape[1]
    big = pl.BlockSpec((1, tiles, state_dim, lanes), lambda r: (r, 0, 0, 0))
    per_step = pl.BlockSpec((1, steps, tiles * lanes), lambda r: (r, 0, 0))
    rows = pl.BlockSpec((1,) + b_rows.shape[1:], lambda r: (r, 0, 0, 0))
    return pl.pallas_call(
        ssm_scan_kernel,
        grid=(requests,),
        in_specs=[big, per_step, per_step, rows, rows],
        out_specs=[big, per_step],
        out_shape=[
            jax.ShapeDtypeStruct(state_tiles.shape, jnp.bfloat16),
            jax.ShapeDtypeStruct(decay_rows.shape, jnp.float32),
        ],
        scratch_shapes=[
            pltpu.VMEM((steps, state_dim, lanes), jnp.float32),
            pltpu.VMEM((steps, state_dim, lanes), jnp.float32),
        ],
    )(state_tiles, decay_rows, dx_rows, b_rows, c_rows)


def ssm_scan_direct_kernel(
    head_dim, group_ref, s_ref, dec_ref, dx_ref, b_ref, c_ref, z_ref, sx_ref, gain_ref,
    s_out_ref, read_ref, gn_ref, bb_ref, cb_ref,
):
    ssm_scan_kernel(s_ref, dec_ref, dx_ref, b_ref, c_ref, s_out_ref, read_ref, bb_ref, cb_ref)
    reading = read_ref[0] + sx_ref[0]
    z = z_ref[0]
    gated = reading * (z * jax.nn.sigmoid(z))
    steps, width = gated.shape
    lane = lax.broadcasted_iota(jnp.int32, (steps, width), 1)
    scale = jnp.zeros_like(gated)
    for h in range(width // head_dim):
        inside = (lane >= h * head_dim) & (lane < (h + 1) * head_dim)
        square_sum = jnp.sum(jnp.where(inside, gated * gated, 0.0), axis=1, keepdims=True)
        scale = jnp.where(inside, lax.rsqrt(square_sum * (1.0 / head_dim) + eps), scale)
    gn_ref[0] = (gated * scale * gain_ref[...]).astype(gn_ref.dtype)


def ssm_scan_direct(
    state_tiles, decay_rows, dx_rows, bc_blocks, group, group_count, z_rows, skip_rows, gain_row, head_dim
):
    requests, tiles, state_dim, lanes = state_tiles.shape
    steps = decay_rows.shape[1]
    cols_local = bc_blocks.shape[3]
    c_start = group_count * state_dim

    def b_map(r, g):
        first = g[0] * state_dim
        return (first // cols_local, r, 0, (first % cols_local) // state_dim)

    def c_map(r, g):
        first = c_start + g[0] * state_dim
        return (first // cols_local, r, 0, (first % cols_local) // state_dim)

    big = pl.BlockSpec((1, tiles, state_dim, lanes), lambda r, g: (r, 0, 0, 0))
    per_step = pl.BlockSpec((1, steps, tiles * lanes), lambda r, g: (r, 0, 0))
    return pl.pallas_call(
        functools.partial(ssm_scan_direct_kernel, head_dim),
        grid_spec=pltpu.PrefetchScalarGridSpec(
            num_scalar_prefetch=1,
            grid=(requests,),
            in_specs=[
                big,
                per_step,
                per_step,
                pl.BlockSpec((1, 1, steps, state_dim), b_map),
                pl.BlockSpec((1, 1, steps, state_dim), c_map),
                per_step,
                per_step,
                pl.BlockSpec((1, tiles * lanes), lambda r, g: (0, 0)),
            ],
            out_specs=[big, per_step, per_step],
            scratch_shapes=[
                pltpu.VMEM((steps, state_dim, lanes), jnp.float32),
                pltpu.VMEM((steps, state_dim, lanes), jnp.float32),
            ],
        ),
        out_shape=[
            jax.ShapeDtypeStruct(state_tiles.shape, jnp.bfloat16),
            jax.ShapeDtypeStruct(decay_rows.shape, jnp.float32),
            jax.ShapeDtypeStruct(decay_rows.shape, jnp.bfloat16),
        ],
    )(group, state_tiles, decay_rows, dx_rows, bc_blocks, bc_blocks, z_rows, skip_rows, gain_row)


def broadcast_gather(block, count):
    copies = jnp.broadcast_to(block[None], (count,) + block.shape)
    return lax.all_to_all(copies, "head", 0, 0, tiled=True)


def shards(
    tokens,
    ssm_state,
    conv_x_state,
    conv_bc_state,
    expert_ids,
    mixer_gain,
    weight_xz,
    weight_bc,
    weight_delta,
    delta_bias,
    decay_log,
    skip_gain,
    conv_x_kernel,
    conv_x_bias,
    conv_bc_kernel,
    conv_bc_bias,
    gated_gain,
    weight_out,
    ffn_gain,
    router_weight,
    weight_up,
    weight_down,
):
    head_count = lax.axis_size("head")
    my_index = lax.axis_index("head")
    tok_local = tokens.shape[1]
    width = tokens.shape[2]
    requests = ssm_state.shape[1]
    heads_local = ssm_state.shape[2]
    head_dim = ssm_state.shape[3]
    state_dim = ssm_state.shape[4]
    gathered = broadcast_gather(tokens[0], head_count)
    inputs = gathered.reshape(requests * STEPS, width)
    normed = norm_rows(inputs.astype(jnp.float32), mixer_gain).astype(jnp.bfloat16)
    bc_fresh = (
        jnp.dot(normed, weight_bc, preferred_element_type=jnp.float32)
        .reshape(requests, STEPS, -1)
        .astype(jnp.bfloat16)
    )
    bc_conv, conv_bc_new = causal_conv(conv_bc_state[0], bc_fresh, conv_bc_kernel, conv_bc_bias)
    x_rows, z_rows = xz_matmul(normed, weight_xz, head_dim)
    bc_conv, x_rows, z_rows = lax.optimization_barrier((bc_conv.astype(jnp.bfloat16), x_rows, z_rows))
    bc_blocks = broadcast_gather(bc_conv, head_count)
    x_fresh = x_rows.reshape(requests, STEPS, heads_local * head_dim)
    z_gate = z_rows.reshape(requests, STEPS, heads_local, head_dim)
    delta = jax.nn.softplus(
        jnp.dot(normed, weight_delta, preferred_element_type=jnp.float32).reshape(
            requests, STEPS, heads_local
        )
        + delta_bias
    )
    x_conv, conv_x_new = causal_conv(conv_x_state[0], x_fresh, conv_x_kernel, conv_x_bias)
    x_heads = x_conv.reshape(requests, STEPS, heads_local, head_dim)
    decay_rate = jnp.exp(delta * -jnp.exp(decay_log))
    pack = 2 if heads_local % 2 == 0 else 1
    tiles = heads_local // pack
    lanes = pack * head_dim

    decay_rows = jnp.broadcast_to(
        decay_rate[..., None], (requests, STEPS, heads_local, head_dim)
    ).reshape(requests, STEPS, heads_local * head_dim)
    dx_rows = (delta[..., None] * x_heads).reshape(requests, STEPS, heads_local * head_dim)
    shared_group = (HEADS // G) % heads_local == 0
    tile_group = (my_index * heads_local + jnp.arange(1 if shared_group else tiles) * pack) // (
        HEADS // G
    )
    state_tiles = (
        ssm_state[0]
        .reshape(requests, tiles, pack, head_dim, state_dim)
        .transpose(0, 1, 4, 2, 3)
        .reshape(requests, tiles, state_dim, lanes)
    )
    fused_gate = shared_group and bc_blocks.shape[3] % state_dim == 0
    if fused_gate:
        skip_rows = (skip_gain[:, None] * x_heads).reshape(requests, STEPS, heads_local * head_dim)
        state_out, read_rows, gn_rows = ssm_scan_direct(
            state_tiles,
            decay_rows,
            dx_rows,
            bc_blocks,
            tile_group.astype(jnp.int32),
            G,
            z_gate.reshape(requests, STEPS, heads_local * head_dim),
            skip_rows,
            gated_gain.reshape(1, heads_local * head_dim),
            head_dim,
        )
    else:
        bc_all = jnp.moveaxis(bc_blocks, 0, 2).reshape(requests, STEPS, -1)
        bc_values = bc_all.astype(jnp.float32).reshape(requests, STEPS, 2, G, state_dim)
        b_rows = jnp.take(bc_values[:, :, 0], tile_group, axis=2).transpose(0, 2, 1, 3)
        c_rows = jnp.take(bc_values[:, :, 1], tile_group, axis=2).transpose(0, 2, 1, 3)
        state_out, read_rows = ssm_scan(state_tiles, decay_rows, dx_rows, b_rows, c_rows)
    ssm_now = (
        state_out.reshape(requests, tiles, state_dim, pack, head_dim)
        .transpose(0, 1, 3, 4, 2)
        .reshape(requests, heads_local, head_dim, state_dim)
    )
    if fused_gate:
        group_normed = gn_rows.reshape(requests * STEPS, heads_local * head_dim)
    else:
        scan_read = read_rows.reshape(requests, STEPS, heads_local, head_dim)
        readings = scan_read + skip_gain[:, None] * x_heads
        gated_out = readings * jax.nn.silu(z_gate)
        group_normed = (
            norm_rows(gated_out, gated_gain.reshape(heads_local, head_dim))
            .astype(jnp.bfloat16)
            .reshape(requests * STEPS, heads_local * head_dim)
        )
    per_expert = head_count // EXPERTS
    mixer_part = jnp.dot(group_normed, weight_out, preferred_element_type=jnp.float32)
    mixer_out = lax.all_to_all(
        mixer_part.reshape(head_count, tok_local, width), "head", 0, 0, tiled=True
    ).sum(axis=0)
    residual = (tokens[0].astype(jnp.float32) + mixer_out).astype(jnp.bfloat16)
    ffn_in = norm_rows(residual.astype(jnp.float32), ffn_gain).astype(jnp.bfloat16)
    share = route_share(ffn_in, router_weight, expert_ids[0])
    chosen = expert_ids[0].reshape(-1)
    onehot = (chosen[:, None] == jnp.arange(EXPERTS)[None, :]).astype(jnp.int32)
    earlier = jnp.cumsum(onehot, axis=0) - onehot
    position = jnp.sum(earlier * onehot, axis=1)
    slot_index = chosen * CAP + position
    place = (jnp.arange(EXPERTS * CAP)[:, None] == slot_index[None, :]).astype(jnp.bfloat16)
    routed_rows = jnp.repeat(ffn_in, TOP, axis=0)
    packed = jnp.dot(place, routed_rows, preferred_element_type=jnp.float32).astype(jnp.bfloat16)
    outgoing = jnp.repeat(packed.reshape(EXPERTS, CAP, width), per_expert, axis=0)
    received = lax.all_to_all(outgoing, "head", split_axis=0, concat_axis=0, tiled=True)
    flat_rows = received.reshape(-1, width)
    hidden = expert_hidden(flat_rows, weight_up)
    computed = jnp.dot(hidden, weight_down, preferred_element_type=jnp.float32).reshape(
        received.shape[0], received.shape[1], width
    )
    returned = lax.all_to_all(
        computed.astype(jnp.bfloat16), "head", split_axis=0, concat_axis=0, tiled=True
    ).astype(computed.dtype)
    summed = (
        returned.reshape(EXPERTS, per_expert, CAP, width).sum(axis=1).reshape(EXPERTS * CAP, width)
    )
    per_route = jnp.dot(place.astype(jnp.float32).T, summed, precision=highest).reshape(
        tok_local, TOP, width
    )
    combined = jnp.sum(share[:, :, None] * per_route, axis=1)
    layer_out = (residual.astype(jnp.float32) + combined).astype(jnp.bfloat16)
    return (layer_out[None], ssm_now[None], conv_x_new[None], conv_bc_new[None])


def solution(mesh):
    return jax.shard_map(
        shards,
        mesh=mesh,
        in_specs=(
            P("req", ("groups", "head"), None),
            P("req", "groups", "head", None, None),
            P("req", "groups", None, "head"),
            P("req", "groups", None, "head"),
            P("req", ("groups", "head"), None),
            P(),
            P(None, "head"),
            P(None, "head"),
            P(None, "head"),
            P("head"),
            P("head"),
            P("head"),
            P(None, "head"),
            P("head"),
            P(None, "head"),
            P("head"),
            P("head"),
            P("head", None),
            P(),
            P(),
            P(None, "head"),
            P("head", None),
        ),
        out_specs=(
            P("req", ("groups", "head"), None),
            P("req", "groups", "head", None, None),
            P("req", "groups", None, "head"),
            P("req", "groups", None, "head"),
        ),
        check_vma=False,
    )
```

```python
import functools

import jax
import jax.numpy as jnp
from jax import lax
from jax.experimental import pallas as pl
from jax.experimental.pallas import tpu as pltpu
from jax.sharding import PartitionSpec as P

HEADS = 128
G = 8
EXPERTS = 8
TOP = 2
STEPS = 8
CAP = 2


eps = 1e-05
highest = lax.Precision.HIGHEST


def norm_rows(values, gain):
    mean_square = jnp.mean(values * values, axis=-1, keepdims=True)
    return values * lax.rsqrt(mean_square + eps) * gain


def causal_conv(past_rows, fresh_rows, kernel, offset):
    window = jnp.concatenate([past_rows, fresh_rows], axis=1)
    window_wide = window.astype(jnp.float32)
    fresh_count = fresh_rows.shape[1]
    running = offset + kernel[0] * window_wide[:, 0:fresh_count]
    for tap_index in range(1, kernel.shape[0]):
        running = running + kernel[tap_index] * window_wide[:, tap_index : tap_index + fresh_count]
    return (jax.nn.silu(running), window[:, fresh_count:])


def route_share(ffn_in, router_weight, chosen_ids):
    logits = jnp.dot(ffn_in, router_weight, preferred_element_type=jnp.float32)
    match_table = (chosen_ids[:, :, None] == jnp.arange(EXPERTS)[None, None, :]).astype(jnp.float32)
    picked = jnp.einsum("mke,me->mk", match_table, logits, precision=highest)
    first_weight = jax.nn.sigmoid(picked[:, 0] - picked[:, 1])
    return jnp.stack([first_weight, 1.0 - first_weight], axis=1)


def expert_hidden(rows_in, weight_up):
    return jnp.square(
        jnp.maximum(jnp.dot(rows_in, weight_up, preferred_element_type=jnp.float32), 0.0)
    ).astype(jnp.bfloat16)


def column_matmul_kernel(a_ref, w_ref, o_ref):
    o_ref[...] = jnp.dot(a_ref[...], w_ref[...], preferred_element_type=jnp.float32)


def column_matmul(rows, weight):
    m, k = rows.shape
    cols = weight.shape[1]
    block = min(1024, cols)
    return pl.pallas_call(
        column_matmul_kernel,
        grid=(cols // block,),
        in_specs=[
            pl.BlockSpec((m, k), lambda j: (0, 0)),
            pl.BlockSpec((k, block), lambda j: (0, j)),
        ],
        out_specs=pl.BlockSpec((m, block), lambda j: (0, j)),
        out_shape=jax.ShapeDtypeStruct((m, cols), jnp.float32),
        cost_estimate=pl.CostEstimate(
            flops=2 * m * k * cols,
            transcendentals=0,
            bytes_accessed=2 * (m * k + k * cols) + 4 * m * cols,
        ),
    )(rows, weight)


def xz_matmul_kernel(head_dim, a_ref, g_ref, w_ref, n_ref, x_ref, z_ref, normed_ref):
    @pl.when(pl.program_id(0) == 0)
    def _():
        values = a_ref[...].astype(jnp.float32)
        mean_square = jnp.mean(values * values, axis=-1, keepdims=True)
        normed = (values * lax.rsqrt(mean_square + eps) * g_ref[...]).astype(jnp.bfloat16)
        normed_ref[...] = normed
        n_ref[...] = normed

    product = jnp.dot(normed_ref[...], w_ref[...], preferred_element_type=jnp.float32)
    width = z_ref.shape[1]
    for h in range(width // head_dim):
        x_ref[:, h * head_dim : (h + 1) * head_dim] = product[
            :, 2 * h * head_dim : (2 * h + 1) * head_dim
        ].astype(x_ref.dtype)
        z_ref[:, h * head_dim : (h + 1) * head_dim] = product[
            :, (2 * h + 1) * head_dim : (2 * h + 2) * head_dim
        ]


def xz_matmul(rows, gain, weight, head_dim):
    m, k = rows.shape
    cols = weight.shape[1]
    block = min(512, cols)
    return pl.pallas_call(
        functools.partial(xz_matmul_kernel, head_dim),
        grid=(cols // block,),
        in_specs=[
            pl.BlockSpec((m, k), lambda j: (0, 0)),
            pl.BlockSpec((1, k), lambda j: (0, 0)),
            pl.BlockSpec((k, block), lambda j: (0, j)),
        ],
        out_specs=[
            pl.BlockSpec((m, k), lambda j: (0, 0)),
            pl.BlockSpec((m, block // 2), lambda j: (0, j)),
            pl.BlockSpec((m, block // 2), lambda j: (0, j)),
        ],
        out_shape=[
            jax.ShapeDtypeStruct((m, k), jnp.bfloat16),
            jax.ShapeDtypeStruct((m, cols // 2), jnp.bfloat16),
            jax.ShapeDtypeStruct((m, cols // 2), jnp.float32),
        ],
        scratch_shapes=[pltpu.VMEM((m, k), jnp.bfloat16)],
        cost_estimate=pl.CostEstimate(
            flops=2 * m * k * cols,
            transcendentals=m,
            bytes_accessed=2 * (2 * m * k + k * cols) + 3 * m * cols,
        ),
    )(rows, gain.reshape(1, k), weight)


def ssm_scan_kernel(s_ref, dec_ref, dx_ref, b_ref, c_ref, s_out_ref, read_ref, bb_ref, cb_ref):
    tiles = s_ref.shape[1]
    state_dim = s_ref.shape[2]
    lanes = s_ref.shape[3]
    steps = dec_ref.shape[1]
    shared = b_ref.shape[1] == 1

    def fill(jb):
        b_cols = b_ref[0, jb].astype(jnp.float32).T
        c_cols = c_ref[0, jb].astype(jnp.float32).T
        for t in range(steps):
            bb_ref[t] = jnp.broadcast_to(b_cols[:, t : t + 1], (state_dim, lanes))
            cb_ref[t] = jnp.broadcast_to(c_cols[:, t : t + 1], (state_dim, lanes))

    if shared:
        fill(0)
    for j in range(tiles):
        if not shared:
            fill(j)
        cols = slice(j * lanes, (j + 1) * lanes)
        state = s_ref[0, j].astype(jnp.float32)
        dec_all = dec_ref[0, :, cols]
        dx_all = dx_ref[0, :, cols]
        for t in range(steps):
            fresh = dec_all[t : t + 1, :] * state + dx_all[t : t + 1, :] * bb_ref[t]
            read_ref[0, t : t + 1, cols] = jnp.sum(fresh * cb_ref[t], axis=0, keepdims=True)
            state = fresh.astype(jnp.bfloat16).astype(jnp.float32)
        s_out_ref[0, j] = state.astype(jnp.bfloat16)


def ssm_scan(state_tiles, decay_rows, dx_rows, b_rows, c_rows):
    requests, tiles, state_dim, lanes = state_tiles.shape
    steps = decay_rows.shape[1]
    big = pl.BlockSpec((1, tiles, state_dim, lanes), lambda r: (r, 0, 0, 0))
    per_step = pl.BlockSpec((1, steps, tiles * lanes), lambda r: (r, 0, 0))
    rows = pl.BlockSpec((1,) + b_rows.shape[1:], lambda r: (r, 0, 0, 0))
    return pl.pallas_call(
        ssm_scan_kernel,
        grid=(requests,),
        in_specs=[big, per_step, per_step, rows, rows],
        out_specs=[big, per_step],
        out_shape=[
            jax.ShapeDtypeStruct(state_tiles.shape, jnp.bfloat16),
            jax.ShapeDtypeStruct(decay_rows.shape, jnp.float32),
        ],
        scratch_shapes=[
            pltpu.VMEM((steps, state_dim, lanes), jnp.float32),
            pltpu.VMEM((steps, state_dim, lanes), jnp.float32),
        ],
    )(state_tiles, decay_rows, dx_rows, b_rows, c_rows)


def ssm_scan_direct_kernel(
    head_dim, group_ref, s_ref, dec_ref, dx_ref, b_ref, c_ref, z_ref, sx_ref, gain_ref,
    s_out_ref, read_ref, gn_ref, bb_ref, cb_ref,
):
    ssm_scan_kernel(s_ref, dec_ref, dx_ref, b_ref, c_ref, s_out_ref, read_ref, bb_ref, cb_ref)
    reading = read_ref[0] + sx_ref[0]
    z = z_ref[0]
    gated = reading * (z * jax.nn.sigmoid(z))
    steps, width = gated.shape
    lane = lax.broadcasted_iota(jnp.int32, (steps, width), 1)
    scale = jnp.zeros_like(gated)
    for h in range(width // head_dim):
        inside = (lane >= h * head_dim) & (lane < (h + 1) * head_dim)
        square_sum = jnp.sum(jnp.where(inside, gated * gated, 0.0), axis=1, keepdims=True)
        scale = jnp.where(inside, lax.rsqrt(square_sum * (1.0 / head_dim) + eps), scale)
    gn_ref[0] = (gated * scale * gain_ref[...]).astype(gn_ref.dtype)


def ssm_scan_direct(
    state_tiles, decay_rows, dx_rows, bc_blocks, group, group_count, z_rows, skip_rows, gain_row, head_dim
):
    requests, tiles, state_dim, lanes = state_tiles.shape
    steps = decay_rows.shape[1]
    cols_local = bc_blocks.shape[3]
    c_start = group_count * state_dim

    def b_map(r, g):
        first = g[0] * state_dim
        return (first // cols_local, r, 0, (first % cols_local) // state_dim)

    def c_map(r, g):
        first = c_start + g[0] * state_dim
        return (first // cols_local, r, 0, (first % cols_local) // state_dim)

    big = pl.BlockSpec((1, tiles, state_dim, lanes), lambda r, g: (r, 0, 0, 0))
    per_step = pl.BlockSpec((1, steps, tiles * lanes), lambda r, g: (r, 0, 0))
    return pl.pallas_call(
        functools.partial(ssm_scan_direct_kernel, head_dim),
        grid_spec=pltpu.PrefetchScalarGridSpec(
            num_scalar_prefetch=1,
            grid=(requests,),
            in_specs=[
                big,
                per_step,
                per_step,
                pl.BlockSpec((1, 1, steps, state_dim), b_map),
                pl.BlockSpec((1, 1, steps, state_dim), c_map),
                per_step,
                per_step,
                pl.BlockSpec((1, tiles * lanes), lambda r, g: (0, 0)),
            ],
            out_specs=[big, per_step, per_step],
            scratch_shapes=[
                pltpu.VMEM((steps, state_dim, lanes), jnp.float32),
                pltpu.VMEM((steps, state_dim, lanes), jnp.float32),
            ],
        ),
        out_shape=[
            jax.ShapeDtypeStruct(state_tiles.shape, jnp.bfloat16),
            jax.ShapeDtypeStruct(decay_rows.shape, jnp.float32),
            jax.ShapeDtypeStruct(decay_rows.shape, jnp.bfloat16),
        ],
    )(group, state_tiles, decay_rows, dx_rows, bc_blocks, bc_blocks, z_rows, skip_rows, gain_row)


def broadcast_gather(block, count):
    copies = jnp.broadcast_to(block[None], (count,) + block.shape)
    return lax.all_to_all(copies, "head", 0, 0, tiled=True)


def shards(
    tokens,
    ssm_state,
    conv_x_state,
    conv_bc_state,
    expert_ids,
    mixer_gain,
    weight_xz,
    weight_bc,
    weight_delta,
    delta_bias,
    decay_log,
    skip_gain,
    conv_x_kernel,
    conv_x_bias,
    conv_bc_kernel,
    conv_bc_bias,
    gated_gain,
    weight_out,
    ffn_gain,
    router_weight,
    weight_up,
    weight_down,
):
    head_count = lax.axis_size("head")
    my_index = lax.axis_index("head")
    tok_local = tokens.shape[1]
    width = tokens.shape[2]
    requests = ssm_state.shape[1]
    heads_local = ssm_state.shape[2]
    head_dim = ssm_state.shape[3]
    state_dim = ssm_state.shape[4]
    gathered = broadcast_gather(tokens[0], head_count)
    inputs = gathered.reshape(requests * STEPS, width)
    normed, x_rows, z_rows = xz_matmul(inputs, mixer_gain, weight_xz, head_dim)
    bc_fresh = (
        jnp.dot(normed, weight_bc, preferred_element_type=jnp.float32)
        .reshape(requests, STEPS, -1)
        .astype(jnp.bfloat16)
    )
    bc_conv, conv_bc_new = causal_conv(conv_bc_state[0], bc_fresh, conv_bc_kernel, conv_bc_bias)
    bc_conv, x_rows, z_rows = lax.optimization_barrier((bc_conv.astype(jnp.bfloat16), x_rows, z_rows))
    bc_blocks = broadcast_gather(bc_conv, head_count)
    x_fresh = x_rows.reshape(requests, STEPS, heads_local * head_dim)
    z_gate = z_rows.reshape(requests, STEPS, heads_local, head_dim)
    delta = jax.nn.softplus(
        jnp.dot(normed, weight_delta, preferred_element_type=jnp.float32).reshape(
            requests, STEPS, heads_local
        )
        + delta_bias
    )
    x_conv, conv_x_new = causal_conv(conv_x_state[0], x_fresh, conv_x_kernel, conv_x_bias)
    x_heads = x_conv.reshape(requests, STEPS, heads_local, head_dim)
    decay_rate = jnp.exp(delta * -jnp.exp(decay_log))
    pack = 2 if heads_local % 2 == 0 else 1
    tiles = heads_local // pack
    lanes = pack * head_dim

    decay_rows = jnp.broadcast_to(
        decay_rate[..., None], (requests, STEPS, heads_local, head_dim)
    ).reshape(requests, STEPS, heads_local * head_dim)
    dx_rows = (delta[..., None] * x_heads).reshape(requests, STEPS, heads_local * head_dim)
    shared_group = (HEADS // G) % heads_local == 0
    tile_group = (my_index * heads_local + jnp.arange(1 if shared_group else tiles) * pack) // (
        HEADS // G
    )
    state_tiles = (
        ssm_state[0]
        .reshape(requests, tiles, pack, head_dim, state_dim)
        .transpose(0, 1, 4, 2, 3)
        .reshape(requests, tiles, state_dim, lanes)
    )
    fused_gate = shared_group and bc_blocks.shape[3] % state_dim == 0
    if fused_gate:
        skip_rows = (skip_gain[:, None] * x_heads).reshape(requests, STEPS, heads_local * head_dim)
        state_out, read_rows, gn_rows = ssm_scan_direct(
            state_tiles,
            decay_rows,
            dx_rows,
            bc_blocks,
            tile_group.astype(jnp.int32),
            G,
            z_gate.reshape(requests, STEPS, heads_local * head_dim),
            skip_rows,
            gated_gain.reshape(1, heads_local * head_dim),
            head_dim,
        )
    else:
        bc_all = jnp.moveaxis(bc_blocks, 0, 2).reshape(requests, STEPS, -1)
        bc_values = bc_all.astype(jnp.float32).reshape(requests, STEPS, 2, G, state_dim)
        b_rows = jnp.take(bc_values[:, :, 0], tile_group, axis=2).transpose(0, 2, 1, 3)
        c_rows = jnp.take(bc_values[:, :, 1], tile_group, axis=2).transpose(0, 2, 1, 3)
        state_out, read_rows = ssm_scan(state_tiles, decay_rows, dx_rows, b_rows, c_rows)
    ssm_now = (
        state_out.reshape(requests, tiles, state_dim, pack, head_dim)
        .transpose(0, 1, 3, 4, 2)
        .reshape(requests, heads_local, head_dim, state_dim)
    )
    if fused_gate:
        group_normed = gn_rows.reshape(requests * STEPS, heads_local * head_dim)
    else:
        scan_read = read_rows.reshape(requests, STEPS, heads_local, head_dim)
        readings = scan_read + skip_gain[:, None] * x_heads
        gated_out = readings * jax.nn.silu(z_gate)
        group_normed = (
            norm_rows(gated_out, gated_gain.reshape(heads_local, head_dim))
            .astype(jnp.bfloat16)
            .reshape(requests * STEPS, heads_local * head_dim)
        )
    per_expert = head_count // EXPERTS
    mixer_part = jnp.dot(group_normed, weight_out, preferred_element_type=jnp.float32)
    mixer_out = lax.all_to_all(
        mixer_part.reshape(head_count, tok_local, width), "head", 0, 0, tiled=True
    ).sum(axis=0)
    residual = (tokens[0].astype(jnp.float32) + mixer_out).astype(jnp.bfloat16)
    ffn_in = norm_rows(residual.astype(jnp.float32), ffn_gain).astype(jnp.bfloat16)
    share = route_share(ffn_in, router_weight, expert_ids[0])
    chosen = expert_ids[0].reshape(-1)
    onehot = (chosen[:, None] == jnp.arange(EXPERTS)[None, :]).astype(jnp.int32)
    earlier = jnp.cumsum(onehot, axis=0) - onehot
    position = jnp.sum(earlier * onehot, axis=1)
    slot_index = chosen * CAP + position
    place = (jnp.arange(EXPERTS * CAP)[:, None] == slot_index[None, :]).astype(jnp.bfloat16)
    routed_rows = jnp.repeat(ffn_in, TOP, axis=0)
    packed = jnp.dot(place, routed_rows, preferred_element_type=jnp.float32).astype(jnp.bfloat16)
    outgoing = jnp.repeat(packed.reshape(EXPERTS, CAP, width), per_expert, axis=0)
    received = lax.all_to_all(outgoing, "head", split_axis=0, concat_axis=0, tiled=True)
    flat_rows = received.reshape(-1, width)
    hidden = expert_hidden(flat_rows, weight_up)
    computed = jnp.dot(hidden, weight_down, preferred_element_type=jnp.float32).reshape(
        received.shape[0], received.shape[1], width
    )
    returned = lax.all_to_all(
        computed.astype(jnp.bfloat16), "head", split_axis=0, concat_axis=0, tiled=True
    ).astype(computed.dtype)
    summed = (
        returned.reshape(EXPERTS, per_expert, CAP, width).sum(axis=1).reshape(EXPERTS * CAP, width)
    )
    per_route = jnp.dot(place.astype(jnp.float32).T, summed, precision=highest).reshape(
        tok_local, TOP, width
    )
    combined = jnp.sum(share[:, :, None] * per_route, axis=1)
    layer_out = (residual.astype(jnp.float32) + combined).astype(jnp.bfloat16)
    return (layer_out[None], ssm_now[None], conv_x_new[None], conv_bc_new[None])


def solution(mesh):
    return jax.shard_map(
        shards,
        mesh=mesh,
        in_specs=(
            P("req", ("groups", "head"), None),
            P("req", "groups", "head", None, None),
            P("req", "groups", None, "head"),
            P("req", "groups", None, "head"),
            P("req", ("groups", "head"), None),
            P(),
            P(None, "head"),
            P(None, "head"),
            P(None, "head"),
            P("head"),
            P("head"),
            P("head"),
            P(None, "head"),
            P("head"),
            P(None, "head"),
            P("head"),
            P("head"),
            P("head", None),
            P(),
            P(),
            P(None, "head"),
            P("head", None),
        ),
        out_specs=(
            P("req", ("groups", "head"), None),
            P("req", "groups", "head", None, None),
            P("req", "groups", None, "head"),
            P("req", "groups", None, "head"),
        ),
        check_vma=False,
    )
```

```python
import functools

import jax
import jax.numpy as jnp
from jax import lax
from jax.experimental import pallas as pl
from jax.experimental.pallas import tpu as pltpu
from jax.sharding import PartitionSpec as P

HEADS = 128
G = 8
EXPERTS = 8
TOP = 2
STEPS = 8
CAP = 2


eps = 1e-05
highest = lax.Precision.HIGHEST


def norm_rows(values, gain):
    mean_square = jnp.mean(values * values, axis=-1, keepdims=True)
    return values * lax.rsqrt(mean_square + eps) * gain


def causal_conv(past_rows, fresh_rows, kernel, offset):
    window = jnp.concatenate([past_rows, fresh_rows], axis=1)
    window_wide = window.astype(jnp.float32)
    fresh_count = fresh_rows.shape[1]
    running = offset + kernel[0] * window_wide[:, 0:fresh_count]
    for tap_index in range(1, kernel.shape[0]):
        running = running + kernel[tap_index] * window_wide[:, tap_index : tap_index + fresh_count]
    return (jax.nn.silu(running), window[:, fresh_count:])


def route_share(ffn_in, router_weight, chosen_ids):
    logits = jnp.dot(ffn_in, router_weight, preferred_element_type=jnp.float32)
    match_table = (chosen_ids[:, :, None] == jnp.arange(EXPERTS)[None, None, :]).astype(jnp.float32)
    picked = jnp.einsum("mke,me->mk", match_table, logits, precision=highest)
    first_weight = jax.nn.sigmoid(picked[:, 0] - picked[:, 1])
    return jnp.stack([first_weight, 1.0 - first_weight], axis=1)


def expert_hidden(rows_in, weight_up):
    return jnp.square(
        jnp.maximum(jnp.dot(rows_in, weight_up, preferred_element_type=jnp.float32), 0.0)
    ).astype(jnp.bfloat16)


def column_matmul_kernel(a_ref, w_ref, o_ref):
    o_ref[...] = jnp.dot(a_ref[...], w_ref[...], preferred_element_type=jnp.float32)


def column_matmul(rows, weight):
    m, k = rows.shape
    cols = weight.shape[1]
    block = min(1024, cols)
    return pl.pallas_call(
        column_matmul_kernel,
        grid=(cols // block,),
        in_specs=[
            pl.BlockSpec((m, k), lambda j: (0, 0)),
            pl.BlockSpec((k, block), lambda j: (0, j)),
        ],
        out_specs=pl.BlockSpec((m, block), lambda j: (0, j)),
        out_shape=jax.ShapeDtypeStruct((m, cols), jnp.float32),
        cost_estimate=pl.CostEstimate(
            flops=2 * m * k * cols,
            transcendentals=0,
            bytes_accessed=2 * (m * k + k * cols) + 4 * m * cols,
        ),
    )(rows, weight)


def xz_matmul_kernel(head_dim, a_ref, g_ref, w_ref, n_ref, x_ref, z_ref, normed_ref):
    @pl.when(pl.program_id(0) == 0)
    def _():
        values = a_ref[...].astype(jnp.float32)
        mean_square = jnp.mean(values * values, axis=-1, keepdims=True)
        normed = (values * lax.rsqrt(mean_square + eps) * g_ref[...]).astype(jnp.bfloat16)
        normed_ref[...] = normed
        n_ref[...] = normed

    product = jnp.dot(normed_ref[...], w_ref[...], preferred_element_type=jnp.float32)
    width = z_ref.shape[1]
    for h in range(width // head_dim):
        x_ref[:, h * head_dim : (h + 1) * head_dim] = product[
            :, 2 * h * head_dim : (2 * h + 1) * head_dim
        ].astype(x_ref.dtype)
        z_ref[:, h * head_dim : (h + 1) * head_dim] = product[
            :, (2 * h + 1) * head_dim : (2 * h + 2) * head_dim
        ]


def xz_matmul(rows, gain, weight, head_dim):
    m, k = rows.shape
    cols = weight.shape[1]
    block = min(512, cols)
    return pl.pallas_call(
        functools.partial(xz_matmul_kernel, head_dim),
        grid=(cols // block,),
        in_specs=[
            pl.BlockSpec((m, k), lambda j: (0, 0)),
            pl.BlockSpec((1, k), lambda j: (0, 0)),
            pl.BlockSpec((k, block), lambda j: (0, j)),
        ],
        out_specs=[
            pl.BlockSpec((m, k), lambda j: (0, 0)),
            pl.BlockSpec((m, block // 2), lambda j: (0, j)),
            pl.BlockSpec((m, block // 2), lambda j: (0, j)),
        ],
        out_shape=[
            jax.ShapeDtypeStruct((m, k), jnp.bfloat16),
            jax.ShapeDtypeStruct((m, cols // 2), jnp.bfloat16),
            jax.ShapeDtypeStruct((m, cols // 2), jnp.float32),
        ],
        scratch_shapes=[pltpu.VMEM((m, k), jnp.bfloat16)],
        cost_estimate=pl.CostEstimate(
            flops=2 * m * k * cols,
            transcendentals=m,
            bytes_accessed=2 * (2 * m * k + k * cols) + 3 * m * cols,
        ),
    )(rows, gain.reshape(1, k), weight)


def ssm_scan_kernel(s_ref, dec_ref, dx_ref, b_ref, c_ref, s_out_ref, read_ref, bb_ref, cb_ref):
    tiles = s_ref.shape[1]
    state_dim = s_ref.shape[2]
    lanes = s_ref.shape[3]
    steps = dec_ref.shape[1]
    shared = b_ref.shape[1] == 1

    def fill(jb):
        b_cols = b_ref[0, jb].astype(jnp.float32).T
        c_cols = c_ref[0, jb].astype(jnp.float32).T
        for t in range(steps):
            bb_ref[t] = jnp.broadcast_to(b_cols[:, t : t + 1], (state_dim, lanes))
            cb_ref[t] = jnp.broadcast_to(c_cols[:, t : t + 1], (state_dim, lanes))

    if shared:
        fill(0)
    for j in range(tiles):
        if not shared:
            fill(j)
        cols = slice(j * lanes, (j + 1) * lanes)
        state = s_ref[0, j].astype(jnp.float32)
        dec_all = dec_ref[0, :, cols]
        dx_all = dx_ref[0, :, cols]
        for t in range(steps):
            fresh = dec_all[t : t + 1, :] * state + dx_all[t : t + 1, :] * bb_ref[t]
            read_ref[0, t : t + 1, cols] = jnp.sum(fresh * cb_ref[t], axis=0, keepdims=True)
            state = fresh.astype(jnp.bfloat16).astype(jnp.float32)
        s_out_ref[0, j] = state.astype(jnp.bfloat16)


def ssm_scan(state_tiles, decay_rows, dx_rows, b_rows, c_rows):
    requests, tiles, state_dim, lanes = state_tiles.shape
    steps = decay_rows.shape[1]
    big = pl.BlockSpec((1, tiles, state_dim, lanes), lambda r: (r, 0, 0, 0))
    per_step = pl.BlockSpec((1, steps, tiles * lanes), lambda r: (r, 0, 0))
    rows = pl.BlockSpec((1,) + b_rows.shape[1:], lambda r: (r, 0, 0, 0))
    return pl.pallas_call(
        ssm_scan_kernel,
        grid=(requests,),
        in_specs=[big, per_step, per_step, rows, rows],
        out_specs=[big, per_step],
        out_shape=[
            jax.ShapeDtypeStruct(state_tiles.shape, jnp.bfloat16),
            jax.ShapeDtypeStruct(decay_rows.shape, jnp.float32),
        ],
        scratch_shapes=[
            pltpu.VMEM((steps, state_dim, lanes), jnp.float32),
            pltpu.VMEM((steps, state_dim, lanes), jnp.float32),
        ],
    )(state_tiles, decay_rows, dx_rows, b_rows, c_rows)


def ssm_scan_direct_kernel(
    head_dim, group_ref, s_ref, dec_ref, dx_ref, b_ref, c_ref, z_ref, sx_ref, gain_ref,
    s_out_ref, read_ref, gn_ref, bb_ref, cb_ref,
):
    ssm_scan_kernel(s_ref, dec_ref, dx_ref, b_ref, c_ref, s_out_ref, read_ref, bb_ref, cb_ref)
    reading = read_ref[0] + sx_ref[0]
    z = z_ref[0]
    gated = reading * (z * jax.nn.sigmoid(z))
    steps, width = gated.shape
    lane = lax.broadcasted_iota(jnp.int32, (steps, width), 1)
    scale = jnp.zeros_like(gated)
    for h in range(width // head_dim):
        inside = (lane >= h * head_dim) & (lane < (h + 1) * head_dim)
        square_sum = jnp.sum(jnp.where(inside, gated * gated, 0.0), axis=1, keepdims=True)
        scale = jnp.where(inside, lax.rsqrt(square_sum * (1.0 / head_dim) + eps), scale)
    gn_ref[0] = (gated * scale * gain_ref[...]).astype(gn_ref.dtype)


def ssm_scan_direct(
    state_tiles, decay_rows, dx_rows, bc_blocks, group, group_count, z_rows, skip_rows, gain_row, head_dim
):
    requests, tiles, state_dim, lanes = state_tiles.shape
    steps = decay_rows.shape[1]
    cols_local = bc_blocks.shape[3]
    c_start = group_count * state_dim

    def b_map(r, g):
        first = g[0] * state_dim
        return (first // cols_local, r, 0, (first % cols_local) // state_dim)

    def c_map(r, g):
        first = c_start + g[0] * state_dim
        return (first // cols_local, r, 0, (first % cols_local) // state_dim)

    big = pl.BlockSpec((1, tiles, state_dim, lanes), lambda r, g: (r, 0, 0, 0))
    per_step = pl.BlockSpec((1, steps, tiles * lanes), lambda r, g: (r, 0, 0))
    return pl.pallas_call(
        functools.partial(ssm_scan_direct_kernel, head_dim),
        grid_spec=pltpu.PrefetchScalarGridSpec(
            num_scalar_prefetch=1,
            grid=(requests,),
            in_specs=[
                big,
                per_step,
                per_step,
                pl.BlockSpec((1, 1, steps, state_dim), b_map),
                pl.BlockSpec((1, 1, steps, state_dim), c_map),
                per_step,
                per_step,
                pl.BlockSpec((1, tiles * lanes), lambda r, g: (0, 0)),
            ],
            out_specs=[big, per_step, per_step],
            scratch_shapes=[
                pltpu.VMEM((steps, state_dim, lanes), jnp.float32),
                pltpu.VMEM((steps, state_dim, lanes), jnp.float32),
            ],
        ),
        out_shape=[
            jax.ShapeDtypeStruct(state_tiles.shape, jnp.bfloat16),
            jax.ShapeDtypeStruct(decay_rows.shape, jnp.float32),
            jax.ShapeDtypeStruct(decay_rows.shape, jnp.bfloat16),
        ],
    )(group, state_tiles, decay_rows, dx_rows, bc_blocks, bc_blocks, z_rows, skip_rows, gain_row)


def broadcast_gather(block, count):
    copies = jnp.broadcast_to(block[None], (count,) + block.shape)
    return lax.all_to_all(copies, "head", 0, 0, tiled=True)


def shards(
    tokens,
    ssm_state,
    conv_x_state,
    conv_bc_state,
    expert_ids,
    mixer_gain,
    weight_xz,
    weight_bc,
    weight_delta,
    delta_bias,
    decay_log,
    skip_gain,
    conv_x_kernel,
    conv_x_bias,
    conv_bc_kernel,
    conv_bc_bias,
    gated_gain,
    weight_out,
    ffn_gain,
    router_weight,
    weight_up,
    weight_down,
):
    head_count = lax.axis_size("head")
    my_index = lax.axis_index("head")
    tok_local = tokens.shape[1]
    width = tokens.shape[2]
    requests = ssm_state.shape[1]
    heads_local = ssm_state.shape[2]
    head_dim = ssm_state.shape[3]
    state_dim = ssm_state.shape[4]
    gathered = broadcast_gather(tokens[0], head_count)
    inputs = gathered.reshape(requests * STEPS, width)
    normed, x_rows, z_rows = xz_matmul(inputs, mixer_gain, weight_xz, head_dim)
    bc_fresh = (
        jnp.dot(normed, weight_bc, preferred_element_type=jnp.float32)
        .reshape(requests, STEPS, -1)
        .astype(jnp.bfloat16)
    )
    bc_conv, conv_bc_new = causal_conv(conv_bc_state[0], bc_fresh, conv_bc_kernel, conv_bc_bias)
    bc_conv, x_rows, z_rows = lax.optimization_barrier((bc_conv.astype(jnp.bfloat16), x_rows, z_rows))
    bc_blocks = broadcast_gather(bc_conv, head_count)
    x_fresh = x_rows.reshape(requests, STEPS, heads_local * head_dim)
    z_gate = z_rows.reshape(requests, STEPS, heads_local, head_dim)
    delta = jax.nn.softplus(
        jnp.dot(normed, weight_delta, preferred_element_type=jnp.float32).reshape(
            requests, STEPS, heads_local
        )
        + delta_bias
    )
    x_conv, conv_x_new = causal_conv(conv_x_state[0], x_fresh, conv_x_kernel, conv_x_bias)
    x_heads = x_conv.reshape(requests, STEPS, heads_local, head_dim)
    decay_rate = jnp.exp(delta * -jnp.exp(decay_log))
    pack = 2 if heads_local % 2 == 0 else 1
    tiles = heads_local // pack
    lanes = pack * head_dim

    decay_rows = jnp.broadcast_to(
        decay_rate[..., None], (requests, STEPS, heads_local, head_dim)
    ).reshape(requests, STEPS, heads_local * head_dim)
    dx_rows = (delta[..., None] * x_heads).reshape(requests, STEPS, heads_local * head_dim)
    shared_group = (HEADS // G) % heads_local == 0
    tile_group = (my_index * heads_local + jnp.arange(1 if shared_group else tiles) * pack) // (
        HEADS // G
    )
    state_tiles = (
        ssm_state[0]
        .reshape(requests, tiles, pack, head_dim, state_dim)
        .transpose(0, 1, 4, 2, 3)
        .reshape(requests, tiles, state_dim, lanes)
    )
    fused_gate = shared_group and bc_blocks.shape[3] % state_dim == 0
    if fused_gate:
        skip_rows = (skip_gain[:, None] * x_heads).reshape(requests, STEPS, heads_local * head_dim)
        state_out, read_rows, gn_rows = ssm_scan_direct(
            state_tiles,
            decay_rows,
            dx_rows,
            bc_blocks,
            tile_group.astype(jnp.int32),
            G,
            z_gate.reshape(requests, STEPS, heads_local * head_dim),
            skip_rows,
            gated_gain.reshape(1, heads_local * head_dim),
            head_dim,
        )
    else:
        bc_all = jnp.moveaxis(bc_blocks, 0, 2).reshape(requests, STEPS, -1)
        bc_values = bc_all.astype(jnp.float32).reshape(requests, STEPS, 2, G, state_dim)
        b_rows = jnp.take(bc_values[:, :, 0], tile_group, axis=2).transpose(0, 2, 1, 3)
        c_rows = jnp.take(bc_values[:, :, 1], tile_group, axis=2).transpose(0, 2, 1, 3)
        state_out, read_rows = ssm_scan(state_tiles, decay_rows, dx_rows, b_rows, c_rows)
    ssm_now = (
        state_out.reshape(requests, tiles, state_dim, pack, head_dim)
        .transpose(0, 1, 3, 4, 2)
        .reshape(requests, heads_local, head_dim, state_dim)
    )
    if fused_gate:
        group_normed = gn_rows.reshape(requests * STEPS, heads_local * head_dim)
    else:
        scan_read = read_rows.reshape(requests, STEPS, heads_local, head_dim)
        readings = scan_read + skip_gain[:, None] * x_heads
        gated_out = readings * jax.nn.silu(z_gate)
        group_normed = (
            norm_rows(gated_out, gated_gain.reshape(heads_local, head_dim))
            .astype(jnp.bfloat16)
            .reshape(requests * STEPS, heads_local * head_dim)
        )
    per_expert = head_count // EXPERTS
    mixer_part = jnp.dot(group_normed, weight_out, preferred_element_type=jnp.float32)
    mixer_out = lax.all_to_all(
        mixer_part.reshape(head_count, tok_local, width), "head", 0, 0, tiled=True
    ).sum(axis=0)
    residual = (tokens[0].astype(jnp.float32) + mixer_out).astype(jnp.bfloat16)
    ffn_in = norm_rows(residual.astype(jnp.float32), ffn_gain).astype(jnp.bfloat16)
    share = route_share(ffn_in, router_weight, expert_ids[0])
    chosen = expert_ids[0].reshape(-1)
    onehot = (chosen[:, None] == jnp.arange(EXPERTS)[None, :]).astype(jnp.int32)
    earlier = jnp.cumsum(onehot, axis=0) - onehot
    position = jnp.sum(earlier * onehot, axis=1)
    slot_index = chosen * CAP + position
    place = (jnp.arange(EXPERTS * CAP)[:, None] == slot_index[None, :]).astype(jnp.bfloat16)
    routed_rows = jnp.repeat(ffn_in, TOP, axis=0)
    packed = jnp.dot(place, routed_rows, preferred_element_type=jnp.float32).astype(jnp.bfloat16)
    outgoing = jnp.repeat(packed.reshape(EXPERTS, CAP, width), per_expert, axis=0)
    received = lax.all_to_all(outgoing, "head", split_axis=0, concat_axis=0, tiled=True)
    flat_rows = received.reshape(-1, width)
    hidden = expert_hidden(flat_rows, weight_up)
    computed = jnp.dot(hidden, weight_down, preferred_element_type=jnp.float32).reshape(
        received.shape[0], received.shape[1], width
    )
    returned = lax.all_to_all(computed, "head", split_axis=0, concat_axis=0, tiled=True)
    summed = (
        returned.reshape(EXPERTS, per_expert, CAP, width).sum(axis=1).reshape(EXPERTS * CAP, width)
    )
    per_route = jnp.dot(place.astype(jnp.float32).T, summed, precision=highest).reshape(
        tok_local, TOP, width
    )
    combined = jnp.sum(share[:, :, None] * per_route, axis=1)
    layer_out = (residual.astype(jnp.float32) + combined).astype(jnp.bfloat16)
    return (layer_out[None], ssm_now[None], conv_x_new[None], conv_bc_new[None])


def solution(mesh):
    return jax.shard_map(
        shards,
        mesh=mesh,
        in_specs=(
            P("req", ("groups", "head"), None),
            P("req", "groups", "head", None, None),
            P("req", "groups", None, "head"),
            P("req", "groups", None, "head"),
            P("req", ("groups", "head"), None),
            P(),
            P(None, "head"),
            P(None, "head"),
            P(None, "head"),
            P("head"),
            P("head"),
            P("head"),
            P(None, "head"),
            P("head"),
            P(None, "head"),
            P("head"),
            P("head"),
            P("head", None),
            P(),
            P(),
            P(None, "head"),
            P("head", None),
        ),
        out_specs=(
            P("req", ("groups", "head"), None),
            P("req", "groups", "head", None, None),
            P("req", "groups", None, "head"),
            P("req", "groups", None, "head"),
        ),
        check_vma=False,
    )
```

```python
import functools

import jax
import jax.numpy as jnp
from jax import lax
from jax.experimental import pallas as pl
from jax.experimental.pallas import tpu as pltpu
from jax.sharding import PartitionSpec as P

HEADS = 128
G = 8
EXPERTS = 8
TOP = 2
STEPS = 8
CAP = 2


eps = 1e-05
highest = lax.Precision.HIGHEST


def norm_rows(values, gain):
    mean_square = jnp.mean(values * values, axis=-1, keepdims=True)
    return values * lax.rsqrt(mean_square + eps) * gain


def causal_conv(past_rows, fresh_rows, kernel, offset):
    window = jnp.concatenate([past_rows, fresh_rows], axis=1)
    window_wide = window.astype(jnp.float32)
    fresh_count = fresh_rows.shape[1]
    running = offset + kernel[0] * window_wide[:, 0:fresh_count]
    for tap_index in range(1, kernel.shape[0]):
        running = running + kernel[tap_index] * window_wide[:, tap_index : tap_index + fresh_count]
    return (jax.nn.silu(running), window[:, fresh_count:])


def route_share(ffn_in, router_weight, chosen_ids):
    logits = jnp.dot(ffn_in, router_weight, preferred_element_type=jnp.float32)
    match_table = (chosen_ids[:, :, None] == jnp.arange(EXPERTS)[None, None, :]).astype(jnp.float32)
    picked = jnp.einsum("mke,me->mk", match_table, logits, precision=highest)
    first_weight = jax.nn.sigmoid(picked[:, 0] - picked[:, 1])
    return jnp.stack([first_weight, 1.0 - first_weight], axis=1)


def expert_hidden(rows_in, weight_up):
    return jnp.square(
        jnp.maximum(jnp.dot(rows_in, weight_up, preferred_element_type=jnp.float32), 0.0)
    ).astype(jnp.bfloat16)


def column_matmul_kernel(a_ref, w_ref, o_ref):
    o_ref[...] = jnp.dot(a_ref[...], w_ref[...], preferred_element_type=jnp.float32)


def column_matmul(rows, weight):
    m, k = rows.shape
    cols = weight.shape[1]
    block = min(1024, cols)
    return pl.pallas_call(
        column_matmul_kernel,
        grid=(cols // block,),
        in_specs=[
            pl.BlockSpec((m, k), lambda j: (0, 0)),
            pl.BlockSpec((k, block), lambda j: (0, j)),
        ],
        out_specs=pl.BlockSpec((m, block), lambda j: (0, j)),
        out_shape=jax.ShapeDtypeStruct((m, cols), jnp.float32),
        cost_estimate=pl.CostEstimate(
            flops=2 * m * k * cols,
            transcendentals=0,
            bytes_accessed=2 * (m * k + k * cols) + 4 * m * cols,
        ),
    )(rows, weight)


def xz_matmul_kernel(head_dim, a_ref, g_ref, w_ref, n_ref, x_ref, z_ref, normed_ref):
    @pl.when(pl.program_id(0) == 0)
    def _():
        values = a_ref[...].astype(jnp.float32)
        mean_square = jnp.mean(values * values, axis=-1, keepdims=True)
        normed = (values * lax.rsqrt(mean_square + eps) * g_ref[...]).astype(jnp.bfloat16)
        normed_ref[...] = normed
        n_ref[...] = normed

    product = jnp.dot(normed_ref[...], w_ref[...], preferred_element_type=jnp.float32)
    width = z_ref.shape[1]
    for h in range(width // head_dim):
        x_ref[:, h * head_dim : (h + 1) * head_dim] = product[
            :, 2 * h * head_dim : (2 * h + 1) * head_dim
        ].astype(x_ref.dtype)
        z_ref[:, h * head_dim : (h + 1) * head_dim] = product[
            :, (2 * h + 1) * head_dim : (2 * h + 2) * head_dim
        ]


def xz_matmul(rows, gain, weight, head_dim):
    m, k = rows.shape
    cols = weight.shape[1]
    block = min(1024, cols)
    return pl.pallas_call(
        functools.partial(xz_matmul_kernel, head_dim),
        grid=(cols // block,),
        in_specs=[
            pl.BlockSpec((m, k), lambda j: (0, 0)),
            pl.BlockSpec((1, k), lambda j: (0, 0)),
            pl.BlockSpec((k, block), lambda j: (0, j)),
        ],
        out_specs=[
            pl.BlockSpec((m, k), lambda j: (0, 0)),
            pl.BlockSpec((m, block // 2), lambda j: (0, j)),
            pl.BlockSpec((m, block // 2), lambda j: (0, j)),
        ],
        out_shape=[
            jax.ShapeDtypeStruct((m, k), jnp.bfloat16),
            jax.ShapeDtypeStruct((m, cols // 2), jnp.bfloat16),
            jax.ShapeDtypeStruct((m, cols // 2), jnp.float32),
        ],
        scratch_shapes=[pltpu.VMEM((m, k), jnp.bfloat16)],
        cost_estimate=pl.CostEstimate(
            flops=2 * m * k * cols,
            transcendentals=m,
            bytes_accessed=2 * (2 * m * k + k * cols) + 3 * m * cols,
        ),
    )(rows, gain.reshape(1, k), weight)


def ssm_scan_kernel(s_ref, dec_ref, dx_ref, b_ref, c_ref, s_out_ref, read_ref, bb_ref, cb_ref):
    tiles = s_ref.shape[1]
    state_dim = s_ref.shape[2]
    lanes = s_ref.shape[3]
    steps = dec_ref.shape[1]
    shared = b_ref.shape[1] == 1

    def fill(jb):
        b_cols = b_ref[0, jb].astype(jnp.float32).T
        c_cols = c_ref[0, jb].astype(jnp.float32).T
        for t in range(steps):
            bb_ref[t] = jnp.broadcast_to(b_cols[:, t : t + 1], (state_dim, lanes))
            cb_ref[t] = jnp.broadcast_to(c_cols[:, t : t + 1], (state_dim, lanes))

    if shared:
        fill(0)
    for j in range(tiles):
        if not shared:
            fill(j)
        cols = slice(j * lanes, (j + 1) * lanes)
        state = s_ref[0, j].astype(jnp.float32)
        dec_all = dec_ref[0, :, cols]
        dx_all = dx_ref[0, :, cols]
        for t in range(steps):
            fresh = dec_all[t : t + 1, :] * state + dx_all[t : t + 1, :] * bb_ref[t]
            read_ref[0, t : t + 1, cols] = jnp.sum(fresh * cb_ref[t], axis=0, keepdims=True)
            state = fresh.astype(jnp.bfloat16).astype(jnp.float32)
        s_out_ref[0, j] = state.astype(jnp.bfloat16)


def ssm_scan(state_tiles, decay_rows, dx_rows, b_rows, c_rows):
    requests, tiles, state_dim, lanes = state_tiles.shape
    steps = decay_rows.shape[1]
    big = pl.BlockSpec((1, tiles, state_dim, lanes), lambda r: (r, 0, 0, 0))
    per_step = pl.BlockSpec((1, steps, tiles * lanes), lambda r: (r, 0, 0))
    rows = pl.BlockSpec((1,) + b_rows.shape[1:], lambda r: (r, 0, 0, 0))
    return pl.pallas_call(
        ssm_scan_kernel,
        grid=(requests,),
        in_specs=[big, per_step, per_step, rows, rows],
        out_specs=[big, per_step],
        out_shape=[
            jax.ShapeDtypeStruct(state_tiles.shape, jnp.bfloat16),
            jax.ShapeDtypeStruct(decay_rows.shape, jnp.float32),
        ],
        scratch_shapes=[
            pltpu.VMEM((steps, state_dim, lanes), jnp.float32),
            pltpu.VMEM((steps, state_dim, lanes), jnp.float32),
        ],
    )(state_tiles, decay_rows, dx_rows, b_rows, c_rows)


def ssm_scan_direct_kernel(
    head_dim, group_ref, s_ref, dec_ref, dx_ref, b_ref, c_ref, z_ref, sx_ref, gain_ref,
    s_out_ref, read_ref, gn_ref, bb_ref, cb_ref,
):
    ssm_scan_kernel(s_ref, dec_ref, dx_ref, b_ref, c_ref, s_out_ref, read_ref, bb_ref, cb_ref)
    reading = read_ref[0] + sx_ref[0]
    z = z_ref[0]
    gated = reading * (z * jax.nn.sigmoid(z))
    steps, width = gated.shape
    lane = lax.broadcasted_iota(jnp.int32, (steps, width), 1)
    scale = jnp.zeros_like(gated)
    for h in range(width // head_dim):
        inside = (lane >= h * head_dim) & (lane < (h + 1) * head_dim)
        square_sum = jnp.sum(jnp.where(inside, gated * gated, 0.0), axis=1, keepdims=True)
        scale = jnp.where(inside, lax.rsqrt(square_sum * (1.0 / head_dim) + eps), scale)
    gn_ref[0] = (gated * scale * gain_ref[...]).astype(gn_ref.dtype)


def ssm_scan_direct(
    state_tiles, decay_rows, dx_rows, bc_blocks, group, group_count, z_rows, skip_rows, gain_row, head_dim
):
    requests, tiles, state_dim, lanes = state_tiles.shape
    steps = decay_rows.shape[1]
    cols_local = bc_blocks.shape[3]
    c_start = group_count * state_dim

    def b_map(r, g):
        first = g[0] * state_dim
        return (first // cols_local, r, 0, (first % cols_local) // state_dim)

    def c_map(r, g):
        first = c_start + g[0] * state_dim
        return (first // cols_local, r, 0, (first % cols_local) // state_dim)

    big = pl.BlockSpec((1, tiles, state_dim, lanes), lambda r, g: (r, 0, 0, 0))
    per_step = pl.BlockSpec((1, steps, tiles * lanes), lambda r, g: (r, 0, 0))
    return pl.pallas_call(
        functools.partial(ssm_scan_direct_kernel, head_dim),
        grid_spec=pltpu.PrefetchScalarGridSpec(
            num_scalar_prefetch=1,
            grid=(requests,),
            in_specs=[
                big,
                per_step,
                per_step,
                pl.BlockSpec((1, 1, steps, state_dim), b_map),
                pl.BlockSpec((1, 1, steps, state_dim), c_map),
                per_step,
                per_step,
                pl.BlockSpec((1, tiles * lanes), lambda r, g: (0, 0)),
            ],
            out_specs=[big, per_step, per_step],
            scratch_shapes=[
                pltpu.VMEM((steps, state_dim, lanes), jnp.float32),
                pltpu.VMEM((steps, state_dim, lanes), jnp.float32),
            ],
        ),
        out_shape=[
            jax.ShapeDtypeStruct(state_tiles.shape, jnp.bfloat16),
            jax.ShapeDtypeStruct(decay_rows.shape, jnp.float32),
            jax.ShapeDtypeStruct(decay_rows.shape, jnp.bfloat16),
        ],
    )(group, state_tiles, decay_rows, dx_rows, bc_blocks, bc_blocks, z_rows, skip_rows, gain_row)


def broadcast_gather(block, count):
    copies = jnp.broadcast_to(block[None], (count,) + block.shape)
    return lax.all_to_all(copies, "head", 0, 0, tiled=True)


def shards(
    tokens,
    ssm_state,
    conv_x_state,
    conv_bc_state,
    expert_ids,
    mixer_gain,
    weight_xz,
    weight_bc,
    weight_delta,
    delta_bias,
    decay_log,
    skip_gain,
    conv_x_kernel,
    conv_x_bias,
    conv_bc_kernel,
    conv_bc_bias,
    gated_gain,
    weight_out,
    ffn_gain,
    router_weight,
    weight_up,
    weight_down,
):
    head_count = lax.axis_size("head")
    my_index = lax.axis_index("head")
    tok_local = tokens.shape[1]
    width = tokens.shape[2]
    requests = ssm_state.shape[1]
    heads_local = ssm_state.shape[2]
    head_dim = ssm_state.shape[3]
    state_dim = ssm_state.shape[4]
    gathered = broadcast_gather(tokens[0], head_count)
    inputs = gathered.reshape(requests * STEPS, width)
    normed, x_rows, z_rows = xz_matmul(inputs, mixer_gain, weight_xz, head_dim)
    bc_fresh = (
        jnp.dot(normed, weight_bc, preferred_element_type=jnp.float32)
        .reshape(requests, STEPS, -1)
        .astype(jnp.bfloat16)
    )
    bc_conv, conv_bc_new = causal_conv(conv_bc_state[0], bc_fresh, conv_bc_kernel, conv_bc_bias)
    bc_conv, x_rows, z_rows = lax.optimization_barrier((bc_conv.astype(jnp.bfloat16), x_rows, z_rows))
    bc_blocks = broadcast_gather(bc_conv, head_count)
    x_fresh = x_rows.reshape(requests, STEPS, heads_local * head_dim)
    z_gate = z_rows.reshape(requests, STEPS, heads_local, head_dim)
    delta = jax.nn.softplus(
        jnp.dot(normed, weight_delta, preferred_element_type=jnp.float32).reshape(
            requests, STEPS, heads_local
        )
        + delta_bias
    )
    x_conv, conv_x_new = causal_conv(conv_x_state[0], x_fresh, conv_x_kernel, conv_x_bias)
    x_heads = x_conv.reshape(requests, STEPS, heads_local, head_dim)
    decay_rate = jnp.exp(delta * -jnp.exp(decay_log))
    pack = 2 if heads_local % 2 == 0 else 1
    tiles = heads_local // pack
    lanes = pack * head_dim

    decay_rows = jnp.broadcast_to(
        decay_rate[..., None], (requests, STEPS, heads_local, head_dim)
    ).reshape(requests, STEPS, heads_local * head_dim)
    dx_rows = (delta[..., None] * x_heads).reshape(requests, STEPS, heads_local * head_dim)
    shared_group = (HEADS // G) % heads_local == 0
    tile_group = (my_index * heads_local + jnp.arange(1 if shared_group else tiles) * pack) // (
        HEADS // G
    )
    state_tiles = (
        ssm_state[0]
        .reshape(requests, tiles, pack, head_dim, state_dim)
        .transpose(0, 1, 4, 2, 3)
        .reshape(requests, tiles, state_dim, lanes)
    )
    fused_gate = shared_group and bc_blocks.shape[3] % state_dim == 0
    if fused_gate:
        skip_rows = (skip_gain[:, None] * x_heads).reshape(requests, STEPS, heads_local * head_dim)
        state_out, read_rows, gn_rows = ssm_scan_direct(
            state_tiles,
            decay_rows,
            dx_rows,
            bc_blocks,
            tile_group.astype(jnp.int32),
            G,
            z_gate.reshape(requests, STEPS, heads_local * head_dim),
            skip_rows,
            gated_gain.reshape(1, heads_local * head_dim),
            head_dim,
        )
    else:
        bc_all = jnp.moveaxis(bc_blocks, 0, 2).reshape(requests, STEPS, -1)
        bc_values = bc_all.astype(jnp.float32).reshape(requests, STEPS, 2, G, state_dim)
        b_rows = jnp.take(bc_values[:, :, 0], tile_group, axis=2).transpose(0, 2, 1, 3)
        c_rows = jnp.take(bc_values[:, :, 1], tile_group, axis=2).transpose(0, 2, 1, 3)
        state_out, read_rows = ssm_scan(state_tiles, decay_rows, dx_rows, b_rows, c_rows)
    ssm_now = (
        state_out.reshape(requests, tiles, state_dim, pack, head_dim)
        .transpose(0, 1, 3, 4, 2)
        .reshape(requests, heads_local, head_dim, state_dim)
    )
    if fused_gate:
        group_normed = gn_rows.reshape(requests * STEPS, heads_local * head_dim)
    else:
        scan_read = read_rows.reshape(requests, STEPS, heads_local, head_dim)
        readings = scan_read + skip_gain[:, None] * x_heads
        gated_out = readings * jax.nn.silu(z_gate)
        group_normed = (
            norm_rows(gated_out, gated_gain.reshape(heads_local, head_dim))
            .astype(jnp.bfloat16)
            .reshape(requests * STEPS, heads_local * head_dim)
        )
    per_expert = head_count // EXPERTS
    mixer_part = jnp.dot(group_normed, weight_out, preferred_element_type=jnp.float32)
    mixer_out = lax.all_to_all(
        mixer_part.reshape(head_count, tok_local, width), "head", 0, 0, tiled=True
    ).sum(axis=0)
    residual = (tokens[0].astype(jnp.float32) + mixer_out).astype(jnp.bfloat16)
    ffn_in = norm_rows(residual.astype(jnp.float32), ffn_gain).astype(jnp.bfloat16)
    share = route_share(ffn_in, router_weight, expert_ids[0])
    chosen = expert_ids[0].reshape(-1)
    onehot = (chosen[:, None] == jnp.arange(EXPERTS)[None, :]).astype(jnp.int32)
    earlier = jnp.cumsum(onehot, axis=0) - onehot
    position = jnp.sum(earlier * onehot, axis=1)
    slot_index = chosen * CAP + position
    place = (jnp.arange(EXPERTS * CAP)[:, None] == slot_index[None, :]).astype(jnp.bfloat16)
    routed_rows = jnp.repeat(ffn_in, TOP, axis=0)
    packed = jnp.dot(place, routed_rows, preferred_element_type=jnp.float32).astype(jnp.bfloat16)
    outgoing = jnp.repeat(packed.reshape(EXPERTS, CAP, width), per_expert, axis=0)
    received = lax.all_to_all(outgoing, "head", split_axis=0, concat_axis=0, tiled=True)
    flat_rows = received.reshape(-1, width)
    hidden = expert_hidden(flat_rows, weight_up)
    computed = jnp.dot(hidden, weight_down, preferred_element_type=jnp.float32).reshape(
        received.shape[0], received.shape[1], width
    )
    returned = lax.all_to_all(
        computed.astype(jnp.bfloat16), "head", split_axis=0, concat_axis=0, tiled=True
    ).astype(computed.dtype)
    summed = (
        returned.reshape(EXPERTS, per_expert, CAP, width).sum(axis=1).reshape(EXPERTS * CAP, width)
    )
    per_route = jnp.dot(place.astype(jnp.float32).T, summed, precision=highest).reshape(
        tok_local, TOP, width
    )
    combined = jnp.sum(share[:, :, None] * per_route, axis=1)
    layer_out = (residual.astype(jnp.float32) + combined).astype(jnp.bfloat16)
    return (layer_out[None], ssm_now[None], conv_x_new[None], conv_bc_new[None])


def solution(mesh):
    return jax.shard_map(
        shards,
        mesh=mesh,
        in_specs=(
            P("req", ("groups", "head"), None),
            P("req", "groups", "head", None, None),
            P("req", "groups", None, "head"),
            P("req", "groups", None, "head"),
            P("req", ("groups", "head"), None),
            P(),
            P(None, "head"),
            P(None, "head"),
            P(None, "head"),
            P("head"),
            P("head"),
            P("head"),
            P(None, "head"),
            P("head"),
            P(None, "head"),
            P("head"),
            P("head"),
            P("head", None),
            P(),
            P(),
            P(None, "head"),
            P("head", None),
        ),
        out_specs=(
            P("req", ("groups", "head"), None),
            P("req", "groups", "head", None, None),
            P("req", "groups", None, "head"),
            P("req", "groups", None, "head"),
        ),
        check_vma=False,
    )
```
